32 devices in a mesh: group: 2 (over y), ctx: 8 (over z, x), tsp: 2 (over core).
Axes of the slice: x: 2, y: 2, z: 4, core: 2. Of those that a mesh axis runs over, the one named last changes fastest.
Arguments:
- query_proj: bfloat16 [4096, 2048], P(('group', 'ctx'), 'tsp'), parts along dimension 0, may hold values from -8 to 8
- key_proj: bfloat16 [4096, 1024], P(('group', 'ctx'), 'tsp'), parts along dimension 0, may hold values from -8 to 8
- value_projection: bfloat16 [4096, 1024], P(('group', 'ctx'), 'tsp'), parts along dimension 0, may hold values from -6 to 6
- grad_out: bfloat16 [4096, 2048], P(('group', 'ctx', 'tsp')), parts along dimension 0, may hold values from -6 to 6
- doc_ids: int32 [4096], P(('group', 'ctx')), parts along dimension 0, may hold values from 0 to 3, never falling along the last dimension, each value on 1 to 1024 neighbouring positions
- advantages: float32 [8], P('group'), parts along dimension 0, may hold values from -4 to 4
- head_window: int32 [16], P('tsp'), may hold values from 512 to 1024, as said below
Outputs:
- query_grad: bfloat16 [4096, 2048], P(('group', 'ctx'), 'tsp'), parts along dimension 0
- key_grad: bfloat16 [4096, 1024], P(('group', 'ctx'), 'tsp'), parts along dimension 0
- value_grad: bfloat16 [4096, 1024], P(('group', 'ctx'), 'tsp'), parts along dimension 0
The draws below stay inside these ranges and needn't reach their ends.
There are 2 independent parts, one for each index of `group`. The reference program is written for one: setup_inputs(seed, part) draws one part's arguments, and reference() takes and returns one part's arrays. A program takes and returns all parts, laid end to end along the dimension named above; an argument that names none is the same for every part. Nothing has to cross between parts.
Inputs may be any that keep to these rules, and one draw needn't show every extreme that they name: `doc_ids`: document numbers never fall along the sequence; every document holds 1 to 1024 positions. `head_window`: some head has a window of exactly 1024.
All inputs are finite; a program needn't handle non-finite values.
Results may differ from the reference program's by a relative error of at most 0.039.
Values may be sent and summed in bfloat16 or wider, within the bound.
No kernel may reach another device: no remote copies, remote signals or barrier semaphores. Data moves between devices by JAX's collectives and lax.ppermute only.
A program may use at most 64 MiB of HBM per device.

```python
import math
import jax
import jax.numpy as jnp
import numpy as np
from jax import lax

HEAD_DIMENSION = 128
QUERY_HEADS = 16
KEY_VALUE_HEADS = 8
WINDOW = 1024
TOK_DEV = 256
SEQUENCE_TOKENS = 2048
DOCS = 4
DOC_MOST = 1024


def query_key_pair(seed_key):
    random_base_key = jax.random.fold_in(seed_key, 4242)
    query_part = jnp.clip(jax.random.normal(jax.random.fold_in(random_base_key, 1), (SEQUENCE_TOKENS, QUERY_HEADS * HEAD_DIMENSION), jnp.float32), -6.0, 6.0)
    key_segment_slice = jnp.clip(jax.random.normal(jax.random.fold_in(random_base_key, 2), (SEQUENCE_TOKENS, KEY_VALUE_HEADS * HEAD_DIMENSION), jnp.float32), -6.0, 6.0)
    return (query_part, key_segment_slice)


def draw_query_proj(key, part):
    return query_key_pair(key)[0].astype(jnp.bfloat16)


def draw_key_proj(key, part):
    return query_key_pair(key)[1].astype(jnp.bfloat16)


def draw_head_window(key, part):
    random_base_key = jax.random.fold_in(key, 77)
    windows = jax.random.randint(jax.random.fold_in(random_base_key, 1), (QUERY_HEADS,), WINDOW // 2, WINDOW + 1, dtype=jnp.int32)
    widest = jax.random.randint(jax.random.fold_in(random_base_key, 2), (), 0, QUERY_HEADS, dtype=jnp.int32)
    return windows.at[widest].set(WINDOW)


def block_scale(stream_key, shape, shards, low, top_value):
    factor_of, own = 1.0, jax.random.fold_in(stream_key, 6)
    for axis_at, parts in shards:
        draws = jnp.exp(jax.random.uniform(jax.random.fold_in(own, axis_at), (parts,), jnp.float32, low / len(shards), top_value / len(shards)))
        factor_of = factor_of * jnp.repeat(draws, shape[axis_at] // parts).reshape([-1 if axis == axis_at else 1 for axis in range(len(shape))])
    return factor_of


def split_up(number_of, total, bound, slope):
    weights = [(1 << 20) // math.isqrt(standing ** slope) + 1 for standing in range(2, number_of + 1)]
    spare, holding = total - bound - (number_of - 1), [1] * (number_of - 1)
    while spare > 0:
        movable = [i for i in range(number_of - 1) if holding[i] < bound]
        pool, budget = sum([weights[i] for i in movable]), spare
        for i in movable:
            extra = min(bound - holding[i], max(1, budget * weights[i] // pool), spare)
            holding[i] = holding[i] + extra
            spare = spare - extra
    return np.array([bound] + holding)


def ragged(key, amount, total, bound, slope):
    if amount == 2:
        one = jax.random.randint(key, (), max(1, total - bound), min(bound, total - 1) + 1)
        return jnp.stack([one, total - one])
    lengths = jnp.asarray(split_up(amount, total, bound, slope), jnp.int32)
    twos = (amount - 1) // 2
    giver, taker = lengths[1:1 + 2 * twos:2], lengths[2:2 + 2 * twos:2]
    margin = jnp.minimum(giver - 1, bound - taker)
    moved = jax.random.randint(jax.random.fold_in(key, 1), (twos,), 0, 1 << 20) % (margin + 1)
    lengths = lengths.at[1:1 + 2 * twos:2].set(giver - moved).at[2:2 + 2 * twos:2].set(taker + moved)
    return lengths[jax.random.permutation(jax.random.fold_in(key, 2), amount)]


def normal_values(stream_key, extent, deviation, bound, cuts=(), held_as=jnp.bfloat16):
    loudness = block_scale(stream_key, extent, cuts, -0.22, 0.18) if cuts else 1.0
    array = jax.random.normal(stream_key, extent, jnp.float32) * deviation * loudness
    return jnp.minimum(jnp.maximum(array, -bound), bound).astype(held_as)


def setup_inputs(seed: int = 0, part: int = 0) -> dict:
    streams_of = jax.random.split(jax.random.key(seed), 8)
    part_keys = jax.random.split(jax.random.fold_in(streams_of[7], part), 8)
    query_proj = draw_query_proj(jax.random.fold_in(jax.random.fold_in(streams_of[7], part), 71), part)
    key_proj = draw_key_proj(jax.random.fold_in(jax.random.fold_in(streams_of[7], part), 71), part)
    value_projection = normal_values(part_keys[2], (SEQUENCE_TOKENS, KEY_VALUE_HEADS * HEAD_DIMENSION), 1.0, 6.0, ((0, 8), (1, 2)))
    grad_out = normal_values(part_keys[3], (SEQUENCE_TOKENS, QUERY_HEADS * HEAD_DIMENSION), 1.0, 6.0, ((0, 16),))
    doc_ids = jnp.searchsorted(jnp.cumsum(ragged(part_keys[4], DOCS, SEQUENCE_TOKENS, DOC_MOST, 1)), jnp.arange(SEQUENCE_TOKENS), side="right").astype(jnp.int32)
    advantages = normal_values(part_keys[5], (DOCS,), 1.0, 4.0, (), jnp.float32)
    head_window = draw_head_window(jax.random.fold_in(streams_of[7], 71), part)
    return dict(query_proj=query_proj, key_proj=key_proj, value_projection=value_projection, grad_out=grad_out, doc_ids=doc_ids, advantages=advantages, head_window=head_window)


score_scale = 168.0 ** -0.5


def head_grads(operands, query_pos, key_pos, doc_start):
    query_row_block, key_rows, value_rows, grad_rows, windows = operands
    row_count = query_row_block.shape[0]
    group_size = windows.shape[0]
    head_size = key_rows.shape[1]
    query_three = query_row_block.reshape(row_count, group_size, head_size).astype(jnp.float32)
    grad_three = grad_rows.reshape(row_count, group_size, head_size).astype(jnp.float32)
    key_float = key_rows.astype(jnp.float32)
    value_float = value_rows.astype(jnp.float32)
    high = lax.Precision.HIGHEST
    scores = jnp.einsum("rgd,sd->grs", query_three, key_float, precision=high) * score_scale
    offset = query_pos[:, None] - key_pos[None, :]
    allowed = (offset >= 0) & (key_pos[None, :] >= doc_start[:, None])
    live = allowed[None, :, :] & (offset[None, :, :] < windows[:, None, None])
    scores = jnp.where(live, scores, jnp.float32(-1e30))
    top = jnp.max(scores, axis=-1, keepdims=True)
    prob = jnp.exp(scores - top)
    prob = prob / jnp.sum(prob, axis=-1, keepdims=True)
    prob_low = lax.optimization_barrier(prob.astype(jnp.bfloat16)).astype(jnp.float32)
    attended = jnp.einsum("grs,sd->rgd", prob_low, value_float, precision=high)
    attended = lax.optimization_barrier(attended.astype(jnp.bfloat16)).astype(jnp.float32)
    delta = jnp.sum(grad_three * attended, axis=-1).T
    dprob = jnp.einsum("rgd,sd->grs", grad_three, value_float, precision=high)
    dscore = prob * (dprob - delta[:, :, None])
    dscore = lax.optimization_barrier(dscore.astype(jnp.bfloat16)).astype(jnp.float32)
    query_part = jnp.einsum("grs,sd->rgd", dscore, key_float, precision=high) * score_scale
    key_segment_slice = jnp.einsum("grs,rgd->sd", dscore, query_three, precision=high) * score_scale
    value_part = jnp.einsum("grs,rgd->sd", prob_low, grad_three, precision=high)
    return query_part.reshape(row_count, group_size * head_size).astype(jnp.bfloat16), key_segment_slice, value_part


def round_cross(block):
    cross = lax.optimization_barrier(block[:WINDOW].astype(jnp.bfloat16)).astype(jnp.float32)
    return jnp.concatenate([cross, block[WINDOW:]], axis=0)


def reference(query_proj, key_proj, value_projection, grad_out, doc_ids, advantages, head_window):
    seq_len = query_proj.shape[0]
    kv_heads = key_proj.shape[1] // HEAD_DIMENSION
    q_heads = query_proj.shape[1] // HEAD_DIMENSION
    group_size = q_heads // kv_heads
    positions = jnp.arange(seq_len, dtype=jnp.int32)
    matches = doc_ids[:, None] == jnp.arange(DOCS, dtype=jnp.int32)[None, :]
    first_pos = jnp.min(jnp.where(matches, positions[:, None], jnp.int32(seq_len)), axis=0)
    doc_start = jnp.max(jnp.where(matches, first_pos[None, :], jnp.int32(0)), axis=1)
    token_weight = jnp.sum(jnp.where(matches, advantages[None, :], jnp.float32(0.0)), axis=1)
    weighted = (token_weight[:, None] * grad_out.astype(jnp.float32)).astype(jnp.bfloat16)
    filler = jnp.zeros((WINDOW, kv_heads * HEAD_DIMENSION), key_proj.dtype)
    key_padded = jnp.concatenate([filler, key_proj], axis=0)
    value_padded = jnp.concatenate([filler, value_projection], axis=0)
    window_stack = head_window.reshape(kv_heads, group_size)
    key_count = TOK_DEV + WINDOW

    def block_step(block_idx, carry):
        query_acc, key_acc, value_acc = carry
        start = jnp.asarray(block_idx, jnp.int32) * jnp.int32(TOK_DEV)
        query_row_block = lax.dynamic_slice_in_dim(query_proj, start, TOK_DEV, 0)
        grad_rows = lax.dynamic_slice_in_dim(weighted, start, TOK_DEV, 0)
        key_rows = lax.dynamic_slice_in_dim(key_padded, start, key_count, 0)
        value_rows = lax.dynamic_slice_in_dim(value_padded, start, key_count, 0)
        query_pos = start + jnp.arange(TOK_DEV, dtype=jnp.int32)
        key_pos = start - jnp.int32(WINDOW) + jnp.arange(key_count, dtype=jnp.int32)
        starts_here = lax.dynamic_slice_in_dim(doc_start, start, TOK_DEV, 0)
        query_stack = query_row_block.reshape(TOK_DEV, kv_heads, group_size * HEAD_DIMENSION).transpose(1, 0, 2)
        grad_stack = grad_rows.reshape(TOK_DEV, kv_heads, group_size * HEAD_DIMENSION).transpose(1, 0, 2)
        key_stack = key_rows.reshape(key_count, kv_heads, HEAD_DIMENSION).transpose(1, 0, 2)
        value_stack = value_rows.reshape(key_count, kv_heads, HEAD_DIMENSION).transpose(1, 0, 2)
        results = lax.map(lambda operands: head_grads(operands, query_pos, key_pos, starts_here),
                          (query_stack, key_stack, value_stack, grad_stack, window_stack))
        query_block = results[0].transpose(1, 0, 2).reshape(TOK_DEV, q_heads * HEAD_DIMENSION)
        key_block = round_cross(results[1].transpose(1, 0, 2).reshape(key_count, kv_heads * HEAD_DIMENSION))
        value_block = round_cross(results[2].transpose(1, 0, 2).reshape(key_count, kv_heads * HEAD_DIMENSION))
        query_acc = lax.dynamic_update_slice_in_dim(query_acc, query_block, start, 0)
        key_old = lax.dynamic_slice_in_dim(key_acc, start, key_count, 0)
        value_old = lax.dynamic_slice_in_dim(value_acc, start, key_count, 0)
        key_acc = lax.dynamic_update_slice_in_dim(key_acc, key_old + key_block, start, 0)
        value_acc = lax.dynamic_update_slice_in_dim(value_acc, value_old + value_block, start, 0)
        return query_acc, key_acc, value_acc

    initial = (jnp.zeros((seq_len, q_heads * HEAD_DIMENSION), jnp.bfloat16),
               jnp.zeros((seq_len + WINDOW, kv_heads * HEAD_DIMENSION), jnp.float32),
               jnp.zeros((seq_len + WINDOW, kv_heads * HEAD_DIMENSION), jnp.float32))
    query_acc, key_acc, value_acc = lax.fori_loop(0, seq_len // TOK_DEV, block_step, initial)
    return query_acc, key_acc[WINDOW:].astype(jnp.bfloat16), value_acc[WINDOW:].astype(jnp.bfloat16)
```

```python
import jax
import jax.numpy as jnp
from jax import lax
from jax.sharding import PartitionSpec as P

HEAD_DIMENSION = 128
WINDOW = 1024
KV_PER_CHUNK = 1


score_scale = 168.0 ** (-0.5)


def passed_along(value, axis, steps):
    count = lax.axis_size(axis)
    initial, last = (max(0, -steps), min(count, count - steps))
    return lax.ppermute(value, axis, [(source, source + steps) for source in range(initial, last)])


def head_grads(query_row_block, key_rows, value_rows, grad_rows, windows, base_live, offset):
    row_count = query_row_block.shape[0]
    group_size = windows.shape[0]
    head_size = key_rows.shape[1]
    query_three = query_row_block.reshape(row_count, group_size, head_size)
    grad_three = grad_rows.reshape(row_count, group_size, head_size)
    scores = (
        jnp.einsum("rgd,sd->grs", query_three, key_rows, preferred_element_type=jnp.float32)
        * score_scale
    )
    live = base_live[None, :, :] & (offset[None, :, :] < windows[:, None, None])
    scores = jnp.where(live, scores, jnp.float32(-1e30))
    top = jnp.max(scores, axis=-1, keepdims=True)
    prob = jnp.exp(scores - top)
    prob = prob / jnp.sum(prob, axis=-1, keepdims=True)
    prob_low = prob.astype(jnp.bfloat16)
    attended = jnp.einsum(
        "grs,sd->rgd", prob_low, value_rows, preferred_element_type=jnp.float32
    ).astype(jnp.bfloat16)
    delta = jnp.sum(grad_three.astype(jnp.float32) * attended.astype(jnp.float32), axis=-1).T
    dprob = jnp.einsum("rgd,sd->grs", grad_three, value_rows, preferred_element_type=jnp.float32)
    dscore = (prob * (dprob - delta[:, :, None])).astype(jnp.bfloat16)
    query_part = (
        jnp.einsum("grs,sd->rgd", dscore, key_rows, preferred_element_type=jnp.float32)
        * score_scale
    )
    key_part = (
        jnp.einsum("grs,rgd->sd", dscore, query_three, preferred_element_type=jnp.float32)
        * score_scale
    )
    value_part = jnp.einsum("grs,rgd->sd", prob_low, grad_three, preferred_element_type=jnp.float32)
    return (
        query_part.reshape(row_count, group_size * head_size).astype(jnp.bfloat16),
        key_part,
        value_part,
    )


def on_device(query_proj, key_proj, value_projection, grad_out, doc_ids, advantages, head_window):
    tok_rows = query_proj.shape[0]
    kv_heads = key_proj.shape[1] // HEAD_DIMENSION
    q_heads = query_proj.shape[1] // HEAD_DIMENSION
    group_size = q_heads // kv_heads
    blocks = WINDOW // tok_rows
    first_pos = lax.axis_index("ctx") * tok_rows
    positions = first_pos + jnp.arange(tok_rows, dtype=jnp.int32)
    doc_count = advantages.shape[0]
    matches = doc_ids[:, None] == jnp.arange(doc_count, dtype=jnp.int32)[None, :]
    token_weight = jnp.sum(jnp.where(matches, advantages[None, :], jnp.float32(0.0)), axis=1)
    grad_local = lax.all_to_all(grad_out, "tsp", split_axis=1, concat_axis=0, tiled=True)
    weighted = (token_weight[:, None] * grad_local.astype(jnp.float32)).astype(jnp.bfloat16)

    ids_earlier = [passed_along(doc_ids, "ctx", distance) for distance in range(blocks, 0, -1)]
    key_ids = jnp.concatenate(ids_earlier + [doc_ids], axis=0)
    key_count = key_ids.shape[0]
    key_pos = first_pos - blocks * tok_rows + jnp.arange(key_count, dtype=jnp.int32)
    offset = positions[:, None] - key_pos[None, :]
    base_live = (
        (offset >= 0) & (key_pos[None, :] >= 0) & (key_ids[None, :] == doc_ids[:, None])
    )

    chunk_heads = KV_PER_CHUNK
    chunk_count = kv_heads // chunk_heads
    chunk_width = chunk_heads * HEAD_DIMENSION
    query_width = group_size * HEAD_DIMENSION
    window_stack = head_window.reshape(kv_heads, group_size)

    query_pieces, key_pieces, value_pieces = [], [], []
    previous = None
    for chunk in range(chunk_count):
        cols = slice(chunk * chunk_width, (chunk + 1) * chunk_width)
        paired = jnp.concatenate([key_proj[:, cols], value_projection[:, cols]], axis=1)
        if previous is not None:
            paired, _ = lax.optimization_barrier((paired, previous))
        earlier = [passed_along(paired, "ctx", distance) for distance in range(blocks, 0, -1)]
        previous = earlier
        paired_all = jnp.concatenate(earlier + [paired], axis=0)
        key_grads, value_grads = [], []
        for inner in range(chunk_heads):
            head = chunk * chunk_heads + inner
            key_rows = paired_all[:, inner * HEAD_DIMENSION : (inner + 1) * HEAD_DIMENSION]
            value_rows = paired_all[
                :, chunk_width + inner * HEAD_DIMENSION : chunk_width + (inner + 1) * HEAD_DIMENSION
            ]
            qcols = slice(head * query_width, (head + 1) * query_width)
            query_part, key_part, value_part = head_grads(
                query_proj[:, qcols],
                key_rows,
                value_rows,
                weighted[:, qcols],
                window_stack[head],
                base_live,
                offset,
            )
            query_pieces.append(query_part)
            key_grads.append(key_part)
            value_grads.append(value_part)
        pair_grads = jnp.concatenate(key_grads + value_grads, axis=1)
        own_part = pair_grads[blocks * tok_rows :]
        cross_low = pair_grads[: blocks * tok_rows].astype(jnp.bfloat16)
        summed = own_part
        for distance in range(1, blocks + 1):
            piece = cross_low[(blocks - distance) * tok_rows : (blocks - distance + 1) * tok_rows]
            arrived = passed_along(piece, "ctx", -distance)
            summed = summed + arrived.astype(jnp.float32)
        key_pieces.append(summed[:, :chunk_width])
        value_pieces.append(summed[:, chunk_width:])
    query_grad = jnp.concatenate(query_pieces, axis=1)
    key_grad = jnp.concatenate(key_pieces, axis=1).astype(jnp.bfloat16)
    value_grad = jnp.concatenate(value_pieces, axis=1).astype(jnp.bfloat16)
    return (query_grad, key_grad, value_grad)


def solution(mesh):
    in_specs = (
        P(("group", "ctx"), "tsp"),
        P(("group", "ctx"), "tsp"),
        P(("group", "ctx"), "tsp"),
        P(("group", "ctx", "tsp"), None),
        P(("group", "ctx")),
        P("group"),
        P("tsp"),
    )
    out_specs = (P(("group", "ctx"), "tsp"), P(("group", "ctx"), "tsp"), P(("group", "ctx"), "tsp"))
    return jax.shard_map(
        on_device, mesh=mesh, in_specs=in_specs, out_specs=out_specs, check_vma=False
    )
```

```python
import functools
import jax
import jax.numpy as jnp
from jax import lax
from jax.experimental import pallas as pl
from jax.experimental.pallas import tpu as pltpu
from jax.sharding import PartitionSpec as P

HEAD_DIMENSION = 128
WINDOW = 1024
KV_PER_CHUNK = 4
score_scale = 168.0 ** (-0.5)


def _nt(a, b):
    return lax.dot_general(a, b, (((1,), (1,)), ((), ())), preferred_element_type=jnp.float32)


def _tn(a, b):
    return lax.dot_general(a, b, (((0,), (0,)), ((), ())), preferred_element_type=jnp.float32)


def _nn(a, b):
    return lax.dot_general(a, b, (((1,), (0,)), ((), ())), preferred_element_type=jnp.float32)


def attention_kernel(win_ref, qid_ref, kid_ref, q_ref, g_ref, *rest, pieces, group_size):
    kv_refs = rest[:pieces]
    dq_ref = rest[pieces]
    own_ref = rest[pieces + 1]
    cross_refs = rest[pieces + 2 :]
    d = HEAD_DIMENSION
    rows = q_ref.shape[0]
    piece_rows = kv_refs[0].shape[0]
    width = kv_refs[0].shape[1] // 2
    key_count = pieces * piece_rows
    row = lax.broadcasted_iota(jnp.int32, (rows, key_count), 0)
    col = lax.broadcasted_iota(jnp.int32, (rows, key_count), 1)
    offset = row + (key_count - rows) - col
    same_doc = kid_ref[...] == qid_ref[...]
    base_live = (offset >= 0) & same_doc
    for kv in range(width // d):
        kv_head(win_ref, q_ref, g_ref, kv_refs, dq_ref, own_ref, cross_refs, offset, base_live,
                kv, width, group_size)


def kv_head(win_ref, q_ref, g_ref, kv_refs, dq_ref, own_ref, cross_refs, offset, base_live,
            kv, width, group_size):
    d = HEAD_DIMENSION
    pieces = len(kv_refs)
    piece_rows = kv_refs[0].shape[0]
    keys = [ref[:, kv * d : (kv + 1) * d] for ref in kv_refs]
    values = [ref[:, width + kv * d : width + (kv + 1) * d] for ref in kv_refs]
    key_acc = [jnp.zeros((piece_rows, d), jnp.float32) for _ in range(pieces)]
    value_acc = [jnp.zeros((piece_rows, d), jnp.float32) for _ in range(pieces)]
    for h in range(group_size):
        head = kv * group_size + h
        query = q_ref[:, head * d : (head + 1) * d]
        grad = g_ref[:, head * d : (head + 1) * d]
        scores = jnp.concatenate([_nt(query, key) for key in keys], axis=1) * score_scale
        live = base_live & (offset < win_ref[head])
        scores = jnp.where(live, scores, jnp.float32(-1e30))
        top = jnp.max(scores, axis=1, keepdims=True)
        prob = jnp.exp(scores - top)
        prob = prob / jnp.sum(prob, axis=1, keepdims=True)
        prob_low = prob.astype(jnp.bfloat16)
        attended = _nn(prob_low[:, :piece_rows], values[0])
        for p in range(1, pieces):
            attended = attended + _nn(prob_low[:, p * piece_rows : (p + 1) * piece_rows], values[p])
        attended = attended.astype(jnp.bfloat16).astype(jnp.float32)
        delta = jnp.sum(grad.astype(jnp.float32) * attended, axis=1, keepdims=True)
        dprob = jnp.concatenate([_nt(grad, value) for value in values], axis=1)
        dscore = (prob * (dprob - delta)).astype(jnp.bfloat16)
        query_acc = _nn(dscore[:, :piece_rows], keys[0])
        for p in range(1, pieces):
            query_acc = query_acc + _nn(dscore[:, p * piece_rows : (p + 1) * piece_rows], keys[p])
        dq_ref[:, head * d : (head + 1) * d] = (query_acc * score_scale).astype(dq_ref.dtype)
        for p in range(pieces):
            cols = slice(p * piece_rows, (p + 1) * piece_rows)
            key_acc[p] = key_acc[p] + _tn(dscore[:, cols], query)
            value_acc[p] = value_acc[p] + _tn(prob_low[:, cols], grad)
    for p in range(pieces):
        target = own_ref if p == pieces - 1 else cross_refs[p]
        target[:, kv * d : (kv + 1) * d] = (key_acc[p] * score_scale).astype(target.dtype)
        target[:, width + kv * d : width + (kv + 1) * d] = value_acc[p].astype(target.dtype)


def head_group_grads(windows, query_ids, key_ids, query, grad, kv_pieces):
    pieces = len(kv_pieces)
    rows = query.shape[0]
    piece_rows = kv_pieces[0].shape[0]
    group_width = query.shape[1]
    pair_width = kv_pieces[0].shape[1]
    group_size = 2 * group_width // pair_width
    vmem = pl.BlockSpec(memory_space=pltpu.VMEM)
    smem = pl.BlockSpec(memory_space=pltpu.SMEM)
    out_shape = (
        [jax.ShapeDtypeStruct((rows, group_width), jnp.bfloat16)]
        + [jax.ShapeDtypeStruct((piece_rows, pair_width), jnp.float32)]
        + [jax.ShapeDtypeStruct((piece_rows, pair_width), jnp.bfloat16)] * (pieces - 1)
    )
    kernel = functools.partial(attention_kernel, pieces=pieces, group_size=group_size)
    outs = pl.pallas_call(
        kernel,
        out_shape=out_shape,
        in_specs=[smem] + [vmem] * (4 + pieces),
        out_specs=[vmem] * (pieces + 1),
        name="attention_group",
    )(windows, query_ids, key_ids, query, grad, *kv_pieces)
    return outs[0], outs[1], outs[2:]


def passed_along(value, axis, steps):
    count = lax.axis_size(axis)
    initial, last = (max(0, -steps), min(count, count - steps))
    return lax.ppermute(value, axis, [(source, source + steps) for source in range(initial, last)])


def on_device(query_proj, key_proj, value_projection, grad_out, doc_ids, advantages, head_window):
    tok_rows = query_proj.shape[0]
    kv_heads = key_proj.shape[1] // HEAD_DIMENSION
    q_heads = query_proj.shape[1] // HEAD_DIMENSION
    group_size = q_heads // kv_heads
    blocks = WINDOW // tok_rows
    first_pos = lax.axis_index("ctx") * tok_rows
    doc_count = advantages.shape[0]
    matches = doc_ids[:, None] == jnp.arange(doc_count, dtype=jnp.int32)[None, :]
    token_weight = jnp.sum(jnp.where(matches, advantages[None, :], jnp.float32(0.0)), axis=1)
    grad_local = lax.all_to_all(grad_out, "tsp", split_axis=1, concat_axis=0, tiled=True)
    weighted = (token_weight[:, None] * grad_local.astype(jnp.float32)).astype(jnp.bfloat16)

    ids_earlier = [passed_along(doc_ids, "ctx", distance) for distance in range(blocks, 0, -1)]
    key_ids = jnp.concatenate(ids_earlier + [doc_ids], axis=0)
    key_pos = first_pos - blocks * tok_rows + jnp.arange(key_ids.shape[0], dtype=jnp.int32)
    key_ids = jnp.where(key_pos >= 0, key_ids, jnp.int32(-1))[None, :]
    query_ids = doc_ids[:, None]

    chunk_heads = min(KV_PER_CHUNK, kv_heads)
    chunk_count = kv_heads // chunk_heads
    chunk_width = chunk_heads * HEAD_DIMENSION
    query_width = group_size * chunk_width

    query_pieces, key_pieces, value_pieces = [], [], []
    previous = None
    for chunk in range(chunk_count):
        cols = slice(chunk * chunk_width, (chunk + 1) * chunk_width)
        qcols = slice(chunk * query_width, (chunk + 1) * query_width)
        paired = jnp.concatenate([key_proj[:, cols], value_projection[:, cols]], axis=1)
        if previous is not None:
            paired, _ = lax.optimization_barrier((paired, previous))
        earlier = [passed_along(paired, "ctx", distance) for distance in range(blocks, 0, -1)]
        previous = earlier
        query_part, own_part, cross_parts = head_group_grads(
            head_window[chunk * group_size * chunk_heads : (chunk + 1) * group_size * chunk_heads],
            query_ids,
            key_ids,
            query_proj[:, qcols],
            weighted[:, qcols],
            earlier + [paired],
        )
        query_pieces.append(query_part)
        summed = own_part
        for index, piece in enumerate(cross_parts):
            arrived = passed_along(piece, "ctx", index - blocks)
            summed = summed + arrived.astype(jnp.float32)
        key_pieces.append(summed[:, :chunk_width])
        value_pieces.append(summed[:, chunk_width:])
    query_grad = jnp.concatenate(query_pieces, axis=1)
    key_grad = jnp.concatenate(key_pieces, axis=1).astype(jnp.bfloat16)
    value_grad = jnp.concatenate(value_pieces, axis=1).astype(jnp.bfloat16)
    return (query_grad, key_grad, value_grad)


def solution(mesh):
    in_specs = (
        P(("group", "ctx"), "tsp"),
        P(("group", "ctx"), "tsp"),
        P(("group", "ctx"), "tsp"),
        P(("group", "ctx", "tsp"), None),
        P(("group", "ctx")),
        P("group"),
        P("tsp"),
    )
    out_specs = (P(("group", "ctx"), "tsp"), P(("group", "ctx"), "tsp"), P(("group", "ctx"), "tsp"))
    return jax.shard_map(
        on_device, mesh=mesh, in_specs=in_specs, out_specs=out_specs, check_vma=False
    )
```

```python
import functools
import jax
import jax.numpy as jnp
from jax import lax
from jax.experimental import pallas as pl
from jax.experimental.pallas import tpu as pltpu
from jax.sharding import PartitionSpec as P

HEAD_DIMENSION = 128
WINDOW = 1024
KV_PER_CHUNK = 2
score_scale = 168.0 ** (-0.5)


def _nt(a, b):
    return lax.dot_general(a, b, (((1,), (1,)), ((), ())), preferred_element_type=jnp.float32)


def _tn(a, b):
    return lax.dot_general(a, b, (((0,), (0,)), ((), ())), preferred_element_type=jnp.float32)


def _nn(a, b):
    return lax.dot_general(a, b, (((1,), (0,)), ((), ())), preferred_element_type=jnp.float32)


def attention_kernel(win_ref, qid_ref, kid_ref, q_ref, g_ref, *rest, pieces, group_size):
    kv_refs = rest[:pieces]
    dq_ref = rest[pieces]
    own_ref = rest[pieces + 1]
    cross_refs = rest[pieces + 2 :]
    d = HEAD_DIMENSION
    rows = q_ref.shape[0]
    piece_rows = kv_refs[0].shape[0]
    width = kv_refs[0].shape[1] // 2
    key_count = pieces * piece_rows
    row = lax.broadcasted_iota(jnp.int32, (rows, key_count), 0)
    col = lax.broadcasted_iota(jnp.int32, (rows, key_count), 1)
    offset = row + (key_count - rows) - col
    same_doc = kid_ref[...] == qid_ref[...]
    base_live = (offset >= 0) & same_doc
    for kv in range(width // d):
        kv_head(win_ref, q_ref, g_ref, kv_refs, dq_ref, own_ref, cross_refs, offset, base_live,
                kv, width, group_size)


def kv_head(win_ref, q_ref, g_ref, kv_refs, dq_ref, own_ref, cross_refs, offset, base_live,
            kv, width, group_size):
    d = HEAD_DIMENSION
    pieces = len(kv_refs)
    piece_rows = kv_refs[0].shape[0]
    keys = [ref[:, kv * d : (kv + 1) * d] for ref in kv_refs]
    values = [ref[:, width + kv * d : width + (kv + 1) * d] for ref in kv_refs]
    key_acc = [jnp.zeros((piece_rows, d), jnp.float32) for _ in range(pieces)]
    value_acc = [jnp.zeros((piece_rows, d), jnp.float32) for _ in range(pieces)]
    for h in range(group_size):
        head = kv * group_size + h
        query = q_ref[:, head * d : (head + 1) * d]
        grad = g_ref[:, head * d : (head + 1) * d]
        scores = jnp.concatenate([_nt(query, key) for key in keys], axis=1) * score_scale
        live = base_live & (offset < win_ref[head])
        scores = jnp.where(live, scores, jnp.float32(-1e30))
        top = jnp.max(scores, axis=1, keepdims=True)
        prob = jnp.exp(scores - top)
        prob = prob / jnp.sum(prob, axis=1, keepdims=True)
        prob_low = prob.astype(jnp.bfloat16)
        attended = _nn(prob_low[:, :piece_rows], values[0])
        for p in range(1, pieces):
            attended = attended + _nn(prob_low[:, p * piece_rows : (p + 1) * piece_rows], values[p])
        attended = attended.astype(jnp.bfloat16).astype(jnp.float32)
        delta = jnp.sum(grad.astype(jnp.float32) * attended, axis=1, keepdims=True)
        dprob = jnp.concatenate([_nt(grad, value) for value in values], axis=1)
        dscore = (prob * (dprob - delta)).astype(jnp.bfloat16)
        query_acc = _nn(dscore[:, :piece_rows], keys[0])
        for p in range(1, pieces):
            query_acc = query_acc + _nn(dscore[:, p * piece_rows : (p + 1) * piece_rows], keys[p])
        dq_ref[:, head * d : (head + 1) * d] = (query_acc * score_scale).astype(dq_ref.dtype)
        for p in range(pieces):
            cols = slice(p * piece_rows, (p + 1) * piece_rows)
            key_acc[p] = key_acc[p] + _tn(dscore[:, cols], query)
            value_acc[p] = value_acc[p] + _tn(prob_low[:, cols], grad)
    for p in range(pieces):
        target = own_ref if p == pieces - 1 else cross_refs[p]
        target[:, kv * d : (kv + 1) * d] = (key_acc[p] * score_scale).astype(target.dtype)
        target[:, width + kv * d : width + (kv + 1) * d] = value_acc[p].astype(target.dtype)


def head_group_grads(windows, query_ids, key_ids, query, grad, kv_pieces):
    pieces = len(kv_pieces)
    rows = query.shape[0]
    piece_rows = kv_pieces[0].shape[0]
    group_width = query.shape[1]
    pair_width = kv_pieces[0].shape[1]
    group_size = 2 * group_width // pair_width
    vmem = pl.BlockSpec(memory_space=pltpu.VMEM)
    smem = pl.BlockSpec(memory_space=pltpu.SMEM)
    out_shape = (
        [jax.ShapeDtypeStruct((rows, group_width), jnp.bfloat16)]
        + [jax.ShapeDtypeStruct((piece_rows, pair_width), jnp.float32)]
        + [jax.ShapeDtypeStruct((piece_rows, pair_width), jnp.bfloat16)] * (pieces - 1)
    )
    kernel = functools.partial(attention_kernel, pieces=pieces, group_size=group_size)
    outs = pl.pallas_call(
        kernel,
        out_shape=out_shape,
        in_specs=[smem] + [vmem] * (4 + pieces),
        out_specs=[vmem] * (pieces + 1),
        name="attention_group",
    )(windows, query_ids, key_ids, query, grad, *kv_pieces)
    return outs[0], outs[1], outs[2:]


def passed_along(value, axis, steps):
    count = lax.axis_size(axis)
    initial, last = (max(0, -steps), min(count, count - steps))
    return lax.ppermute(value, axis, [(source, source + steps) for source in range(initial, last)])


def on_device(query_proj, key_proj, value_projection, grad_out, doc_ids, advantages, head_window):
    tok_rows = query_proj.shape[0]
    kv_heads = key_proj.shape[1] // HEAD_DIMENSION
    q_heads = query_proj.shape[1] // HEAD_DIMENSION
    group_size = q_heads // kv_heads
    blocks = WINDOW // tok_rows
    first_pos = lax.axis_index("ctx") * tok_rows
    doc_count = advantages.shape[0]
    matches = doc_ids[:, None] == jnp.arange(doc_count, dtype=jnp.int32)[None, :]
    token_weight = jnp.sum(jnp.where(matches, advantages[None, :], jnp.float32(0.0)), axis=1)
    grad_local = lax.all_to_all(grad_out, "tsp", split_axis=1, concat_axis=0, tiled=True)
    weighted = (token_weight[:, None] * grad_local.astype(jnp.float32)).astype(jnp.bfloat16)

    ids_earlier = [passed_along(doc_ids, "ctx", distance) for distance in range(blocks, 0, -1)]
    key_ids = jnp.concatenate(ids_earlier + [doc_ids], axis=0)
    key_pos = first_pos - blocks * tok_rows + jnp.arange(key_ids.shape[0], dtype=jnp.int32)
    key_ids = jnp.where(key_pos >= 0, key_ids, jnp.int32(-1))[None, :]
    query_ids = doc_ids[:, None]

    chunk_heads = min(KV_PER_CHUNK, kv_heads)
    chunk_count = kv_heads // chunk_heads
    chunk_width = chunk_heads * HEAD_DIMENSION
    query_width = group_size * chunk_width

    query_pieces, key_pieces, value_pieces = [], [], []
    previous = None
    for chunk in range(chunk_count):
        cols = slice(chunk * chunk_width, (chunk + 1) * chunk_width)
        qcols = slice(chunk * query_width, (chunk + 1) * query_width)
        paired = jnp.concatenate([key_proj[:, cols], value_projection[:, cols]], axis=1)
        if previous is not None:
            paired, _ = lax.optimization_barrier((paired, previous))
        earlier = [passed_along(paired, "ctx", distance) for distance in range(blocks, 0, -1)]
        previous = earlier
        query_part, own_part, cross_parts = head_group_grads(
            head_window[chunk * group_size * chunk_heads : (chunk + 1) * group_size * chunk_heads],
            query_ids,
            key_ids,
            query_proj[:, qcols],
            weighted[:, qcols],
            earlier + [paired],
        )
        query_pieces.append(query_part)
        summed = own_part
        for index, piece in enumerate(cross_parts):
            arrived = passed_along(piece, "ctx", index - blocks)
            summed = summed + arrived.astype(jnp.float32)
        key_pieces.append(summed[:, :chunk_width])
        value_pieces.append(summed[:, chunk_width:])
    query_grad = jnp.concatenate(query_pieces, axis=1)
    key_grad = jnp.concatenate(key_pieces, axis=1).astype(jnp.bfloat16)
    value_grad = jnp.concatenate(value_pieces, axis=1).astype(jnp.bfloat16)
    return (query_grad, key_grad, value_grad)


def solution(mesh):
    in_specs = (
        P(("group", "ctx"), "tsp"),
        P(("group", "ctx"), "tsp"),
        P(("group", "ctx"), "tsp"),
        P(("group", "ctx", "tsp"), None),
        P(("group", "ctx")),
        P("group"),
        P("tsp"),
    )
    out_specs = (P(("group", "ctx"), "tsp"), P(("group", "ctx"), "tsp"), P(("group", "ctx"), "tsp"))
    return jax.shard_map(
        on_device, mesh=mesh, in_specs=in_specs, out_specs=out_specs, check_vma=False
    )
```

```python
import functools
import jax
import jax.numpy as jnp
from jax import lax
from jax.experimental import pallas as pl
from jax.experimental.pallas import tpu as pltpu
from jax.sharding import PartitionSpec as P

HEAD_DIMENSION = 128
WINDOW = 1024
KV_PER_CHUNK = 2
ID_ROWS = 16
score_scale = 168.0 ** (-0.5)


def _nt(a, b):
    return lax.dot_general(a, b, (((1,), (1,)), ((), ())), preferred_element_type=jnp.float32)


def _tn(a, b):
    return lax.dot_general(a, b, (((0,), (0,)), ((), ())), preferred_element_type=jnp.float32)


def _nn(a, b):
    return lax.dot_general(a, b, (((1,), (0,)), ((), ())), preferred_element_type=jnp.float32)


def attention_kernel(win_ref, qid_ref, kid_ref, q_ref, g_ref, *rest, pieces, group_size):
    kv_refs = rest[:pieces]
    dq_ref = rest[pieces]
    own_ref = rest[pieces + 1]
    cross_refs = rest[pieces + 2 :]
    d = HEAD_DIMENSION
    rows = q_ref.shape[0]
    width = kv_refs[0].shape[1] // 2
    key_count = pieces * rows
    row = lax.broadcasted_iota(jnp.int32, (rows, key_count), 0)
    col = lax.broadcasted_iota(jnp.int32, (rows, key_count), 1)
    offset = row + (key_count - rows) - col
    same_doc = kid_ref[...] == qid_ref[...]
    base_live = (offset >= 0) & same_doc
    for kv in range(width // d):
        kv_head(win_ref, q_ref, g_ref, kv_refs, dq_ref, own_ref, cross_refs, offset, base_live,
                kv, width, group_size)


def kv_head(win_ref, q_ref, g_ref, kv_refs, dq_ref, own_ref, cross_refs, offset, base_live,
            kv, width, group_size):
    d = HEAD_DIMENSION
    pieces = len(kv_refs)
    piece_rows = q_ref.shape[0]
    keys = [ref[:piece_rows, kv * d : (kv + 1) * d] for ref in kv_refs]
    values = [ref[:piece_rows, width + kv * d : width + (kv + 1) * d] for ref in kv_refs]
    key_acc = [jnp.zeros((piece_rows, d), jnp.float32) for _ in range(pieces)]
    value_acc = [jnp.zeros((piece_rows, d), jnp.float32) for _ in range(pieces)]
    for h in range(group_size):
        head = kv * group_size + h
        query = q_ref[:, head * d : (head + 1) * d]
        grad = g_ref[:, head * d : (head + 1) * d]
        scores = jnp.concatenate([_nt(query, key) for key in keys], axis=1) * score_scale
        live = base_live & (offset < win_ref[head])
        scores = jnp.where(live, scores, jnp.float32(-1e30))
        top = jnp.max(scores, axis=1, keepdims=True)
        prob = jnp.exp(scores - top)
        prob = prob / jnp.sum(prob, axis=1, keepdims=True)
        prob_low = prob.astype(jnp.bfloat16)
        attended = _nn(prob_low[:, :piece_rows], values[0])
        for p in range(1, pieces):
            attended = attended + _nn(prob_low[:, p * piece_rows : (p + 1) * piece_rows], values[p])
        attended = attended.astype(jnp.bfloat16).astype(jnp.float32)
        delta = jnp.sum(grad.astype(jnp.float32) * attended, axis=1, keepdims=True)
        dprob = jnp.concatenate([_nt(grad, value) for value in values], axis=1)
        dscore = (prob * (dprob - delta)).astype(jnp.bfloat16)
        query_acc = _nn(dscore[:, :piece_rows], keys[0])
        for p in range(1, pieces):
            query_acc = query_acc + _nn(dscore[:, p * piece_rows : (p + 1) * piece_rows], keys[p])
        dq_ref[:, head * d : (head + 1) * d] = (query_acc * score_scale).astype(dq_ref.dtype)
        for p in range(pieces):
            cols = slice(p * piece_rows, (p + 1) * piece_rows)
            key_acc[p] = key_acc[p] + _tn(dscore[:, cols], query)
            value_acc[p] = value_acc[p] + _tn(prob_low[:, cols], grad)
    for p in range(pieces):
        target = own_ref if p == pieces - 1 else cross_refs[p]
        target[:, kv * d : (kv + 1) * d] = (key_acc[p] * score_scale).astype(target.dtype)
        target[:, width + kv * d : width + (kv + 1) * d] = value_acc[p].astype(target.dtype)


def head_group_grads(windows, query_ids, key_ids, query, grad, kv_pieces):
    pieces = len(kv_pieces)
    rows = query.shape[0]
    piece_rows = rows
    group_width = query.shape[1]
    pair_width = kv_pieces[0].shape[1]
    group_size = 2 * group_width // pair_width
    vmem = pl.BlockSpec(memory_space=pltpu.VMEM)
    smem = pl.BlockSpec(memory_space=pltpu.SMEM)
    out_shape = (
        [jax.ShapeDtypeStruct((rows, group_width), jnp.bfloat16)]
        + [jax.ShapeDtypeStruct((piece_rows, pair_width), jnp.float32)]
        + [jax.ShapeDtypeStruct((piece_rows, pair_width), jnp.bfloat16)] * (pieces - 1)
    )
    kernel = functools.partial(attention_kernel, pieces=pieces, group_size=group_size)
    outs = pl.pallas_call(
        kernel,
        out_shape=out_shape,
        in_specs=[smem] + [vmem] * (4 + pieces),
        out_specs=[vmem] * (pieces + 1),
        name="attention_group",
    )(windows, query_ids, key_ids, query, grad, *kv_pieces)
    return outs[0], outs[1], outs[2:]


def passed_along(value, axis, steps):
    count = lax.axis_size(axis)
    initial, last = (max(0, -steps), min(count, count - steps))
    return lax.ppermute(value, axis, [(source, source + steps) for source in range(initial, last)])


def on_device(query_proj, key_proj, value_projection, grad_out, doc_ids, advantages, head_window):
    tok_rows = query_proj.shape[0]
    kv_heads = key_proj.shape[1] // HEAD_DIMENSION
    q_heads = query_proj.shape[1] // HEAD_DIMENSION
    group_size = q_heads // kv_heads
    blocks = WINDOW // tok_rows
    first_pos = lax.axis_index("ctx") * tok_rows
    doc_count = advantages.shape[0]
    matches = doc_ids[:, None] == jnp.arange(doc_count, dtype=jnp.int32)[None, :]
    token_weight = jnp.sum(jnp.where(matches, advantages[None, :], jnp.float32(0.0)), axis=1)
    grad_local = lax.all_to_all(grad_out, "tsp", split_axis=1, concat_axis=0, tiled=True)
    weighted = (token_weight[:, None] * grad_local.astype(jnp.float32)).astype(jnp.bfloat16)

    query_ids = (doc_ids + 1).astype(jnp.float32)[:, None]
    key_ids = None

    chunk_heads = min(KV_PER_CHUNK, kv_heads)
    chunk_count = kv_heads // chunk_heads
    chunk_width = chunk_heads * HEAD_DIMENSION
    query_width = group_size * chunk_width

    query_pieces, key_pieces, value_pieces = [], [], []
    previous = None
    for chunk in range(chunk_count):
        cols = slice(chunk * chunk_width, (chunk + 1) * chunk_width)
        qcols = slice(chunk * query_width, (chunk + 1) * query_width)
        paired = jnp.concatenate([key_proj[:, cols], value_projection[:, cols]], axis=1)
        if key_ids is None:
            id_row = jnp.zeros((ID_ROWS, 2 * chunk_width), jnp.bfloat16)
            id_row = id_row.at[0, :tok_rows].set((doc_ids + 1).astype(jnp.bfloat16))
            paired = jnp.concatenate([paired, id_row], axis=0)
        if previous is not None:
            paired, _ = lax.optimization_barrier((paired, previous))
        earlier = [passed_along(paired, "ctx", distance) for distance in range(blocks, 0, -1)]
        previous = earlier
        if key_ids is None:
            key_ids = jnp.concatenate(
                [piece[tok_rows, :tok_rows] for piece in earlier + [paired]], axis=0
            ).astype(jnp.float32)[None, :]
        query_part, own_part, cross_parts = head_group_grads(
            head_window[chunk * group_size * chunk_heads : (chunk + 1) * group_size * chunk_heads],
            query_ids,
            key_ids,
            query_proj[:, qcols],
            weighted[:, qcols],
            earlier + [paired],
        )
        query_pieces.append(query_part)
        summed = own_part
        for index, piece in enumerate(cross_parts):
            arrived = passed_along(piece, "ctx", index - blocks)
            summed = summed + arrived.astype(jnp.float32)
        key_pieces.append(summed[:, :chunk_width])
        value_pieces.append(summed[:, chunk_width:])
    query_grad = jnp.concatenate(query_pieces, axis=1)
    key_grad = jnp.concatenate(key_pieces, axis=1).astype(jnp.bfloat16)
    value_grad = jnp.concatenate(value_pieces, axis=1).astype(jnp.bfloat16)
    return (query_grad, key_grad, value_grad)


def solution(mesh):
    in_specs = (
        P(("group", "ctx"), "tsp"),
        P(("group", "ctx"), "tsp"),
        P(("group", "ctx"), "tsp"),
        P(("group", "ctx", "tsp"), None),
        P(("group", "ctx")),
        P("group"),
        P("tsp"),
    )
    out_specs = (P(("group", "ctx"), "tsp"), P(("group", "ctx"), "tsp"), P(("group", "ctx"), "tsp"))
    return jax.shard_map(
        on_device, mesh=mesh, in_specs=in_specs, out_specs=out_specs, check_vma=False
    )
```

```python
import functools
import jax
import jax.numpy as jnp
from jax import lax
from jax.experimental import pallas as pl
from jax.experimental.pallas import tpu as pltpu
from jax.sharding import PartitionSpec as P

HEAD_DIMENSION = 128
WINDOW = 1024
KV_PER_CHUNK = 1
ID_ROWS = 16
score_scale = 168.0 ** (-0.5)


def _nt(a, b):
    return lax.dot_general(a, b, (((1,), (1,)), ((), ())), preferred_element_type=jnp.float32)


def _tn(a, b):
    return lax.dot_general(a, b, (((0,), (0,)), ((), ())), preferred_element_type=jnp.float32)


def _nn(a, b):
    return lax.dot_general(a, b, (((1,), (0,)), ((), ())), preferred_element_type=jnp.float32)


def attention_kernel(win_ref, qid_ref, kid_ref, q_ref, g_ref, *rest, pieces, group_size):
    kv_refs = rest[:pieces]
    dq_ref = rest[pieces]
    own_ref = rest[pieces + 1]
    cross_refs = rest[pieces + 2 :]
    d = HEAD_DIMENSION
    rows = q_ref.shape[0]
    width = kv_refs[0].shape[1] // 2
    key_count = pieces * rows
    row = lax.broadcasted_iota(jnp.int32, (rows, key_count), 0)
    col = lax.broadcasted_iota(jnp.int32, (rows, key_count), 1)
    offset = row + (key_count - rows) - col
    same_doc = kid_ref[...] == qid_ref[...]
    base_live = (offset >= 0) & same_doc
    for kv in range(width // d):
        kv_head(win_ref, q_ref, g_ref, kv_refs, dq_ref, own_ref, cross_refs, offset, base_live,
                kv, width, group_size)


def kv_head(win_ref, q_ref, g_ref, kv_refs, dq_ref, own_ref, cross_refs, offset, base_live,
            kv, width, group_size):
    d = HEAD_DIMENSION
    pieces = len(kv_refs)
    piece_rows = q_ref.shape[0]
    keys = [ref[:piece_rows, kv * d : (kv + 1) * d] for ref in kv_refs]
    values = [ref[:piece_rows, width + kv * d : width + (kv + 1) * d] for ref in kv_refs]
    key_acc = [jnp.zeros((piece_rows, d), jnp.float32) for _ in range(pieces)]
    value_acc = [jnp.zeros((piece_rows, d), jnp.float32) for _ in range(pieces)]
    for h in range(group_size):
        head = kv * group_size + h
        query = q_ref[:, head * d : (head + 1) * d]
        grad = g_ref[:, head * d : (head + 1) * d]
        scores = jnp.concatenate([_nt(query, key) for key in keys], axis=1) * score_scale
        live = base_live & (offset < win_ref[head])
        scores = jnp.where(live, scores, jnp.float32(-1e30))
        top = jnp.max(scores, axis=1, keepdims=True)
        prob = jnp.exp(scores - top)
        prob = prob / jnp.sum(prob, axis=1, keepdims=True)
        prob_low = prob.astype(jnp.bfloat16)
        attended = _nn(prob_low[:, :piece_rows], values[0])
        for p in range(1, pieces):
            attended = attended + _nn(prob_low[:, p * piece_rows : (p + 1) * piece_rows], values[p])
        attended = attended.astype(jnp.bfloat16).astype(jnp.float32)
        delta = jnp.sum(grad.astype(jnp.float32) * attended, axis=1, keepdims=True)
        dprob = jnp.concatenate([_nt(grad, value) for value in values], axis=1)
        dscore = (prob * (dprob - delta)).astype(jnp.bfloat16)
        query_acc = _nn(dscore[:, :piece_rows], keys[0])
        for p in range(1, pieces):
            query_acc = query_acc + _nn(dscore[:, p * piece_rows : (p + 1) * piece_rows], keys[p])
        dq_ref[:, head * d : (head + 1) * d] = (query_acc * score_scale).astype(dq_ref.dtype)
        for p in range(pieces):
            cols = slice(p * piece_rows, (p + 1) * piece_rows)
            key_acc[p] = key_acc[p] + _tn(dscore[:, cols], query)
            value_acc[p] = value_acc[p] + _tn(prob_low[:, cols], grad)
    for p in range(pieces):
        target = own_ref if p == pieces - 1 else cross_refs[p]
        target[:, kv * d : (kv + 1) * d] = (key_acc[p] * score_scale).astype(target.dtype)
        target[:, width + kv * d : width + (kv + 1) * d] = value_acc[p].astype(target.dtype)


def head_group_grads(windows, query_ids, key_ids, query, grad, kv_pieces):
    pieces = len(kv_pieces)
    rows = query.shape[0]
    piece_rows = rows
    group_width = query.shape[1]
    pair_width = kv_pieces[0].shape[1]
    group_size = 2 * group_width // pair_width
    vmem = pl.BlockSpec(memory_space=pltpu.VMEM)
    smem = pl.BlockSpec(memory_space=pltpu.SMEM)
    out_shape = (
        [jax.ShapeDtypeStruct((rows, group_width), jnp.bfloat16)]
        + [jax.ShapeDtypeStruct((piece_rows, pair_width), jnp.float32)]
        + [jax.ShapeDtypeStruct((piece_rows, pair_width), jnp.bfloat16)] * (pieces - 1)
    )
    kernel = functools.partial(attention_kernel, pieces=pieces, group_size=group_size)
    outs = pl.pallas_call(
        kernel,
        out_shape=out_shape,
        in_specs=[smem] + [vmem] * (4 + pieces),
        out_specs=[vmem] * (pieces + 1),
        name="attention_group",
    )(windows, query_ids, key_ids, query, grad, *kv_pieces)
    return outs[0], outs[1], outs[2:]


def passed_along(value, axis, steps):
    count = lax.axis_size(axis)
    initial, last = (max(0, -steps), min(count, count - steps))
    return lax.ppermute(value, axis, [(source, source + steps) for source in range(initial, last)])


def on_device(query_proj, key_proj, value_projection, grad_out, doc_ids, advantages, head_window):
    tok_rows = query_proj.shape[0]
    kv_heads = key_proj.shape[1] // HEAD_DIMENSION
    q_heads = query_proj.shape[1] // HEAD_DIMENSION
    group_size = q_heads // kv_heads
    blocks = WINDOW // tok_rows
    first_pos = lax.axis_index("ctx") * tok_rows
    doc_count = advantages.shape[0]
    matches = doc_ids[:, None] == jnp.arange(doc_count, dtype=jnp.int32)[None, :]
    token_weight = jnp.sum(jnp.where(matches, advantages[None, :], jnp.float32(0.0)), axis=1)
    grad_local = lax.all_to_all(grad_out, "tsp", split_axis=1, concat_axis=0, tiled=True)
    weighted = (token_weight[:, None] * grad_local.astype(jnp.float32)).astype(jnp.bfloat16)

    query_ids = (doc_ids + 1).astype(jnp.float32)[:, None]
    key_ids = None

    chunk_heads = min(KV_PER_CHUNK, kv_heads)
    chunk_count = kv_heads // chunk_heads
    chunk_width = chunk_heads * HEAD_DIMENSION
    query_width = group_size * chunk_width

    query_pieces, key_pieces, value_pieces = [], [], []
    previous = None
    for chunk in range(chunk_count):
        cols = slice(chunk * chunk_width, (chunk + 1) * chunk_width)
        qcols = slice(chunk * query_width, (chunk + 1) * query_width)
        paired = jnp.concatenate([key_proj[:, cols], value_projection[:, cols]], axis=1)
        if key_ids is None:
            id_row = jnp.zeros((ID_ROWS, 2 * chunk_width), jnp.bfloat16)
            id_row = id_row.at[0, :tok_rows].set((doc_ids + 1).astype(jnp.bfloat16))
            paired = jnp.concatenate([paired, id_row], axis=0)
        if previous is not None:
            paired, _ = lax.optimization_barrier((paired, previous))
        earlier = [passed_along(paired, "ctx", distance) for distance in range(blocks, 0, -1)]
        previous = earlier
        if key_ids is None:
            key_ids = jnp.concatenate(
                [piece[tok_rows, :tok_rows] for piece in earlier + [paired]], axis=0
            ).astype(jnp.float32)[None, :]
        query_part, own_part, cross_parts = head_group_grads(
            head_window[chunk * group_size * chunk_heads : (chunk + 1) * group_size * chunk_heads],
            query_ids,
            key_ids,
            query_proj[:, qcols],
            weighted[:, qcols],
            earlier + [paired],
        )
        query_pieces.append(query_part)
        summed = own_part
        for index, piece in enumerate(cross_parts):
            arrived = passed_along(piece, "ctx", index - blocks)
            summed = summed + arrived.astype(jnp.float32)
        key_pieces.append(summed[:, :chunk_width])
        value_pieces.append(summed[:, chunk_width:])
    query_grad = jnp.concatenate(query_pieces, axis=1)
    key_grad = jnp.concatenate(key_pieces, axis=1).astype(jnp.bfloat16)
    value_grad = jnp.concatenate(value_pieces, axis=1).astype(jnp.bfloat16)
    return (query_grad, key_grad, value_grad)


def solution(mesh):
    in_specs = (
        P(("group", "ctx"), "tsp"),
        P(("group", "ctx"), "tsp"),
        P(("group", "ctx"), "tsp"),
        P(("group", "ctx", "tsp"), None),
        P(("group", "ctx")),
        P("group"),
        P("tsp"),
    )
    out_specs = (P(("group", "ctx"), "tsp"), P(("group", "ctx"), "tsp"), P(("group", "ctx"), "tsp"))
    return jax.shard_map(
        on_device, mesh=mesh, in_specs=in_specs, out_specs=out_specs, check_vma=False
    )
```

```python
import functools
import jax
import jax.numpy as jnp
from jax import lax
from jax.experimental import pallas as pl
from jax.experimental.pallas import tpu as pltpu
from jax.sharding import PartitionSpec as P

HEAD_DIMENSION = 128
WINDOW = 1024
CHUNK_HEADS = (1, 2, 1)
ID_ROWS = 16
score_scale = 168.0 ** (-0.5)


def _nt(a, b):
    return lax.dot_general(a, b, (((1,), (1,)), ((), ())), preferred_element_type=jnp.float32)


def _tn(a, b):
    return lax.dot_general(a, b, (((0,), (0,)), ((), ())), preferred_element_type=jnp.float32)


def _nn(a, b):
    return lax.dot_general(a, b, (((1,), (0,)), ((), ())), preferred_element_type=jnp.float32)


def attention_kernel(win_ref, qid_ref, kid_ref, q_ref, g_ref, *rest, pieces, group_size):
    kv_refs = rest[:pieces]
    dq_ref = rest[pieces]
    own_ref = rest[pieces + 1]
    cross_refs = rest[pieces + 2 :]
    d = HEAD_DIMENSION
    rows = q_ref.shape[0]
    width = kv_refs[0].shape[1] // 2
    key_count = pieces * rows
    row = lax.broadcasted_iota(jnp.int32, (rows, key_count), 0)
    col = lax.broadcasted_iota(jnp.int32, (rows, key_count), 1)
    offset = row + (key_count - rows) - col
    same_doc = kid_ref[...] == qid_ref[...]
    base_live = (offset >= 0) & same_doc
    for kv in range(width // d):
        kv_head(win_ref, q_ref, g_ref, kv_refs, dq_ref, own_ref, cross_refs, offset, base_live,
                kv, width, group_size)


def kv_head(win_ref, q_ref, g_ref, kv_refs, dq_ref, own_ref, cross_refs, offset, base_live,
            kv, width, group_size):
    d = HEAD_DIMENSION
    pieces = len(kv_refs)
    piece_rows = q_ref.shape[0]
    keys = [ref[:piece_rows, kv * d : (kv + 1) * d] for ref in kv_refs]
    values = [ref[:piece_rows, width + kv * d : width + (kv + 1) * d] for ref in kv_refs]
    key_acc = [jnp.zeros((piece_rows, d), jnp.float32) for _ in range(pieces)]
    value_acc = [jnp.zeros((piece_rows, d), jnp.float32) for _ in range(pieces)]
    for h in range(group_size):
        head = kv * group_size + h
        query = q_ref[:, head * d : (head + 1) * d]
        grad = g_ref[:, head * d : (head + 1) * d]
        scores = jnp.concatenate([_nt(query, key) for key in keys], axis=1) * score_scale
        live = base_live & (offset < win_ref[head])
        scores = jnp.where(live, scores, jnp.float32(-1e30))
        top = jnp.max(scores, axis=1, keepdims=True)
        prob = jnp.exp(scores - top)
        prob = prob / jnp.sum(prob, axis=1, keepdims=True)
        prob_low = prob.astype(jnp.bfloat16)
        attended = _nn(prob_low[:, :piece_rows], values[0])
        for p in range(1, pieces):
            attended = attended + _nn(prob_low[:, p * piece_rows : (p + 1) * piece_rows], values[p])
        attended = attended.astype(jnp.bfloat16).astype(jnp.float32)
        delta = jnp.sum(grad.astype(jnp.float32) * attended, axis=1, keepdims=True)
        dprob = jnp.concatenate([_nt(grad, value) for value in values], axis=1)
        dscore = (prob * (dprob - delta)).astype(jnp.bfloat16)
        query_acc = _nn(dscore[:, :piece_rows], keys[0])
        for p in range(1, pieces):
            query_acc = query_acc + _nn(dscore[:, p * piece_rows : (p + 1) * piece_rows], keys[p])
        dq_ref[:, head * d : (head + 1) * d] = (query_acc * score_scale).astype(dq_ref.dtype)
        for p in range(pieces):
            cols = slice(p * piece_rows, (p + 1) * piece_rows)
            key_acc[p] = key_acc[p] + _tn(dscore[:, cols], query)
            value_acc[p] = value_acc[p] + _tn(prob_low[:, cols], grad)
    for p in range(pieces):
        target = own_ref if p == pieces - 1 else cross_refs[p]
        target[:, kv * d : (kv + 1) * d] = (key_acc[p] * score_scale).astype(target.dtype)
        target[:, width + kv * d : width + (kv + 1) * d] = value_acc[p].astype(target.dtype)


def head_group_grads(windows, query_ids, key_ids, query, grad, kv_pieces):
    pieces = len(kv_pieces)
    rows = query.shape[0]
    piece_rows = rows
    group_width = query.shape[1]
    pair_width = kv_pieces[0].shape[1]
    group_size = 2 * group_width // pair_width
    vmem = pl.BlockSpec(memory_space=pltpu.VMEM)
    smem = pl.BlockSpec(memory_space=pltpu.SMEM)
    out_shape = (
        [jax.ShapeDtypeStruct((rows, group_width), jnp.bfloat16)]
        + [jax.ShapeDtypeStruct((piece_rows, pair_width), jnp.float32)]
        + [jax.ShapeDtypeStruct((piece_rows, pair_width), jnp.bfloat16)] * (pieces - 1)
    )
    kernel = functools.partial(attention_kernel, pieces=pieces, group_size=group_size)
    outs = pl.pallas_call(
        kernel,
        out_shape=out_shape,
        in_specs=[smem] + [vmem] * (4 + pieces),
        out_specs=[vmem] * (pieces + 1),
        name="attention_group",
    )(windows, query_ids, key_ids, query, grad, *kv_pieces)
    return outs[0], outs[1], outs[2:]


def passed_along(value, axis, steps):
    count = lax.axis_size(axis)
    initial, last = (max(0, -steps), min(count, count - steps))
    return lax.ppermute(value, axis, [(source, source + steps) for source in range(initial, last)])


def on_device(query_proj, key_proj, value_projection, grad_out, doc_ids, advantages, head_window):
    tok_rows = query_proj.shape[0]
    kv_heads = key_proj.shape[1] // HEAD_DIMENSION
    q_heads = query_proj.shape[1] // HEAD_DIMENSION
    group_size = q_heads // kv_heads
    blocks = WINDOW // tok_rows
    first_pos = lax.axis_index("ctx") * tok_rows
    doc_count = advantages.shape[0]
    matches = doc_ids[:, None] == jnp.arange(doc_count, dtype=jnp.int32)[None, :]
    token_weight = jnp.sum(jnp.where(matches, advantages[None, :], jnp.float32(0.0)), axis=1)
    grad_local = lax.all_to_all(grad_out, "tsp", split_axis=1, concat_axis=0, tiled=True)
    weighted = (token_weight[:, None] * grad_local.astype(jnp.float32)).astype(jnp.bfloat16)

    query_ids = (doc_ids + 1).astype(jnp.float32)[:, None]
    key_ids = None

    chunk_sizes = CHUNK_HEADS if sum(CHUNK_HEADS) == kv_heads else (1,) * kv_heads

    query_pieces, key_pieces, value_pieces = [], [], []
    previous = None
    chunk_first = 0
    for chunk_heads in chunk_sizes:
        chunk_width = chunk_heads * HEAD_DIMENSION
        query_width = group_size * chunk_width
        cols = slice(chunk_first * HEAD_DIMENSION, chunk_first * HEAD_DIMENSION + chunk_width)
        qcols = slice(chunk_first * group_size * HEAD_DIMENSION,
                      chunk_first * group_size * HEAD_DIMENSION + query_width)
        windows = head_window[chunk_first * group_size : (chunk_first + chunk_heads) * group_size]
        chunk_first += chunk_heads
        paired = jnp.concatenate([key_proj[:, cols], value_projection[:, cols]], axis=1)
        if key_ids is None:
            id_row = jnp.zeros((ID_ROWS, 2 * chunk_width), jnp.bfloat16)
            id_row = id_row.at[0, :tok_rows].set((doc_ids + 1).astype(jnp.bfloat16))
            paired = jnp.concatenate([paired, id_row], axis=0)
        if previous is not None:
            paired, _ = lax.optimization_barrier((paired, previous))
        earlier = [passed_along(paired, "ctx", distance) for distance in range(blocks, 0, -1)]
        previous = earlier
        if key_ids is None:
            key_ids = jnp.concatenate(
                [piece[tok_rows, :tok_rows] for piece in earlier + [paired]], axis=0
            ).astype(jnp.float32)[None, :]
        query_part, own_part, cross_parts = head_group_grads(
            windows,
            query_ids,
            key_ids,
            query_proj[:, qcols],
            weighted[:, qcols],
            earlier + [paired],
        )
        query_pieces.append(query_part)
        summed = own_part
        for index, piece in enumerate(cross_parts):
            arrived = passed_along(piece, "ctx", index - blocks)
            summed = summed + arrived.astype(jnp.float32)
        key_pieces.append(summed[:, :chunk_width])
        value_pieces.append(summed[:, chunk_width:])
    query_grad = jnp.concatenate(query_pieces, axis=1)
    key_grad = jnp.concatenate(key_pieces, axis=1).astype(jnp.bfloat16)
    value_grad = jnp.concatenate(value_pieces, axis=1).astype(jnp.bfloat16)
    return (query_grad, key_grad, value_grad)


def solution(mesh):
    in_specs = (
        P(("group", "ctx"), "tsp"),
        P(("group", "ctx"), "tsp"),
        P(("group", "ctx"), "tsp"),
        P(("group", "ctx", "tsp"), None),
        P(("group", "ctx")),
        P("group"),
        P("tsp"),
    )
    out_specs = (P(("group", "ctx"), "tsp"), P(("group", "ctx"), "tsp"), P(("group", "ctx"), "tsp"))
    return jax.shard_map(
        on_device, mesh=mesh, in_specs=in_specs, out_specs=out_specs, check_vma=False
    )
```

```python
import functools
import jax
import jax.numpy as jnp
from jax import lax
from jax.experimental import pallas as pl
from jax.experimental.pallas import tpu as pltpu
from jax.sharding import PartitionSpec as P

HEAD_DIMENSION = 128
WINDOW = 1024
CHUNK_HEADS = (2, 2)
SERIAL_SENDS = False
ID_ROWS = 16
score_scale = 168.0 ** (-0.5)


def _nt(a, b):
    return lax.dot_general(a, b, (((1,), (1,)), ((), ())), preferred_element_type=jnp.float32)


def _tn(a, b):
    return lax.dot_general(a, b, (((0,), (0,)), ((), ())), preferred_element_type=jnp.float32)


def _nn(a, b):
    return lax.dot_general(a, b, (((1,), (0,)), ((), ())), preferred_element_type=jnp.float32)


def attention_kernel(win_ref, qid_ref, kid_ref, q_ref, g_ref, *rest, pieces, group_size):
    kv_refs = rest[:pieces]
    dq_ref = rest[pieces]
    own_ref = rest[pieces + 1]
    cross_refs = rest[pieces + 2 :]
    d = HEAD_DIMENSION
    rows = q_ref.shape[0]
    width = kv_refs[0].shape[1] // 2
    key_count = pieces * rows
    row = lax.broadcasted_iota(jnp.int32, (rows, key_count), 0)
    col = lax.broadcasted_iota(jnp.int32, (rows, key_count), 1)
    offset = row + (key_count - rows) - col
    same_doc = kid_ref[...] == qid_ref[...]
    base_live = (offset >= 0) & same_doc
    for kv in range(width // d):
        kv_head(win_ref, q_ref, g_ref, kv_refs, dq_ref, own_ref, cross_refs, offset, base_live,
                kv, width, group_size)


def kv_head(win_ref, q_ref, g_ref, kv_refs, dq_ref, own_ref, cross_refs, offset, base_live,
            kv, width, group_size):
    d = HEAD_DIMENSION
    pieces = len(kv_refs)
    piece_rows = q_ref.shape[0]
    keys = [ref[:piece_rows, kv * d : (kv + 1) * d] for ref in kv_refs]
    values = [ref[:piece_rows, width + kv * d : width + (kv + 1) * d] for ref in kv_refs]
    key_acc = [jnp.zeros((piece_rows, d), jnp.float32) for _ in range(pieces)]
    value_acc = [jnp.zeros((piece_rows, d), jnp.float32) for _ in range(pieces)]
    for h in range(group_size):
        head = kv * group_size + h
        query = q_ref[:, head * d : (head + 1) * d]
        grad = g_ref[:, head * d : (head + 1) * d]
        scores = jnp.concatenate([_nt(query, key) for key in keys], axis=1) * score_scale
        live = base_live & (offset < win_ref[head])
        scores = jnp.where(live, scores, jnp.float32(-1e30))
        top = jnp.max(scores, axis=1, keepdims=True)
        prob = jnp.exp(scores - top)
        prob = prob / jnp.sum(prob, axis=1, keepdims=True)
        prob_low = prob.astype(jnp.bfloat16)
        attended = _nn(prob_low[:, :piece_rows], values[0])
        for p in range(1, pieces):
            attended = attended + _nn(prob_low[:, p * piece_rows : (p + 1) * piece_rows], values[p])
        attended = attended.astype(jnp.bfloat16).astype(jnp.float32)
        delta = jnp.sum(grad.astype(jnp.float32) * attended, axis=1, keepdims=True)
        dprob = jnp.concatenate([_nt(grad, value) for value in values], axis=1)
        dscore = (prob * (dprob - delta)).astype(jnp.bfloat16)
        query_acc = _nn(dscore[:, :piece_rows], keys[0])
        for p in range(1, pieces):
            query_acc = query_acc + _nn(dscore[:, p * piece_rows : (p + 1) * piece_rows], keys[p])
        dq_ref[:, head * d : (head + 1) * d] = (query_acc * score_scale).astype(dq_ref.dtype)
        for p in range(pieces):
            cols = slice(p * piece_rows, (p + 1) * piece_rows)
            key_acc[p] = key_acc[p] + _tn(dscore[:, cols], query)
            value_acc[p] = value_acc[p] + _tn(prob_low[:, cols], grad)
    for p in range(pieces):
        target = own_ref if p == pieces - 1 else cross_refs[p]
        target[:, kv * d : (kv + 1) * d] = (key_acc[p] * score_scale).astype(target.dtype)
        target[:, width + kv * d : width + (kv + 1) * d] = value_acc[p].astype(target.dtype)


def head_group_grads(windows, query_ids, key_ids, query, grad, kv_pieces):
    pieces = len(kv_pieces)
    rows = query.shape[0]
    piece_rows = rows
    group_width = query.shape[1]
    pair_width = kv_pieces[0].shape[1]
    group_size = 2 * group_width // pair_width
    vmem = pl.BlockSpec(memory_space=pltpu.VMEM)
    smem = pl.BlockSpec(memory_space=pltpu.SMEM)
    out_shape = (
        [jax.ShapeDtypeStruct((rows, group_width), jnp.bfloat16)]
        + [jax.ShapeDtypeStruct((piece_rows, pair_width), jnp.float32)]
        + [jax.ShapeDtypeStruct((piece_rows, pair_width), jnp.bfloat16)] * (pieces - 1)
    )
    kernel = functools.partial(attention_kernel, pieces=pieces, group_size=group_size)
    outs = pl.pallas_call(
        kernel,
        out_shape=out_shape,
        in_specs=[smem] + [vmem] * (4 + pieces),
        out_specs=[vmem] * (pieces + 1),
        name="attention_group",
    )(windows, query_ids, key_ids, query, grad, *kv_pieces)
    return outs[0], outs[1], outs[2:]


def passed_along(value, axis, steps):
    count = lax.axis_size(axis)
    initial, last = (max(0, -steps), min(count, count - steps))
    return lax.ppermute(value, axis, [(source, source + steps) for source in range(initial, last)])


def on_device(query_proj, key_proj, value_projection, grad_out, doc_ids, advantages, head_window):
    tok_rows = query_proj.shape[0]
    kv_heads = key_proj.shape[1] // HEAD_DIMENSION
    q_heads = query_proj.shape[1] // HEAD_DIMENSION
    group_size = q_heads // kv_heads
    blocks = WINDOW // tok_rows
    first_pos = lax.axis_index("ctx") * tok_rows
    doc_count = advantages.shape[0]
    matches = doc_ids[:, None] == jnp.arange(doc_count, dtype=jnp.int32)[None, :]
    token_weight = jnp.sum(jnp.where(matches, advantages[None, :], jnp.float32(0.0)), axis=1)
    grad_local = lax.all_to_all(grad_out, "tsp", split_axis=1, concat_axis=0, tiled=True)
    weighted = (token_weight[:, None] * grad_local.astype(jnp.float32)).astype(jnp.bfloat16)

    query_ids = (doc_ids + 1).astype(jnp.float32)[:, None]
    key_ids = None

    chunk_sizes = CHUNK_HEADS if sum(CHUNK_HEADS) == kv_heads else (1,) * kv_heads

    query_pieces, key_pieces, value_pieces = [], [], []
    previous = None
    chunk_first = 0
    for chunk_heads in chunk_sizes:
        chunk_width = chunk_heads * HEAD_DIMENSION
        query_width = group_size * chunk_width
        cols = slice(chunk_first * HEAD_DIMENSION, chunk_first * HEAD_DIMENSION + chunk_width)
        qcols = slice(chunk_first * group_size * HEAD_DIMENSION,
                      chunk_first * group_size * HEAD_DIMENSION + query_width)
        windows = head_window[chunk_first * group_size : (chunk_first + chunk_heads) * group_size]
        chunk_first += chunk_heads
        paired = jnp.concatenate([key_proj[:, cols], value_projection[:, cols]], axis=1)
        if key_ids is None:
            id_row = jnp.zeros((ID_ROWS, 2 * chunk_width), jnp.bfloat16)
            id_row = id_row.at[0, :tok_rows].set((doc_ids + 1).astype(jnp.bfloat16))
            paired = jnp.concatenate([paired, id_row], axis=0)
        if SERIAL_SENDS and previous is not None:
            paired, _ = lax.optimization_barrier((paired, previous))
        earlier = [passed_along(paired, "ctx", distance) for distance in range(blocks, 0, -1)]
        previous = earlier
        if key_ids is None:
            key_ids = jnp.concatenate(
                [piece[tok_rows, :tok_rows] for piece in earlier + [paired]], axis=0
            ).astype(jnp.float32)[None, :]
        query_part, own_part, cross_parts = head_group_grads(
            windows,
            query_ids,
            key_ids,
            query_proj[:, qcols],
            weighted[:, qcols],
            earlier + [paired],
        )
        query_pieces.append(query_part)
        summed = own_part
        for index, piece in enumerate(cross_parts):
            arrived = passed_along(piece, "ctx", index - blocks)
            summed = summed + arrived.astype(jnp.float32)
        key_pieces.append(summed[:, :chunk_width])
        value_pieces.append(summed[:, chunk_width:])
    query_grad = jnp.concatenate(query_pieces, axis=1)
    key_grad = jnp.concatenate(key_pieces, axis=1).astype(jnp.bfloat16)
    value_grad = jnp.concatenate(value_pieces, axis=1).astype(jnp.bfloat16)
    return (query_grad, key_grad, value_grad)


def solution(mesh):
    in_specs = (
        P(("group", "ctx"), "tsp"),
        P(("group", "ctx"), "tsp"),
        P(("group", "ctx"), "tsp"),
        P(("group", "ctx", "tsp"), None),
        P(("group", "ctx")),
        P("group"),
        P("tsp"),
    )
    out_specs = (P(("group", "ctx"), "tsp"), P(("group", "ctx"), "tsp"), P(("group", "ctx"), "tsp"))
    return jax.shard_map(
        on_device, mesh=mesh, in_specs=in_specs, out_specs=out_specs, check_vma=False
    )
```

```python
import functools
import jax
import jax.numpy as jnp
from jax import lax
from jax.experimental import pallas as pl
from jax.experimental.pallas import tpu as pltpu
from jax.sharding import PartitionSpec as P

HEAD_DIMENSION = 128
WINDOW = 1024
ID_ROWS = 16
score_scale = 168.0 ** (-0.5)


def _nt(a, b):
    return lax.dot_general(a, b, (((1,), (1,)), ((), ())), preferred_element_type=jnp.float32)


def _tn(a, b):
    return lax.dot_general(a, b, (((0,), (0,)), ((), ())), preferred_element_type=jnp.float32)


def _nn(a, b):
    return lax.dot_general(a, b, (((1,), (0,)), ((), ())), preferred_element_type=jnp.float32)


def attention_kernel(win_ref, odd_ref, qid_ref, q_ref, g_ref, *rest, group_size):
    r1, r2, r3, r4, r5, own = rest[:6]
    dq_ref, p4_ref, p2_ref, p1_ref, p3_ref, b3_ref, own_ref = rest[6:]
    d = HEAD_DIMENSION
    rows = q_ref.shape[0]
    width = own.shape[1] // 2
    odd = odd_ref[0] == 1

    def pick(odd_source, even_source):
        def load(index):
            return jnp.where(odd, odd_source[index], even_source[index])
        return load

    def plain(ref):
        def load(index):
            return ref[index]
        return load

    sources = [plain(r4), pick(r3, r5), plain(r2), pick(r1, r3), plain(own)]
    pieces = len(sources)
    key_count = pieces * rows
    row = lax.broadcasted_iota(jnp.int32, (rows, key_count), 0)
    col = lax.broadcasted_iota(jnp.int32, (rows, key_count), 1)
    offset = row + (key_count - rows) - col
    key_ids = jnp.concatenate(
        [src((slice(rows, rows + 1), slice(0, rows))).astype(jnp.float32) for src in sources], axis=1
    )
    base_live = (offset >= 0) & (key_ids == qid_ref[...])
    for kv in range(width // d):
        keys = [src((slice(0, rows), slice(kv * d, (kv + 1) * d))) for src in sources]
        values = [src((slice(0, rows), slice(width + kv * d, width + (kv + 1) * d))) for src in sources]
        parts = kv_head(win_ref, q_ref, g_ref, dq_ref, keys, values, offset, base_live, kv, group_size)
        kcols = slice(kv * d, (kv + 1) * d)
        vcols = slice(width + kv * d, width + (kv + 1) * d)
        for target, p in ((p4_ref, 0), (p2_ref, 2), (p1_ref, 3), (p3_ref, 1)):
            target[:, kcols] = parts[p][0].astype(target.dtype)
            target[:, vcols] = parts[p][1].astype(target.dtype)
        b3_ref[:, kcols] = jnp.where(odd, parts[1][0], parts[3][0]).astype(b3_ref.dtype)
        b3_ref[:, vcols] = jnp.where(odd, parts[1][1], parts[3][1]).astype(b3_ref.dtype)
        own_ref[:, kcols] = parts[4][0]
        own_ref[:, vcols] = parts[4][1]


def kv_head(win_ref, q_ref, g_ref, dq_ref, keys, values, offset, base_live, kv, group_size):
    d = HEAD_DIMENSION
    pieces = len(keys)
    piece_rows = q_ref.shape[0]
    key_acc = [jnp.zeros((piece_rows, d), jnp.float32) for _ in range(pieces)]
    value_acc = [jnp.zeros((piece_rows, d), jnp.float32) for _ in range(pieces)]
    for h in range(group_size):
        head = kv * group_size + h
        query = q_ref[:, head * d : (head + 1) * d]
        grad = g_ref[:, head * d : (head + 1) * d]
        scores = jnp.concatenate([_nt(query, key) for key in keys], axis=1) * score_scale
        live = base_live & (offset < win_ref[head])
        scores = jnp.where(live, scores, jnp.float32(-1e30))
        top = jnp.max(scores, axis=1, keepdims=True)
        prob = jnp.exp(scores - top)
        prob = prob / jnp.sum(prob, axis=1, keepdims=True)
        prob_low = prob.astype(jnp.bfloat16)
        attended = _nn(prob_low[:, :piece_rows], values[0])
        for p in range(1, pieces):
            attended = attended + _nn(prob_low[:, p * piece_rows : (p + 1) * piece_rows], values[p])
        attended = attended.astype(jnp.bfloat16).astype(jnp.float32)
        delta = jnp.sum(grad.astype(jnp.float32) * attended, axis=1, keepdims=True)
        dprob = jnp.concatenate([_nt(grad, value) for value in values], axis=1)
        dscore = (prob * (dprob - delta)).astype(jnp.bfloat16)
        query_acc = _nn(dscore[:, :piece_rows], keys[0])
        for p in range(1, pieces):
            query_acc = query_acc + _nn(dscore[:, p * piece_rows : (p + 1) * piece_rows], keys[p])
        dq_ref[:, head * d : (head + 1) * d] = (query_acc * score_scale).astype(dq_ref.dtype)
        for p in range(pieces):
            cols = slice(p * piece_rows, (p + 1) * piece_rows)
            key_acc[p] = key_acc[p] + _tn(dscore[:, cols], query)
            value_acc[p] = value_acc[p] + _tn(prob_low[:, cols], grad)
    return [(key_acc[p] * score_scale, value_acc[p]) for p in range(pieces)]


def head_group_grads(windows, odd, query_ids, query, grad, payloads):
    rows = query.shape[0]
    pair_width = payloads[0].shape[1]
    group_size = 2 * query.shape[1] // pair_width
    vmem = pl.BlockSpec(memory_space=pltpu.VMEM)
    smem = pl.BlockSpec(memory_space=pltpu.SMEM)
    wide = jax.ShapeDtypeStruct((rows, pair_width), jnp.float32)
    low = jax.ShapeDtypeStruct((rows, pair_width), jnp.bfloat16)
    out_shape = [jax.ShapeDtypeStruct(query.shape, jnp.bfloat16), wide, wide, low, low, low, wide]
    kernel = functools.partial(attention_kernel, group_size=group_size)
    return pl.pallas_call(
        kernel,
        out_shape=out_shape,
        in_specs=[smem, smem] + [vmem] * (3 + len(payloads)),
        out_specs=[vmem] * len(out_shape),
        name="attention_group",
    )(windows, odd, query_ids, query, grad, *payloads)


def passed_along(value, axis, steps):
    count = lax.axis_size(axis)
    initial, last = (max(0, -steps), min(count, count - steps))
    return lax.ppermute(value, axis, [(source, source + steps) for source in range(initial, last)])


def permuted(value, axis, pairs):
    return lax.ppermute(value, axis, [pair for pair in pairs if 0 <= pair[1] < lax.axis_size(axis)])


def on_device(query_proj, key_proj, value_projection, grad_out, doc_ids, advantages, head_window):
    tok_rows = query_proj.shape[0]
    kv_width = key_proj.shape[1]
    count = lax.axis_size("ctx")
    assert WINDOW // tok_rows == 4 and count % 2 == 0
    index = lax.axis_index("ctx")
    odd = (index % 2).astype(jnp.int32).reshape(1)
    doc_count = advantages.shape[0]
    matches = doc_ids[:, None] == jnp.arange(doc_count, dtype=jnp.int32)[None, :]
    token_weight = jnp.sum(jnp.where(matches, advantages[None, :], jnp.float32(0.0)), axis=1)
    grad_local = lax.all_to_all(grad_out, "tsp", split_axis=1, concat_axis=0, tiled=True)
    weighted = (token_weight[:, None] * grad_local.astype(jnp.float32)).astype(jnp.bfloat16)
    query_ids = (doc_ids + 1).astype(jnp.float32)[:, None]

    paired = jnp.concatenate([key_proj, value_projection], axis=1)
    id_rows = jnp.zeros((ID_ROWS, 2 * kv_width), jnp.bfloat16)
    id_rows = id_rows.at[0, :tok_rows].set((doc_ids + 1).astype(jnp.bfloat16))
    payload = jnp.concatenate([paired, id_rows], axis=0)

    evens = range(0, count, 2)
    odds = range(1, count, 2)
    everyone = range(count)
    swap = [(c, c + 1) for c in evens] + [(c, c - 1) for c in odds]
    got1 = permuted(payload, "ctx", [(c, c + 1) for c in evens])
    got2 = permuted(payload, "ctx", [(c, c + 2) for c in everyone])
    got3 = permuted(got2, "ctx", swap)
    got4 = permuted(got2, "ctx", [(c, c + 2) for c in everyone])
    got5 = permuted(got4, "ctx", [(c, c - 1) for c in odds])

    query_grad, part4, part2, part1, part3, back3, own_part = head_group_grads(
        head_window, odd, query_ids, query_proj, weighted, [got1, got2, got3, got4, got5, payload]
    )
    from5 = permuted(part3, "ctx", [(c, c + 1) for c in evens])
    from3 = permuted(back3, "ctx", swap)
    from1 = permuted(part1, "ctx", [(c, c - 1) for c in odds])
    send4 = (part4 + from5.astype(jnp.float32)).astype(jnp.bfloat16)
    from4 = permuted(send4, "ctx", [(c, c - 2) for c in everyone])
    send2 = (part2 + from4.astype(jnp.float32) + from3.astype(jnp.float32)).astype(jnp.bfloat16)
    from2 = permuted(send2, "ctx", [(c, c - 2) for c in everyone])
    summed = own_part + from2.astype(jnp.float32) + from1.astype(jnp.float32)
    key_grad = summed[:, :kv_width].astype(jnp.bfloat16)
    value_grad = summed[:, kv_width:].astype(jnp.bfloat16)
    return (query_grad, key_grad, value_grad)


def solution(mesh):
    in_specs = (
        P(("group", "ctx"), "tsp"),
        P(("group", "ctx"), "tsp"),
        P(("group", "ctx"), "tsp"),
        P(("group", "ctx", "tsp"), None),
        P(("group", "ctx")),
        P("group"),
        P("tsp"),
    )
    out_specs = (P(("group", "ctx"), "tsp"), P(("group", "ctx"), "tsp"), P(("group", "ctx"), "tsp"))
    return jax.shard_map(
        on_device, mesh=mesh, in_specs=in_specs, out_specs=out_specs, check_vma=False
    )
```

```python
import functools
import jax
import jax.numpy as jnp
from jax import lax
from jax.experimental import pallas as pl
from jax.experimental.pallas import tpu as pltpu
from jax.sharding import PartitionSpec as P

HEAD_DIMENSION = 128
WINDOW = 1024
ID_ROWS = 16
score_scale = 168.0 ** (-0.5)


def _nt(a, b):
    return lax.dot_general(a, b, (((1,), (1,)), ((), ())), preferred_element_type=jnp.float32)


def _tn(a, b):
    return lax.dot_general(a, b, (((0,), (0,)), ((), ())), preferred_element_type=jnp.float32)


def _nn(a, b):
    return lax.dot_general(a, b, (((1,), (0,)), ((), ())), preferred_element_type=jnp.float32)


def attention_kernel(win_ref, odd_ref, qid_ref, q_ref, g_ref, *rest, group_size):
    r1, r2, r3, r4, r5, own = rest[:6]
    dq_ref, p4_ref, p2_ref, p1_ref, p3_ref, b3_ref, own_ref = rest[6:]
    d = HEAD_DIMENSION
    rows = q_ref.shape[0]
    width = own.shape[1] // 2
    odd = odd_ref[0] == 1

    def pick(odd_source, even_source):
        def load(index):
            return jnp.where(odd, odd_source[index], even_source[index])

        return load

    def plain(ref):
        def load(index):
            return ref[index]

        return load

    sources = [plain(r4), pick(r3, r5), plain(r2), pick(r1, r3), plain(own)]
    pieces = len(sources)
    key_count = pieces * rows
    row = lax.broadcasted_iota(jnp.int32, (rows, key_count), 0)
    col = lax.broadcasted_iota(jnp.int32, (rows, key_count), 1)
    offset = row + (key_count - rows) - col
    key_ids = jnp.concatenate(
        [src((slice(rows, rows + 1), slice(0, rows))).astype(jnp.float32) for src in sources], axis=1
    )
    base_live = (offset >= 0) & (key_ids == qid_ref[...])
    for kv in range(width // d):
        keys = [src((slice(0, rows), slice(kv * d, (kv + 1) * d))) for src in sources]
        values = [src((slice(0, rows), slice(width + kv * d, width + (kv + 1) * d))) for src in sources]
        parts = kv_head(win_ref, q_ref, g_ref, dq_ref, keys, values, offset, base_live, kv, group_size)
        kcols = slice(kv * d, (kv + 1) * d)
        vcols = slice(width + kv * d, width + (kv + 1) * d)
        for target, p in ((p4_ref, 0), (p2_ref, 2), (p1_ref, 3), (p3_ref, 1)):
            target[:, kcols] = parts[p][0].astype(target.dtype)
            target[:, vcols] = parts[p][1].astype(target.dtype)
        b3_ref[:, kcols] = jnp.where(odd, parts[1][0], parts[3][0]).astype(b3_ref.dtype)
        b3_ref[:, vcols] = jnp.where(odd, parts[1][1], parts[3][1]).astype(b3_ref.dtype)
        own_ref[:, kcols] = parts[4][0]
        own_ref[:, vcols] = parts[4][1]


def kv_head(win_ref, q_ref, g_ref, dq_ref, keys, values, offset, base_live, kv, group_size):
    d = HEAD_DIMENSION
    pieces = len(keys)
    piece_rows = q_ref.shape[0]
    key_acc = [jnp.zeros((piece_rows, d), jnp.float32) for _ in range(pieces)]
    value_acc = [jnp.zeros((piece_rows, d), jnp.float32) for _ in range(pieces)]
    for h in range(group_size):
        head = kv * group_size + h
        query = q_ref[:, head * d : (head + 1) * d]
        grad = g_ref[:, head * d : (head + 1) * d]
        scores = jnp.concatenate([_nt(query, key) for key in keys], axis=1) * score_scale
        live = base_live & (offset < win_ref[head])
        scores = jnp.where(live, scores, jnp.float32(-1e30))
        top = jnp.max(scores, axis=1, keepdims=True)
        prob = jnp.exp(scores - top)
        prob = prob / jnp.sum(prob, axis=1, keepdims=True)
        prob_low = prob.astype(jnp.bfloat16)
        attended = _nn(prob_low[:, :piece_rows], values[0])
        for p in range(1, pieces):
            attended = attended + _nn(prob_low[:, p * piece_rows : (p + 1) * piece_rows], values[p])
        attended = attended.astype(jnp.bfloat16).astype(jnp.float32)
        delta = jnp.sum(grad.astype(jnp.float32) * attended, axis=1, keepdims=True)
        dprob = jnp.concatenate([_nt(grad, value) for value in values], axis=1)
        dscore = (prob * (dprob - delta)).astype(jnp.bfloat16)
        query_acc = _nn(dscore[:, :piece_rows], keys[0])
        for p in range(1, pieces):
            query_acc = query_acc + _nn(dscore[:, p * piece_rows : (p + 1) * piece_rows], keys[p])
        dq_ref[:, head * d : (head + 1) * d] = (query_acc * score_scale).astype(dq_ref.dtype)
        for p in range(pieces):
            cols = slice(p * piece_rows, (p + 1) * piece_rows)
            key_acc[p] = key_acc[p] + _tn(dscore[:, cols], query)
            value_acc[p] = value_acc[p] + _tn(prob_low[:, cols], grad)
    return [(key_acc[p] * score_scale, value_acc[p]) for p in range(pieces)]


def head_group_grads(windows, odd, query_ids, query, grad, payloads):
    rows = query.shape[0]
    pair_width = payloads[0].shape[1]
    group_size = 2 * query.shape[1] // pair_width
    vmem = pl.BlockSpec(memory_space=pltpu.VMEM)
    smem = pl.BlockSpec(memory_space=pltpu.SMEM)
    wide = jax.ShapeDtypeStruct((rows, pair_width), jnp.float32)
    low = jax.ShapeDtypeStruct((rows, pair_width), jnp.bfloat16)
    out_shape = [jax.ShapeDtypeStruct(query.shape, jnp.bfloat16), wide, wide, low, low, low, wide]
    kernel = functools.partial(attention_kernel, group_size=group_size)
    return pl.pallas_call(
        kernel,
        out_shape=out_shape,
        in_specs=[smem, smem] + [vmem] * (3 + len(payloads)),
        out_specs=[vmem] * len(out_shape),
        name="attention_group",
    )(windows, odd, query_ids, query, grad, *payloads)


def permuted(value, axis, pairs):
    return lax.ppermute(value, axis, [pair for pair in pairs if 0 <= pair[1] < lax.axis_size(axis)])


def device_body(query_proj, key_proj, value_projection, grad_out, doc_ids, advantages, head_window):
    tok_rows = query_proj.shape[0]
    kv_width = key_proj.shape[1]
    count = lax.axis_size("ctx")
    assert WINDOW // tok_rows == 4 and count % 2 == 0
    index = lax.axis_index("ctx")
    odd = (index % 2).astype(jnp.int32).reshape(1)
    doc_count = advantages.shape[0]
    matches = doc_ids[:, None] == jnp.arange(doc_count, dtype=jnp.int32)[None, :]
    token_weight = jnp.sum(jnp.where(matches, advantages[None, :], jnp.float32(0.0)), axis=1)
    grad_local = lax.all_to_all(grad_out, "tsp", split_axis=1, concat_axis=0, tiled=True)
    weighted = (token_weight[:, None] * grad_local.astype(jnp.float32)).astype(jnp.bfloat16)
    query_ids = (doc_ids + 1).astype(jnp.float32)[:, None]

    paired = jnp.concatenate([key_proj, value_projection], axis=1)
    id_rows = jnp.zeros((ID_ROWS, 2 * kv_width), jnp.bfloat16)
    id_rows = id_rows.at[0, :tok_rows].set((doc_ids + 1).astype(jnp.bfloat16))
    payload = jnp.concatenate([paired, id_rows], axis=0)

    evens = range(0, count, 2)
    odds = range(1, count, 2)
    everyone = range(count)
    swap = [(c, c + 1) for c in evens] + [(c, c - 1) for c in odds]
    got1 = permuted(payload, "ctx", [(c, c + 1) for c in evens])
    got2 = permuted(payload, "ctx", [(c, c + 2) for c in everyone])
    got3 = permuted(got2, "ctx", swap)
    got4 = permuted(got2, "ctx", [(c, c + 2) for c in everyone])
    got5 = permuted(got4, "ctx", [(c, c - 1) for c in odds])

    query_grad, part4, part2, part1, part3, back3, own_part = head_group_grads(
        head_window, odd, query_ids, query_proj, weighted, [got1, got2, got3, got4, got5, payload]
    )
    from5 = permuted(part3, "ctx", [(c, c + 1) for c in evens])
    from3 = permuted(back3, "ctx", swap)
    from1 = permuted(part1, "ctx", [(c, c - 1) for c in odds])
    send4 = (part4 + from5.astype(jnp.float32)).astype(jnp.bfloat16)
    from4 = permuted(send4, "ctx", [(c, c - 2) for c in everyone])
    send2 = (part2 + from4.astype(jnp.float32) + from3.astype(jnp.float32)).astype(jnp.bfloat16)
    from2 = permuted(send2, "ctx", [(c, c - 2) for c in everyone])
    summed = own_part + from2.astype(jnp.float32) + from1.astype(jnp.float32)
    key_grad = summed[:, :kv_width].astype(jnp.bfloat16)
    value_grad = summed[:, kv_width:].astype(jnp.bfloat16)
    return (query_grad, key_grad, value_grad)


def solution(mesh):
    in_specs = (
        P(("group", "ctx"), "tsp"),
        P(("group", "ctx"), "tsp"),
        P(("group", "ctx"), "tsp"),
        P(("group", "ctx", "tsp"), None),
        P(("group", "ctx")),
        P("group"),
        P("tsp"),
    )
    out_specs = (P(("group", "ctx"), "tsp"), P(("group", "ctx"), "tsp"), P(("group", "ctx"), "tsp"))
    return jax.shard_map(
        device_body, mesh=mesh, in_specs=in_specs, out_specs=out_specs, check_vma=False
    )
```

```python
import functools
import jax
import jax.numpy as jnp
from jax import lax
from jax.experimental import pallas as pl
from jax.experimental.pallas import tpu as pltpu
from jax.sharding import PartitionSpec as P

HEAD_DIMENSION = 128
WINDOW = 1024
ID_ROWS = 16
CHUNK_HEADS = (2, 2)
score_scale = 168.0 ** (-0.5)


def _nt(a, b):
    return lax.dot_general(a, b, (((1,), (1,)), ((), ())), preferred_element_type=jnp.float32)


def _tn(a, b):
    return lax.dot_general(a, b, (((0,), (0,)), ((), ())), preferred_element_type=jnp.float32)


def _nn(a, b):
    return lax.dot_general(a, b, (((1,), (0,)), ((), ())), preferred_element_type=jnp.float32)


def attention_kernel(win_ref, odd_ref, qid_ref, q_ref, g_ref, *rest, group_size, first_head):
    r1, r2, r3, r4, r5, own = rest[:6]
    dq_ref, p4_ref, p2_ref, p1_ref, p3_ref, b3_ref, own_ref = rest[6:]
    d = HEAD_DIMENSION
    rows = q_ref.shape[0]
    width = own.shape[1] // 2
    odd = odd_ref[0] == 1

    def pick(odd_source, even_source):
        def load(index):
            return jnp.where(odd, odd_source[index], even_source[index])

        return load

    def plain(ref):
        def load(index):
            return ref[index]

        return load

    sources = [plain(r4), pick(r3, r5), plain(r2), pick(r1, r3), plain(own)]
    pieces = len(sources)
    key_count = pieces * rows
    row = lax.broadcasted_iota(jnp.int32, (rows, key_count), 0)
    col = lax.broadcasted_iota(jnp.int32, (rows, key_count), 1)
    offset = row + (key_count - rows) - col
    key_ids = jnp.concatenate(
        [src((slice(rows, rows + 1), slice(0, rows))).astype(jnp.float32) for src in sources], axis=1
    )
    base_live = (offset >= 0) & (key_ids == qid_ref[...])
    for kv in range(width // d):
        keys = [src((slice(0, rows), slice(kv * d, (kv + 1) * d))) for src in sources]
        values = [src((slice(0, rows), slice(width + kv * d, width + (kv + 1) * d))) for src in sources]
        parts = kv_head(win_ref, q_ref, g_ref, dq_ref, keys, values, offset, base_live, kv, group_size,
                        first_head)
        kcols = slice(kv * d, (kv + 1) * d)
        vcols = slice(width + kv * d, width + (kv + 1) * d)
        for target, p in ((p4_ref, 0), (p2_ref, 2), (p1_ref, 3), (p3_ref, 1)):
            target[:, kcols] = parts[p][0].astype(target.dtype)
            target[:, vcols] = parts[p][1].astype(target.dtype)
        b3_ref[:, kcols] = jnp.where(odd, parts[1][0], parts[3][0]).astype(b3_ref.dtype)
        b3_ref[:, vcols] = jnp.where(odd, parts[1][1], parts[3][1]).astype(b3_ref.dtype)
        own_ref[:, kcols] = parts[4][0]
        own_ref[:, vcols] = parts[4][1]


def kv_head(win_ref, q_ref, g_ref, dq_ref, keys, values, offset, base_live, kv, group_size,
            first_head):
    d = HEAD_DIMENSION
    pieces = len(keys)
    piece_rows = q_ref.shape[0]
    key_acc = [jnp.zeros((piece_rows, d), jnp.float32) for _ in range(pieces)]
    value_acc = [jnp.zeros((piece_rows, d), jnp.float32) for _ in range(pieces)]
    for h in range(group_size):
        head = kv * group_size + h
        column = (first_head + head) * d
        query = q_ref[:, column : column + d]
        grad = g_ref[:, column : column + d]
        scores = jnp.concatenate([_nt(query, key) for key in keys], axis=1) * score_scale
        live = base_live & (offset < win_ref[first_head + head])
        scores = jnp.where(live, scores, jnp.float32(-1e30))
        top = jnp.max(scores, axis=1, keepdims=True)
        prob = jnp.exp(scores - top)
        prob = prob / jnp.sum(prob, axis=1, keepdims=True)
        prob_low = prob.astype(jnp.bfloat16)
        attended = _nn(prob_low[:, :piece_rows], values[0])
        for p in range(1, pieces):
            attended = attended + _nn(prob_low[:, p * piece_rows : (p + 1) * piece_rows], values[p])
        attended = attended.astype(jnp.bfloat16).astype(jnp.float32)
        delta = jnp.sum(grad.astype(jnp.float32) * attended, axis=1, keepdims=True)
        dprob = jnp.concatenate([_nt(grad, value) for value in values], axis=1)
        dscore = (prob * (dprob - delta)).astype(jnp.bfloat16)
        query_acc = _nn(dscore[:, :piece_rows], keys[0])
        for p in range(1, pieces):
            query_acc = query_acc + _nn(dscore[:, p * piece_rows : (p + 1) * piece_rows], keys[p])
        dq_ref[:, head * d : (head + 1) * d] = (query_acc * score_scale).astype(dq_ref.dtype)
        for p in range(pieces):
            cols = slice(p * piece_rows, (p + 1) * piece_rows)
            key_acc[p] = key_acc[p] + _tn(dscore[:, cols], query)
            value_acc[p] = value_acc[p] + _tn(prob_low[:, cols], grad)
    return [(key_acc[p] * score_scale, value_acc[p]) for p in range(pieces)]


def head_group_grads(windows, odd, query_ids, query, grad, payloads, group_size, first_head):
    rows = query.shape[0]
    pair_width = payloads[0].shape[1]
    vmem = pl.BlockSpec(memory_space=pltpu.VMEM)
    smem = pl.BlockSpec(memory_space=pltpu.SMEM)
    wide = jax.ShapeDtypeStruct((rows, pair_width), jnp.float32)
    low = jax.ShapeDtypeStruct((rows, pair_width), jnp.bfloat16)
    dq_shape = jax.ShapeDtypeStruct((rows, group_size * pair_width // 2), jnp.bfloat16)
    out_shape = [dq_shape, wide, wide, low, low, low, wide]
    kernel = functools.partial(attention_kernel, group_size=group_size, first_head=first_head)
    return pl.pallas_call(
        kernel,
        out_shape=out_shape,
        in_specs=[smem, smem] + [vmem] * (3 + len(payloads)),
        out_specs=[vmem] * len(out_shape),
        name="attention_group",
    )(windows, odd, query_ids, query, grad, *payloads)


def permuted(value, axis, pairs):
    return lax.ppermute(value, axis, [pair for pair in pairs if 0 <= pair[1] < lax.axis_size(axis)])


def device_body(query_proj, key_proj, value_projection, grad_out, doc_ids, advantages, head_window):
    tok_rows = query_proj.shape[0]
    kv_width = key_proj.shape[1]
    count = lax.axis_size("ctx")
    assert WINDOW // tok_rows == 4 and count % 2 == 0
    index = lax.axis_index("ctx")
    odd = (index % 2).astype(jnp.int32).reshape(1)
    doc_count = advantages.shape[0]
    matches = doc_ids[:, None] == jnp.arange(doc_count, dtype=jnp.int32)[None, :]
    token_weight = jnp.sum(jnp.where(matches, advantages[None, :], jnp.float32(0.0)), axis=1)
    grad_local = lax.all_to_all(grad_out, "tsp", split_axis=1, concat_axis=0, tiled=True)
    weighted = (token_weight[:, None] * grad_local.astype(jnp.float32)).astype(jnp.bfloat16)
    query_ids = (doc_ids + 1).astype(jnp.float32)[:, None]

    kv_heads = kv_width // HEAD_DIMENSION
    group_size = query_proj.shape[1] // kv_width
    evens = range(0, count, 2)
    odds = range(1, count, 2)
    everyone = range(count)
    swap = [(c, c + 1) for c in evens] + [(c, c - 1) for c in odds]
    chunk_sizes = CHUNK_HEADS if sum(CHUNK_HEADS) == kv_heads else (kv_heads,)
    query_pieces, key_pieces, value_pieces = [], [], []
    previous = None
    chunk_first = 0
    for chunk_heads in chunk_sizes:
        width = chunk_heads * HEAD_DIMENSION
        cols = slice(chunk_first * HEAD_DIMENSION, chunk_first * HEAD_DIMENSION + width)
        paired = jnp.concatenate([key_proj[:, cols], value_projection[:, cols]], axis=1)
        id_rows = jnp.zeros((ID_ROWS, 2 * width), jnp.bfloat16)
        id_rows = id_rows.at[0, :tok_rows].set((doc_ids + 1).astype(jnp.bfloat16))
        payload = jnp.concatenate([paired, id_rows], axis=0)
        if previous is not None:
            payload, _ = lax.optimization_barrier((payload, previous))
        got1 = permuted(payload, "ctx", [(c, c + 1) for c in evens])
        got2 = permuted(payload, "ctx", [(c, c + 2) for c in everyone])
        got3 = permuted(got2, "ctx", swap)
        got4 = permuted(got2, "ctx", [(c, c + 2) for c in everyone])
        got5 = permuted(got4, "ctx", [(c, c - 1) for c in odds])
        previous = (got1, got3, got5)
        query_part, part4, part2, part1, part3, back3, own_part = head_group_grads(
            head_window, odd, query_ids, query_proj, weighted,
            [got1, got2, got3, got4, got5, payload], group_size, chunk_first * group_size,
        )
        chunk_first += chunk_heads
        from5 = permuted(part3, "ctx", [(c, c + 1) for c in evens])
        from3 = permuted(back3, "ctx", swap)
        from1 = permuted(part1, "ctx", [(c, c - 1) for c in odds])
        send4 = (part4 + from5.astype(jnp.float32)).astype(jnp.bfloat16)
        from4 = permuted(send4, "ctx", [(c, c - 2) for c in everyone])
        send2 = (part2 + from4.astype(jnp.float32) + from3.astype(jnp.float32)).astype(jnp.bfloat16)
        from2 = permuted(send2, "ctx", [(c, c - 2) for c in everyone])
        summed = own_part + from2.astype(jnp.float32) + from1.astype(jnp.float32)
        query_pieces.append(query_part)
        key_pieces.append(summed[:, :width])
        value_pieces.append(summed[:, width:])
    query_grad = jnp.concatenate(query_pieces, axis=1)
    key_grad = jnp.concatenate(key_pieces, axis=1).astype(jnp.bfloat16)
    value_grad = jnp.concatenate(value_pieces, axis=1).astype(jnp.bfloat16)
    return (query_grad, key_grad, value_grad)


def solution(mesh):
    in_specs = (
        P(("group", "ctx"), "tsp"),
        P(("group", "ctx"), "tsp"),
        P(("group", "ctx"), "tsp"),
        P(("group", "ctx", "tsp"), None),
        P(("group", "ctx")),
        P("group"),
        P("tsp"),
    )
    out_specs = (P(("group", "ctx"), "tsp"), P(("group", "ctx"), "tsp"), P(("group", "ctx"), "tsp"))
    return jax.shard_map(
        device_body, mesh=mesh, in_specs=in_specs, out_specs=out_specs, check_vma=False
    )
```

```python
import functools
import jax
import jax.numpy as jnp
from jax import lax
from jax.experimental import pallas as pl
from jax.experimental.pallas import tpu as pltpu
from jax.sharding import PartitionSpec as P

HEAD_DIMENSION = 128
WINDOW = 1024
ID_ROWS = 16
score_scale = 168.0 ** (-0.5)


def _nt(a, b):
    return lax.dot_general(a, b, (((1,), (1,)), ((), ())), preferred_element_type=jnp.float32)


def _tn(a, b):
    return lax.dot_general(a, b, (((0,), (0,)), ((), ())), preferred_element_type=jnp.float32)


def _nn(a, b):
    return lax.dot_general(a, b, (((1,), (0,)), ((), ())), preferred_element_type=jnp.float32)


def attention_kernel(win_ref, odd_ref, qid_ref, q_ref, g_ref, *rest, group_size):
    r1, r2, r3, r4, r5, own = rest[:6]
    dq_ref, p4_ref, p2_ref, p1_ref, p3_ref, b3_ref, own_ref = rest[6:]
    d = HEAD_DIMENSION
    rows = q_ref.shape[0]
    width = own.shape[1] // 2
    odd = odd_ref[0] == 1

    def pick(odd_source, even_source):
        def load(index):
            return jnp.where(odd, odd_source[index], even_source[index])
        return load

    def plain(ref):
        def load(index):
            return ref[index]
        return load

    sources = [plain(r4), pick(r3, r5), plain(r2), pick(r1, r3), plain(own)]
    pieces = len(sources)
    key_count = pieces * rows
    row = lax.broadcasted_iota(jnp.int32, (rows, key_count), 0)
    col = lax.broadcasted_iota(jnp.int32, (rows, key_count), 1)
    offset = row + (key_count - rows) - col
    key_ids = jnp.concatenate(
        [src((slice(rows, rows + 1), slice(0, rows))).astype(jnp.float32) for src in sources], axis=1
    )
    base_live = (offset >= 0) & (key_ids == qid_ref[...])
    for kv in range(width // d):
        keys = [src((slice(0, rows), slice(kv * d, (kv + 1) * d))) for src in sources]
        values = [src((slice(0, rows), slice(width + kv * d, width + (kv + 1) * d))) for src in sources]
        parts = kv_head(win_ref, q_ref, g_ref, dq_ref, keys, values, offset, base_live, kv, group_size)
        kcols = slice(kv * d, (kv + 1) * d)
        vcols = slice(width + kv * d, width + (kv + 1) * d)
        for target, p in ((p4_ref, 0), (p2_ref, 2), (p1_ref, 3), (p3_ref, 1)):
            target[:, kcols] = parts[p][0].astype(target.dtype)
            target[:, vcols] = parts[p][1].astype(target.dtype)
        b3_ref[:, kcols] = jnp.where(odd, parts[1][0], parts[3][0]).astype(b3_ref.dtype)
        b3_ref[:, vcols] = jnp.where(odd, parts[1][1], parts[3][1]).astype(b3_ref.dtype)
        own_ref[:, kcols] = parts[4][0]
        own_ref[:, vcols] = parts[4][1]


def kv_head(win_ref, q_ref, g_ref, dq_ref, keys, values, offset, base_live, kv, group_size):
    d = HEAD_DIMENSION
    pieces = len(keys)
    piece_rows = q_ref.shape[0]
    key_acc = [jnp.zeros((piece_rows, d), jnp.float32) for _ in range(pieces)]
    value_acc = [jnp.zeros((piece_rows, d), jnp.float32) for _ in range(pieces)]
    for h in range(group_size):
        head = kv * group_size + h
        query = q_ref[:, head * d : (head + 1) * d]
        grad = g_ref[:, head * d : (head + 1) * d]
        scores = jnp.concatenate([_nt(query, key) for key in keys], axis=1) * score_scale
        live = base_live & (offset < win_ref[head])
        scores = jnp.where(live, scores, jnp.float32(-1e30))
        top = jnp.max(scores, axis=1, keepdims=True)
        prob = jnp.exp(scores - top)
        prob = prob * (1.0 / jnp.sum(prob, axis=1, keepdims=True))
        prob_low = prob.astype(jnp.bfloat16)
        attended = _nn(prob_low[:, :piece_rows], values[0])
        for p in range(1, pieces):
            attended = attended + _nn(prob_low[:, p * piece_rows : (p + 1) * piece_rows], values[p])
        attended = attended.astype(jnp.bfloat16).astype(jnp.float32)
        delta = jnp.sum(grad.astype(jnp.float32) * attended, axis=1, keepdims=True)
        dprob = jnp.concatenate([_nt(grad, value) for value in values], axis=1)
        dscore = (prob * (dprob - delta)).astype(jnp.bfloat16)
        query_acc = _nn(dscore[:, :piece_rows], keys[0])
        for p in range(1, pieces):
            query_acc = query_acc + _nn(dscore[:, p * piece_rows : (p + 1) * piece_rows], keys[p])
        dq_ref[:, head * d : (head + 1) * d] = (query_acc * score_scale).astype(dq_ref.dtype)
        for p in range(pieces):
            cols = slice(p * piece_rows, (p + 1) * piece_rows)
            key_acc[p] = key_acc[p] + _tn(dscore[:, cols], query)
            value_acc[p] = value_acc[p] + _tn(prob_low[:, cols], grad)
    return [(key_acc[p] * score_scale, value_acc[p]) for p in range(pieces)]


def head_group_grads(windows, odd, query_ids, query, grad, payloads):
    rows = query.shape[0]
    pair_width = payloads[0].shape[1]
    group_size = 2 * query.shape[1] // pair_width
    vmem = pl.BlockSpec(memory_space=pltpu.VMEM)
    smem = pl.BlockSpec(memory_space=pltpu.SMEM)
    wide = jax.ShapeDtypeStruct((rows, pair_width), jnp.float32)
    low = jax.ShapeDtypeStruct((rows, pair_width), jnp.bfloat16)
    out_shape = [jax.ShapeDtypeStruct(query.shape, jnp.bfloat16), wide, wide, low, low, low, wide]
    kernel = functools.partial(attention_kernel, group_size=group_size)
    return pl.pallas_call(
        kernel,
        out_shape=out_shape,
        in_specs=[smem, smem] + [vmem] * (3 + len(payloads)),
        out_specs=[vmem] * len(out_shape),
        name="attention_group",
    )(windows, odd, query_ids, query, grad, *payloads)


def passed_along(value, axis, steps):
    count = lax.axis_size(axis)
    initial, last = (max(0, -steps), min(count, count - steps))
    return lax.ppermute(value, axis, [(source, source + steps) for source in range(initial, last)])


def permuted(value, axis, pairs):
    return lax.ppermute(value, axis, [pair for pair in pairs if 0 <= pair[1] < lax.axis_size(axis)])


def on_device(query_proj, key_proj, value_projection, grad_out, doc_ids, advantages, head_window):
    tok_rows = query_proj.shape[0]
    kv_width = key_proj.shape[1]
    count = lax.axis_size("ctx")
    assert WINDOW // tok_rows == 4 and count % 2 == 0
    index = lax.axis_index("ctx")
    odd = (index % 2).astype(jnp.int32).reshape(1)
    doc_count = advantages.shape[0]
    matches = doc_ids[:, None] == jnp.arange(doc_count, dtype=jnp.int32)[None, :]
    token_weight = jnp.sum(jnp.where(matches, advantages[None, :], jnp.float32(0.0)), axis=1)
    grad_local = lax.all_to_all(grad_out, "tsp", split_axis=1, concat_axis=0, tiled=True)
    weighted = (token_weight[:, None] * grad_local.astype(jnp.float32)).astype(jnp.bfloat16)
    query_ids = (doc_ids + 1).astype(jnp.float32)[:, None]

    paired = jnp.concatenate([key_proj, value_projection], axis=1)
    id_rows = jnp.zeros((ID_ROWS, 2 * kv_width), jnp.bfloat16)
    id_rows = id_rows.at[0, :tok_rows].set((doc_ids + 1).astype(jnp.bfloat16))
    payload = jnp.concatenate([paired, id_rows], axis=0)

    evens = range(0, count, 2)
    odds = range(1, count, 2)
    everyone = range(count)
    swap = [(c, c + 1) for c in evens] + [(c, c - 1) for c in odds]
    got1 = permuted(payload, "ctx", [(c, c + 1) for c in evens])
    got2 = permuted(payload, "ctx", [(c, c + 2) for c in everyone])
    got3 = permuted(got2, "ctx", swap)
    got4 = permuted(got2, "ctx", [(c, c + 2) for c in everyone])
    got5 = permuted(got4, "ctx", [(c, c - 1) for c in odds])

    query_grad, part4, part2, part1, part3, back3, own_part = head_group_grads(
        head_window, odd, query_ids, query_proj, weighted, [got1, got2, got3, got4, got5, payload]
    )
    from5 = permuted(part3, "ctx", [(c, c + 1) for c in evens])
    from3 = permuted(back3, "ctx", swap)
    from1 = permuted(part1, "ctx", [(c, c - 1) for c in odds])
    send4 = (part4 + from5.astype(jnp.float32)).astype(jnp.bfloat16)
    from4 = permuted(send4, "ctx", [(c, c - 2) for c in everyone])
    send2 = (part2 + from4.astype(jnp.float32) + from3.astype(jnp.float32)).astype(jnp.bfloat16)
    from2 = permuted(send2, "ctx", [(c, c - 2) for c in everyone])
    summed = own_part + from2.astype(jnp.float32) + from1.astype(jnp.float32)
    key_grad = summed[:, :kv_width].astype(jnp.bfloat16)
    value_grad = summed[:, kv_width:].astype(jnp.bfloat16)
    return (query_grad, key_grad, value_grad)


def solution(mesh):
    in_specs = (
        P(("group", "ctx"), "tsp"),
        P(("group", "ctx"), "tsp"),
        P(("group", "ctx"), "tsp"),
        P(("group", "ctx", "tsp"), None),
        P(("group", "ctx")),
        P("group"),
        P("tsp"),
    )
    out_specs = (P(("group", "ctx"), "tsp"), P(("group", "ctx"), "tsp"), P(("group", "ctx"), "tsp"))
    return jax.shard_map(
        on_device, mesh=mesh, in_specs=in_specs, out_specs=out_specs, check_vma=False
    )
```

```python
import functools
import jax
import jax.numpy as jnp
from jax import lax
from jax.experimental import pallas as pl
from jax.experimental.pallas import tpu as pltpu
from jax.sharding import PartitionSpec as P

HEAD_DIMENSION = 128
WINDOW = 1024
ID_ROWS = 16
HALVES = 2
score_scale = 168.0 ** (-0.5)


def _nt(a, b):
    return lax.dot_general(a, b, (((1,), (1,)), ((), ())), preferred_element_type=jnp.float32)


def _tn(a, b):
    return lax.dot_general(a, b, (((0,), (0,)), ((), ())), preferred_element_type=jnp.float32)


def _nn(a, b):
    return lax.dot_general(a, b, (((1,), (0,)), ((), ())), preferred_element_type=jnp.float32)


def attention_kernel(win_ref, odd_ref, qid_ref, q_ref, g_ref, *rest, group_size, first_head):
    key_refs = rest[:6]
    value_refs = rest[6:12]
    dq_ref, p4_ref, p2_ref, p1_ref, p3_ref, b3_ref, own_ref = rest[12:]
    d = HEAD_DIMENSION
    rows = q_ref.shape[0]
    width = key_refs[0].shape[1]
    odd = odd_ref[0] == 1

    def pick(odd_source, even_source):
        def load(index):
            return jnp.where(odd, odd_source[index], even_source[index])
        return load

    def plain(ref):
        def load(index):
            return ref[index]
        return load

    def arrange(refs):
        r1, r2, r3, r4, r5, own = refs
        return [plain(r4), pick(r3, r5), plain(r2), pick(r1, r3), plain(own)]

    key_sources = arrange(key_refs)
    value_sources = arrange(value_refs)
    pieces = len(key_sources)
    key_count = pieces * rows
    row = lax.broadcasted_iota(jnp.int32, (rows, key_count), 0)
    col = lax.broadcasted_iota(jnp.int32, (rows, key_count), 1)
    offset = row + (key_count - rows) - col
    key_ids = jnp.concatenate(
        [src((slice(rows, rows + 1), slice(0, rows))).astype(jnp.float32) for src in key_sources],
        axis=1,
    )
    base_live = (offset >= 0) & (key_ids == qid_ref[...])
    for kv in range(width // d):
        kcols = slice(kv * d, (kv + 1) * d)
        vcols = slice(width + kv * d, width + (kv + 1) * d)
        keys = [src((slice(0, rows), kcols)) for src in key_sources]
        values = [src((slice(0, rows), kcols)) for src in value_sources]
        parts = kv_head(win_ref, q_ref, g_ref, dq_ref, keys, values, offset, base_live, kv, group_size,
                        first_head)
        for target, p in ((p4_ref, 0), (p2_ref, 2), (p1_ref, 3), (p3_ref, 1)):
            target[:, kcols] = parts[p][0].astype(target.dtype)
            target[:, vcols] = parts[p][1].astype(target.dtype)
        b3_ref[:, kcols] = jnp.where(odd, parts[1][0], parts[3][0]).astype(b3_ref.dtype)
        b3_ref[:, vcols] = jnp.where(odd, parts[1][1], parts[3][1]).astype(b3_ref.dtype)
        own_ref[:, kcols] = parts[4][0]
        own_ref[:, vcols] = parts[4][1]


def kv_head(win_ref, q_ref, g_ref, dq_ref, keys, values, offset, base_live, kv, group_size,
            first_head):
    d = HEAD_DIMENSION
    pieces = len(keys)
    piece_rows = q_ref.shape[0]
    key_acc = [jnp.zeros((piece_rows, d), jnp.float32) for _ in range(pieces)]
    value_acc = [jnp.zeros((piece_rows, d), jnp.float32) for _ in range(pieces)]
    for h in range(group_size):
        head = kv * group_size + h
        query = q_ref[:, head * d : (head + 1) * d]
        grad = g_ref[:, head * d : (head + 1) * d]
        scores = jnp.concatenate([_nt(query, key) for key in keys], axis=1) * score_scale
        live = base_live & (offset < win_ref[first_head + head])
        scores = jnp.where(live, scores, jnp.float32(-1e30))
        top = jnp.max(scores, axis=1, keepdims=True)
        prob = jnp.exp(scores - top)
        prob = prob * (1.0 / jnp.sum(prob, axis=1, keepdims=True))
        prob_low = prob.astype(jnp.bfloat16)
        attended = _nn(prob_low[:, :piece_rows], values[0])
        for p in range(1, pieces):
            attended = attended + _nn(prob_low[:, p * piece_rows : (p + 1) * piece_rows], values[p])
        attended = attended.astype(jnp.bfloat16).astype(jnp.float32)
        delta = jnp.sum(grad.astype(jnp.float32) * attended, axis=1, keepdims=True)
        dprob = jnp.concatenate([_nt(grad, value) for value in values], axis=1)
        dscore = (prob * (dprob - delta)).astype(jnp.bfloat16)
        query_acc = _nn(dscore[:, :piece_rows], keys[0])
        for p in range(1, pieces):
            query_acc = query_acc + _nn(dscore[:, p * piece_rows : (p + 1) * piece_rows], keys[p])
        dq_ref[:, head * d : (head + 1) * d] = (query_acc * score_scale).astype(dq_ref.dtype)
        for p in range(pieces):
            cols = slice(p * piece_rows, (p + 1) * piece_rows)
            key_acc[p] = key_acc[p] + _tn(dscore[:, cols], query)
            value_acc[p] = value_acc[p] + _tn(prob_low[:, cols], grad)
    return [(key_acc[p] * score_scale, value_acc[p]) for p in range(pieces)]


def head_group_grads(windows, odd, query_ids, query, grad, payloads, half, halves):
    rows = query.shape[0]
    payload_rows = payloads[0].shape[0]
    kv_width = payloads[0].shape[1] // 2
    width = kv_width // halves
    group_size = query.shape[1] // kv_width
    smem = pl.BlockSpec(memory_space=pltpu.SMEM)
    key_spec = pl.BlockSpec((payload_rows, width), lambda i: (0, half))
    value_spec = pl.BlockSpec((payload_rows, width), lambda i: (0, halves + half))
    query_spec = pl.BlockSpec((rows, group_size * width), lambda i: (0, half))
    id_spec = pl.BlockSpec((rows, 1), lambda i: (0, 0))
    pair_spec = pl.BlockSpec((rows, 2 * width), lambda i: (0, 0))
    wide = jax.ShapeDtypeStruct((rows, 2 * width), jnp.float32)
    low = jax.ShapeDtypeStruct((rows, 2 * width), jnp.bfloat16)
    out_shape = [jax.ShapeDtypeStruct((rows, group_size * width), jnp.bfloat16)]
    out_shape += [wide, wide, low, low, low, wide]
    kernel = functools.partial(
        attention_kernel, group_size=group_size, first_head=half * group_size * width // HEAD_DIMENSION
    )
    return pl.pallas_call(
        kernel,
        out_shape=out_shape,
        grid=(1,),
        in_specs=[smem, smem, id_spec, query_spec, query_spec]
        + [key_spec] * len(payloads)
        + [value_spec] * len(payloads),
        out_specs=[pl.BlockSpec((rows, group_size * width), lambda i: (0, 0))] + [pair_spec] * 6,
        name="attention_group",
    )(windows, odd, query_ids, query, grad, *payloads, *payloads)


def passed_along(value, axis, steps):
    count = lax.axis_size(axis)
    initial, last = (max(0, -steps), min(count, count - steps))
    return lax.ppermute(value, axis, [(source, source + steps) for source in range(initial, last)])


def permuted(value, axis, pairs, scope=None):
    return lax.ppermute(value, axis, [pair for pair in pairs if 0 <= pair[1] < lax.axis_size(axis)])


def on_device(query_proj, key_proj, value_projection, grad_out, doc_ids, advantages, head_window):
    tok_rows = query_proj.shape[0]
    kv_width = key_proj.shape[1]
    count = lax.axis_size("ctx")
    assert WINDOW // tok_rows == 4 and count % 2 == 0
    index = lax.axis_index("ctx")
    odd = (index % 2).astype(jnp.int32).reshape(1)
    doc_count = advantages.shape[0]
    matches = doc_ids[:, None] == jnp.arange(doc_count, dtype=jnp.int32)[None, :]
    token_weight = jnp.sum(jnp.where(matches, advantages[None, :], jnp.float32(0.0)), axis=1)
    grad_local = lax.all_to_all(grad_out, "tsp", split_axis=1, concat_axis=0, tiled=True)
    weighted = (token_weight[:, None] * grad_local.astype(jnp.float32)).astype(jnp.bfloat16)
    query_ids = (doc_ids + 1).astype(jnp.float32)[:, None]

    paired = jnp.concatenate([key_proj, value_projection], axis=1)
    id_rows = jnp.zeros((ID_ROWS, 2 * kv_width), jnp.bfloat16)
    id_rows = id_rows.at[0, :].set(
        jnp.tile((doc_ids + 1).astype(jnp.bfloat16), 2 * kv_width // tok_rows)
    )
    payload = jnp.concatenate([paired, id_rows], axis=0)

    evens = range(0, count, 2)
    odds = range(1, count, 2)
    everyone = range(count)
    swap = [(c, c + 1) for c in evens] + [(c, c - 1) for c in odds]
    got1 = permuted(payload, "ctx", [(c, c + 1) for c in evens])
    got2 = permuted(payload, "ctx", [(c, c + 2) for c in everyone])
    got3 = permuted(got2, "ctx", swap)
    got4 = permuted(got2, "ctx", [(c, c + 2) for c in everyone])
    got5 = permuted(got4, "ctx", [(c, c - 1) for c in odds])

    halves = HALVES
    query_pieces, key_pieces, value_pieces = [], [], []
    for half in range(halves):
        query_part, part4, part2, part1, part3, back3, own_part = head_group_grads(
            head_window, odd, query_ids, query_proj, weighted,
            [got1, got2, got3, got4, got5, payload], half, halves,
        )
        tag = str(half)
        from5 = permuted(part3, "ctx", [(c, c + 1) for c in evens], "b5_" + tag)
        from3 = permuted(back3, "ctx", swap, "b3_" + tag)
        from1 = permuted(part1, "ctx", [(c, c - 1) for c in odds], "b1_" + tag)
        send4 = (part4 + from5.astype(jnp.float32)).astype(jnp.bfloat16)
        from4 = permuted(send4, "ctx", [(c, c - 2) for c in everyone], "b4_" + tag)
        send2 = (part2 + from4.astype(jnp.float32) + from3.astype(jnp.float32)).astype(jnp.bfloat16)
        from2 = permuted(send2, "ctx", [(c, c - 2) for c in everyone], "b2_" + tag)
        summed = own_part + from2.astype(jnp.float32) + from1.astype(jnp.float32)
        width = summed.shape[1] // 2
        query_pieces.append(query_part)
        key_pieces.append(summed[:, :width])
        value_pieces.append(summed[:, width:])
    query_grad = jnp.concatenate(query_pieces, axis=1)
    key_grad = jnp.concatenate(key_pieces, axis=1).astype(jnp.bfloat16)
    value_grad = jnp.concatenate(value_pieces, axis=1).astype(jnp.bfloat16)
    return (query_grad, key_grad, value_grad)


def solution(mesh):
    in_specs = (
        P(("group", "ctx"), "tsp"),
        P(("group", "ctx"), "tsp"),
        P(("group", "ctx"), "tsp"),
        P(("group", "ctx", "tsp"), None),
        P(("group", "ctx")),
        P("group"),
        P("tsp"),
    )
    out_specs = (P(("group", "ctx"), "tsp"), P(("group", "ctx"), "tsp"), P(("group", "ctx"), "tsp"))
    return jax.shard_map(
        on_device, mesh=mesh, in_specs=in_specs, out_specs=out_specs, check_vma=False
    )
```

```python
import functools
import jax
import jax.numpy as jnp
from jax import lax
from jax.experimental import pallas as pl
from jax.experimental.pallas import tpu as pltpu
from jax.sharding import PartitionSpec as P

HEAD_DIMENSION = 128
WINDOW = 1024
ID_ROWS = 16
HALVES = 2
score_scale = 168.0 ** (-0.5)


def _nt(a, b):
    return lax.dot_general(a, b, (((1,), (1,)), ((), ())), preferred_element_type=jnp.float32)


def _tn(a, b):
    return lax.dot_general(a, b, (((0,), (0,)), ((), ())), preferred_element_type=jnp.float32)


def _nn(a, b):
    return lax.dot_general(a, b, (((1,), (0,)), ((), ())), preferred_element_type=jnp.float32)


def attention_kernel(win_ref, odd_ref, qid_ref, q_ref, g_ref, *rest, group_size, first_head):
    key_refs = rest[:6]
    value_refs = rest[6:12]
    dq_ref, p4_ref, p2_ref, swap_ref, own_ref = rest[12:]
    d = HEAD_DIMENSION
    rows = q_ref.shape[0]
    width = key_refs[0].shape[1]
    odd = odd_ref[0] == 1

    def pick(odd_source, even_source):
        def load(index):
            return jnp.where(odd, odd_source[index], even_source[index])
        return load

    def plain(ref):
        def load(index):
            return ref[index]
        return load

    def arrange(refs):
        r1, r2, r3, r4, r5, own = refs
        return [plain(r4), pick(r3, r5), plain(r2), pick(r1, r3), plain(own)]

    key_sources = arrange(key_refs)
    value_sources = arrange(value_refs)
    pieces = len(key_sources)
    key_count = pieces * rows
    row = lax.broadcasted_iota(jnp.int32, (rows, key_count), 0)
    col = lax.broadcasted_iota(jnp.int32, (rows, key_count), 1)
    offset = row + (key_count - rows) - col
    key_ids = jnp.concatenate(
        [src((slice(rows, rows + 1), slice(0, rows))).astype(jnp.float32) for src in key_sources],
        axis=1,
    )
    base_live = (offset >= 0) & (key_ids == qid_ref[...])
    for kv in range(width // d):
        kcols = slice(kv * d, (kv + 1) * d)
        vcols = slice(width + kv * d, width + (kv + 1) * d)
        keys = [src((slice(0, rows), kcols)) for src in key_sources]
        values = [src((slice(0, rows), kcols)) for src in value_sources]
        parts = kv_head(win_ref, q_ref, g_ref, dq_ref, keys, values, offset, base_live, kv, group_size,
                        first_head)
        for target, p in ((p4_ref, 0), (p2_ref, 2)):
            target[:, kcols] = parts[p][0].astype(target.dtype)
            target[:, vcols] = parts[p][1].astype(target.dtype)
        for slot, (odd_part, even_part) in enumerate(((1, 3), (3, 1))):
            base = slot * 2 * width
            for side, cols in ((0, kcols), (1, vcols)):
                shifted = slice(base + cols.start, base + cols.stop)
                swap_ref[:, shifted] = jnp.where(
                    odd, parts[odd_part][side], parts[even_part][side]
                ).astype(swap_ref.dtype)
        own_ref[:, kcols] = parts[4][0]
        own_ref[:, vcols] = parts[4][1]


def kv_head(win_ref, q_ref, g_ref, dq_ref, keys, values, offset, base_live, kv, group_size,
            first_head):
    d = HEAD_DIMENSION
    pieces = len(keys)
    piece_rows = q_ref.shape[0]
    key_acc = [jnp.zeros((piece_rows, d), jnp.float32) for _ in range(pieces)]
    value_acc = [jnp.zeros((piece_rows, d), jnp.float32) for _ in range(pieces)]
    for h in range(group_size):
        head = kv * group_size + h
        query = q_ref[:, head * d : (head + 1) * d]
        grad = g_ref[:, head * d : (head + 1) * d]
        scores = jnp.concatenate([_nt(query, key) for key in keys], axis=1) * score_scale
        live = base_live & (offset < win_ref[first_head + head])
        scores = jnp.where(live, scores, jnp.float32(-1e30))
        top = jnp.max(scores, axis=1, keepdims=True)
        prob = jnp.exp(scores - top)
        prob = prob * (1.0 / jnp.sum(prob, axis=1, keepdims=True))
        prob_low = prob.astype(jnp.bfloat16)
        attended = _nn(prob_low[:, :piece_rows], values[0])
        for p in range(1, pieces):
            attended = attended + _nn(prob_low[:, p * piece_rows : (p + 1) * piece_rows], values[p])
        attended = attended.astype(jnp.bfloat16).astype(jnp.float32)
        delta = jnp.sum(grad.astype(jnp.float32) * attended, axis=1, keepdims=True)
        dprob = jnp.concatenate([_nt(grad, value) for value in values], axis=1)
        dscore = (prob * (dprob - delta)).astype(jnp.bfloat16)
        query_acc = _nn(dscore[:, :piece_rows], keys[0])
        for p in range(1, pieces):
            query_acc = query_acc + _nn(dscore[:, p * piece_rows : (p + 1) * piece_rows], keys[p])
        dq_ref[:, head * d : (head + 1) * d] = (query_acc * score_scale).astype(dq_ref.dtype)
        for p in range(pieces):
            cols = slice(p * piece_rows, (p + 1) * piece_rows)
            key_acc[p] = key_acc[p] + _tn(dscore[:, cols], query)
            value_acc[p] = value_acc[p] + _tn(prob_low[:, cols], grad)
    return [(key_acc[p] * score_scale, value_acc[p]) for p in range(pieces)]


def head_group_grads(windows, odd, query_ids, query, grad, payloads, half, halves):
    rows = query.shape[0]
    payload_rows = payloads[0].shape[0]
    kv_width = payloads[0].shape[1] // 2
    width = kv_width // halves
    group_size = query.shape[1] // kv_width
    smem = pl.BlockSpec(memory_space=pltpu.SMEM)
    key_spec = pl.BlockSpec((payload_rows, width), lambda i: (0, half))
    value_spec = pl.BlockSpec((payload_rows, width), lambda i: (0, halves + half))
    query_spec = pl.BlockSpec((rows, group_size * width), lambda i: (0, half))
    id_spec = pl.BlockSpec((rows, 1), lambda i: (0, 0))
    pair_spec = pl.BlockSpec((rows, 2 * width), lambda i: (0, 0))
    wide = jax.ShapeDtypeStruct((rows, 2 * width), jnp.float32)
    low = jax.ShapeDtypeStruct((rows, 2 * width), jnp.bfloat16)
    out_shape = [jax.ShapeDtypeStruct((rows, group_size * width), jnp.bfloat16)]
    out_shape += [wide, wide, jax.ShapeDtypeStruct((rows, 4 * width), jnp.bfloat16), wide]
    kernel = functools.partial(
        attention_kernel, group_size=group_size, first_head=half * group_size * width // HEAD_DIMENSION
    )
    return pl.pallas_call(
        kernel,
        out_shape=out_shape,
        grid=(1,),
        in_specs=[smem, smem, id_spec, query_spec, query_spec]
        + [key_spec] * len(payloads)
        + [value_spec] * len(payloads),
        out_specs=[pl.BlockSpec((rows, group_size * width), lambda i: (0, 0))]
        + [pair_spec] * 2
        + [pl.BlockSpec((rows, 4 * width), lambda i: (0, 0)), pair_spec],
        name="attention_group",
    )(windows, odd, query_ids, query, grad, *payloads, *payloads)


def passed_along(value, axis, steps):
    count = lax.axis_size(axis)
    initial, last = (max(0, -steps), min(count, count - steps))
    return lax.ppermute(value, axis, [(source, source + steps) for source in range(initial, last)])


def permuted(value, axis, pairs, scope=None):
    return lax.ppermute(value, axis, [pair for pair in pairs if 0 <= pair[1] < lax.axis_size(axis)])


def on_device(query_proj, key_proj, value_projection, grad_out, doc_ids, advantages, head_window):
    tok_rows = query_proj.shape[0]
    kv_width = key_proj.shape[1]
    count = lax.axis_size("ctx")
    assert WINDOW // tok_rows == 4 and count % 2 == 0
    index = lax.axis_index("ctx")
    odd = (index % 2).astype(jnp.int32).reshape(1)
    doc_count = advantages.shape[0]
    matches = doc_ids[:, None] == jnp.arange(doc_count, dtype=jnp.int32)[None, :]
    token_weight = jnp.sum(jnp.where(matches, advantages[None, :], jnp.float32(0.0)), axis=1)
    grad_local = lax.all_to_all(grad_out, "tsp", split_axis=1, concat_axis=0, tiled=True)
    weighted = (token_weight[:, None] * grad_local.astype(jnp.float32)).astype(jnp.bfloat16)
    query_ids = (doc_ids + 1).astype(jnp.float32)[:, None]

    paired = jnp.concatenate([key_proj, value_projection], axis=1)
    id_rows = jnp.zeros((ID_ROWS, 2 * kv_width), jnp.bfloat16)
    id_rows = id_rows.at[0, :].set(
        jnp.tile((doc_ids + 1).astype(jnp.bfloat16), 2 * kv_width // tok_rows)
    )
    payload = jnp.concatenate([paired, id_rows], axis=0)

    evens = range(0, count, 2)
    odds = range(1, count, 2)
    everyone = range(count)
    swap = [(c, c + 1) for c in evens] + [(c, c - 1) for c in odds]
    got1 = permuted(payload, "ctx", [(c, c + 1) for c in evens])
    got2 = permuted(payload, "ctx", [(c, c + 2) for c in everyone])
    got3 = permuted(got2, "ctx", swap)
    got4 = permuted(got2, "ctx", [(c, c + 2) for c in everyone])
    got5 = permuted(got4, "ctx", [(c, c - 1) for c in odds])

    halves = HALVES
    query_pieces, key_pieces, value_pieces = [], [], []
    for half in range(halves):
        query_part, part4, part2, swap_send, own_part = head_group_grads(
            head_window, odd, query_ids, query_proj, weighted,
            [got1, got2, got3, got4, got5, payload], half, halves,
        )
        tag = str(half)
        pair_width = part4.shape[1]
        swapped = permuted(swap_send, "ctx", swap, "b3_" + tag).astype(jnp.float32)
        from3 = swapped[:, :pair_width]
        second = swapped[:, pair_width:]
        is_odd = odd[0] == 1
        from5 = jnp.where(is_odd, second, jnp.float32(0.0))
        from1 = jnp.where(is_odd, jnp.float32(0.0), second)
        send4 = (part4 + from5).astype(jnp.bfloat16)
        from4 = permuted(send4, "ctx", [(c, c - 2) for c in everyone], "b4_" + tag)
        send2 = (part2 + from4.astype(jnp.float32) + from3).astype(jnp.bfloat16)
        from2 = permuted(send2, "ctx", [(c, c - 2) for c in everyone], "b2_" + tag)
        summed = own_part + from2.astype(jnp.float32) + from1
        width = summed.shape[1] // 2
        query_pieces.append(query_part)
        key_pieces.append(summed[:, :width])
        value_pieces.append(summed[:, width:])
    query_grad = jnp.concatenate(query_pieces, axis=1)
    key_grad = jnp.concatenate(key_pieces, axis=1).astype(jnp.bfloat16)
    value_grad = jnp.concatenate(value_pieces, axis=1).astype(jnp.bfloat16)
    return (query_grad, key_grad, value_grad)


def solution(mesh):
    in_specs = (
        P(("group", "ctx"), "tsp"),
        P(("group", "ctx"), "tsp"),
        P(("group", "ctx"), "tsp"),
        P(("group", "ctx", "tsp"), None),
        P(("group", "ctx")),
        P("group"),
        P("tsp"),
    )
    out_specs = (P(("group", "ctx"), "tsp"), P(("group", "ctx"), "tsp"), P(("group", "ctx"), "tsp"))
    return jax.shard_map(
        on_device, mesh=mesh, in_specs=in_specs, out_specs=out_specs, check_vma=False
    )
```

```python
import functools
import jax
import jax.numpy as jnp
from jax import lax
from jax.experimental import pallas as pl
from jax.experimental.pallas import tpu as pltpu
from jax.sharding import PartitionSpec as P

HEAD_DIMENSION = 128
WINDOW = 1024
ID_ROWS = 16
HALVES = 2
score_scale = 168.0 ** (-0.5)


def _nt(a, b):
    return lax.dot_general(a, b, (((1,), (1,)), ((), ())), preferred_element_type=jnp.float32)


def _tn(a, b):
    return lax.dot_general(a, b, (((0,), (0,)), ((), ())), preferred_element_type=jnp.float32)


def _nn(a, b):
    return lax.dot_general(a, b, (((1,), (0,)), ((), ())), preferred_element_type=jnp.float32)


def attention_kernel(win_ref, odd_ref, qid_ref, q_ref, g_ref, *rest, group_size, first_head):
    key_refs = rest[:6]
    value_refs = rest[6:12]
    dq_ref, p4_ref, p2_ref, p1_ref, p3_ref, b3_ref, own_ref = rest[12:]
    d = HEAD_DIMENSION
    rows = q_ref.shape[0]
    width = key_refs[0].shape[1]
    odd = odd_ref[0] == 1

    def pick(odd_source, even_source):
        def load(index):
            return jnp.where(odd, odd_source[index], even_source[index])
        return load

    def plain(ref):
        def load(index):
            return ref[index]
        return load

    def arrange(refs):
        r1, r2, r3, r4, r5, own = refs
        return [plain(r4), pick(r3, r5), plain(r2), pick(r1, r3), plain(own)]

    key_sources = arrange(key_refs)
    value_sources = arrange(value_refs)
    pieces = len(key_sources)
    key_count = pieces * rows
    row = lax.broadcasted_iota(jnp.int32, (rows, key_count), 0)
    col = lax.broadcasted_iota(jnp.int32, (rows, key_count), 1)
    offset = row + (key_count - rows) - col
    key_ids = jnp.concatenate(
        [src((slice(rows, rows + 1), slice(0, rows))).astype(jnp.float32) for src in key_sources],
        axis=1,
    )
    base_live = (offset >= 0) & (key_ids == qid_ref[...])
    for kv in range(width // d):
        kcols = slice(kv * d, (kv + 1) * d)
        vcols = slice(width + kv * d, width + (kv + 1) * d)
        keys = [src((slice(0, rows), kcols)) for src in key_sources]
        values = [src((slice(0, rows), kcols)) for src in value_sources]
        parts = kv_head(win_ref, q_ref, g_ref, dq_ref, keys, values, offset, base_live, kv, group_size,
                        first_head)
        for target, p in ((p4_ref, 0), (p2_ref, 2), (p1_ref, 3), (p3_ref, 1)):
            target[:, kcols] = parts[p][0].astype(target.dtype)
            target[:, vcols] = parts[p][1].astype(target.dtype)
        b3_ref[:, kcols] = jnp.where(odd, parts[1][0], parts[3][0]).astype(b3_ref.dtype)
        b3_ref[:, vcols] = jnp.where(odd, parts[1][1], parts[3][1]).astype(b3_ref.dtype)
        own_ref[:, kcols] = parts[4][0]
        own_ref[:, vcols] = parts[4][1]


def kv_head(win_ref, q_ref, g_ref, dq_ref, keys, values, offset, base_live, kv, group_size,
            first_head):
    d = HEAD_DIMENSION
    pieces = len(keys)
    piece_rows = q_ref.shape[0]
    key_acc = [jnp.zeros((piece_rows, d), jnp.float32) for _ in range(pieces)]
    value_acc = [jnp.zeros((piece_rows, d), jnp.float32) for _ in range(pieces)]
    for h in range(group_size):
        head = kv * group_size + h
        query = q_ref[:, head * d : (head + 1) * d]
        grad = g_ref[:, head * d : (head + 1) * d]
        scores = jnp.concatenate([_nt(query, key) for key in keys], axis=1) * score_scale
        live = base_live & (offset < win_ref[first_head + head])
        scores = jnp.where(live, scores, jnp.float32(-1e30))
        top = jnp.max(scores, axis=1, keepdims=True)
        prob = jnp.exp(scores - top)
        prob = prob * (1.0 / jnp.sum(prob, axis=1, keepdims=True))
        prob_low = prob.astype(jnp.bfloat16)
        attended = _nn(prob_low[:, :piece_rows], values[0])
        for p in range(1, pieces):
            attended = attended + _nn(prob_low[:, p * piece_rows : (p + 1) * piece_rows], values[p])
        attended = attended.astype(jnp.bfloat16).astype(jnp.float32)
        delta = jnp.sum(grad.astype(jnp.float32) * attended, axis=1, keepdims=True)
        dprob = jnp.concatenate([_nt(grad, value) for value in values], axis=1)
        dscore = (prob * (dprob - delta)).astype(jnp.bfloat16)
        query_acc = _nn(dscore[:, :piece_rows], keys[0])
        for p in range(1, pieces):
            query_acc = query_acc + _nn(dscore[:, p * piece_rows : (p + 1) * piece_rows], keys[p])
        dq_ref[:, head * d : (head + 1) * d] = (query_acc * score_scale).astype(dq_ref.dtype)
        for p in range(pieces):
            cols = slice(p * piece_rows, (p + 1) * piece_rows)
            key_acc[p] = key_acc[p] + _tn(dscore[:, cols], query)
            value_acc[p] = value_acc[p] + _tn(prob_low[:, cols], grad)
    return [(key_acc[p] * score_scale, value_acc[p]) for p in range(pieces)]


def head_group_grads(windows, odd, query_ids, query, grad, payloads, half, width, key_block,
                     group_size):
    rows = query.shape[0]
    payload_rows = payloads[0].shape[0]
    value_block = key_block + payloads[0].shape[1] // (2 * width)
    smem = pl.BlockSpec(memory_space=pltpu.SMEM)
    key_spec = pl.BlockSpec((payload_rows, width), lambda i: (0, key_block))
    value_spec = pl.BlockSpec((payload_rows, width), lambda i: (0, value_block))
    query_spec = pl.BlockSpec((rows, group_size * width), lambda i: (0, half))
    id_spec = pl.BlockSpec((rows, 1), lambda i: (0, 0))
    pair_spec = pl.BlockSpec((rows, 2 * width), lambda i: (0, 0))
    wide = jax.ShapeDtypeStruct((rows, 2 * width), jnp.float32)
    low = jax.ShapeDtypeStruct((rows, 2 * width), jnp.bfloat16)
    out_shape = [jax.ShapeDtypeStruct((rows, group_size * width), jnp.bfloat16)]
    out_shape += [wide, wide, low, low, low, wide]
    kernel = functools.partial(
        attention_kernel, group_size=group_size, first_head=half * group_size * width // HEAD_DIMENSION
    )
    return pl.pallas_call(
        kernel,
        out_shape=out_shape,
        grid=(1,),
        in_specs=[smem, smem, id_spec, query_spec, query_spec]
        + [key_spec] * len(payloads)
        + [value_spec] * len(payloads),
        out_specs=[pl.BlockSpec((rows, group_size * width), lambda i: (0, 0))] + [pair_spec] * 6,
        name="attention_group",
    )(windows, odd, query_ids, query, grad, *payloads, *payloads)


def passed_along(value, axis, steps):
    count = lax.axis_size(axis)
    initial, last = (max(0, -steps), min(count, count - steps))
    return lax.ppermute(value, axis, [(source, source + steps) for source in range(initial, last)])


def permuted(value, axis, pairs, scope=None):
    return lax.ppermute(value, axis, [pair for pair in pairs if 0 <= pair[1] < lax.axis_size(axis)])


def on_device(query_proj, key_proj, value_projection, grad_out, doc_ids, advantages, head_window):
    tok_rows = query_proj.shape[0]
    kv_width = key_proj.shape[1]
    count = lax.axis_size("ctx")
    assert WINDOW // tok_rows == 4 and count % 2 == 0
    index = lax.axis_index("ctx")
    odd = (index % 2).astype(jnp.int32).reshape(1)
    doc_count = advantages.shape[0]
    matches = doc_ids[:, None] == jnp.arange(doc_count, dtype=jnp.int32)[None, :]
    token_weight = jnp.sum(jnp.where(matches, advantages[None, :], jnp.float32(0.0)), axis=1)
    grad_local = lax.all_to_all(grad_out, "tsp", split_axis=1, concat_axis=0, tiled=True)
    weighted = (token_weight[:, None] * grad_local.astype(jnp.float32)).astype(jnp.bfloat16)
    query_ids = (doc_ids + 1).astype(jnp.float32)[:, None]

    kv_heads = kv_width // HEAD_DIMENSION
    group_size = query_proj.shape[1] // kv_width
    halves = HALVES
    width = kv_width // halves
    evens = range(0, count, 2)
    odds = range(1, count, 2)
    everyone = range(count)
    swap = [(c, c + 1) for c in evens] + [(c, c - 1) for c in odds]
    arrived = []
    for half in range(halves):
        cols = slice(half * width, (half + 1) * width)
        paired = jnp.concatenate([key_proj[:, cols], value_projection[:, cols]], axis=1)
        id_rows = jnp.zeros((ID_ROWS, 2 * width), jnp.bfloat16)
        id_rows = id_rows.at[0, :].set(
            jnp.tile((doc_ids + 1).astype(jnp.bfloat16), 2 * width // tok_rows)
        )
        payload = jnp.concatenate([paired, id_rows], axis=0)
        got1 = permuted(payload, "ctx", [(c, c + 1) for c in evens])
        got2 = permuted(payload, "ctx", [(c, c + 2) for c in everyone])
        got3 = permuted(got2, "ctx", swap)
        got4 = permuted(got2, "ctx", [(c, c + 2) for c in everyone])
        got5 = permuted(got4, "ctx", [(c, c - 1) for c in odds])
        arrived.append([got1, got2, got3, got4, got5, payload])

    query_pieces, key_pieces, value_pieces = [], [], []
    for half in range(halves):
        query_part, part4, part2, part1, part3, back3, own_part = head_group_grads(
            head_window, odd, query_ids, query_proj, weighted, arrived[half], half, width, 0,
            group_size,
        )
        from5 = permuted(part3, "ctx", [(c, c + 1) for c in evens])
        from3 = permuted(back3, "ctx", swap)
        from1 = permuted(part1, "ctx", [(c, c - 1) for c in odds])
        send4 = (part4 + from5.astype(jnp.float32)).astype(jnp.bfloat16)
        from4 = permuted(send4, "ctx", [(c, c - 2) for c in everyone])
        send2 = (part2 + from4.astype(jnp.float32) + from3.astype(jnp.float32)).astype(jnp.bfloat16)
        from2 = permuted(send2, "ctx", [(c, c - 2) for c in everyone])
        summed = own_part + from2.astype(jnp.float32) + from1.astype(jnp.float32)
        query_pieces.append(query_part)
        key_pieces.append(summed[:, :width])
        value_pieces.append(summed[:, width:])
    query_grad = jnp.concatenate(query_pieces, axis=1)
    key_grad = jnp.concatenate(key_pieces, axis=1).astype(jnp.bfloat16)
    value_grad = jnp.concatenate(value_pieces, axis=1).astype(jnp.bfloat16)
    return (query_grad, key_grad, value_grad)


def solution(mesh):
    in_specs = (
        P(("group", "ctx"), "tsp"),
        P(("group", "ctx"), "tsp"),
        P(("group", "ctx"), "tsp"),
        P(("group", "ctx", "tsp"), None),
        P(("group", "ctx")),
        P("group"),
        P("tsp"),
    )
    out_specs = (P(("group", "ctx"), "tsp"), P(("group", "ctx"), "tsp"), P(("group", "ctx"), "tsp"))
    return jax.shard_map(
        on_device, mesh=mesh, in_specs=in_specs, out_specs=out_specs, check_vma=False
    )
```

```python
import functools
import jax
import jax.numpy as jnp
from jax import lax
from jax.experimental import pallas as pl
from jax.experimental.pallas import tpu as pltpu
from jax.sharding import PartitionSpec as P

HEAD_DIMENSION = 128
WINDOW = 1024
ID_ROWS = 16
HALVES = 2
score_scale = 168.0 ** (-0.5)


def _nt(a, b):
    return lax.dot_general(a, b, (((1,), (1,)), ((), ())), preferred_element_type=jnp.float32)


def _tn(a, b):
    return lax.dot_general(a, b, (((0,), (0,)), ((), ())), preferred_element_type=jnp.float32)


def _nn(a, b):
    return lax.dot_general(a, b, (((1,), (0,)), ((), ())), preferred_element_type=jnp.float32)


def attention_kernel(win_ref, odd_ref, qid_ref, q_ref, g_ref, *rest, group_size, first_head):
    key_refs = rest[:6]
    value_refs = rest[6:12]
    dq_ref, p4_ref, p2_ref, p1_ref, p3_ref, b3_ref, own_ref = rest[12:]
    d = HEAD_DIMENSION
    rows = q_ref.shape[0]
    width = key_refs[0].shape[1]
    odd = odd_ref[0] == 1

    def pick(odd_source, even_source):
        def load(index):
            return jnp.where(odd, odd_source[index], even_source[index])
        return load

    def plain(ref):
        def load(index):
            return ref[index]
        return load

    def arrange(refs):
        r1, r2, r3, r4, r5, own = refs
        return [plain(r4), pick(r3, r5), plain(r2), pick(r1, r3), plain(own)]

    key_sources = arrange(key_refs)
    value_sources = arrange(value_refs)
    pieces = len(key_sources)
    key_count = pieces * rows
    row = lax.broadcasted_iota(jnp.int32, (rows, key_count), 0)
    col = lax.broadcasted_iota(jnp.int32, (rows, key_count), 1)
    offset = row + (key_count - rows) - col
    key_ids = jnp.concatenate(
        [src((slice(rows, rows + 1), slice(0, rows))).astype(jnp.float32) for src in key_sources],
        axis=1,
    )
    base_live = (offset >= 0) & (key_ids == qid_ref[...])
    for kv in range(width // d):
        kcols = slice(kv * d, (kv + 1) * d)
        vcols = slice(width + kv * d, width + (kv + 1) * d)
        keys = [src((slice(0, rows), kcols)) for src in key_sources]
        values = [src((slice(0, rows), kcols)) for src in value_sources]
        parts = kv_head(win_ref, q_ref, g_ref, dq_ref, keys, values, offset, base_live, kv, group_size,
                        first_head)
        for target, p in ((p4_ref, 0), (p2_ref, 2), (p1_ref, 3), (p3_ref, 1)):
            target[:, kcols] = parts[p][0].astype(target.dtype)
            target[:, vcols] = parts[p][1].astype(target.dtype)
        b3_ref[:, kcols] = jnp.where(odd, parts[1][0], parts[3][0]).astype(b3_ref.dtype)
        b3_ref[:, vcols] = jnp.where(odd, parts[1][1], parts[3][1]).astype(b3_ref.dtype)
        own_ref[:, kcols] = parts[4][0]
        own_ref[:, vcols] = parts[4][1]


def kv_head(win_ref, q_ref, g_ref, dq_ref, keys, values, offset, base_live, kv, group_size,
            first_head):
    d = HEAD_DIMENSION
    pieces = len(keys)
    piece_rows = q_ref.shape[0]
    key_acc = [jnp.zeros((piece_rows, d), jnp.float32) for _ in range(pieces)]
    value_acc = [jnp.zeros((piece_rows, d), jnp.float32) for _ in range(pieces)]
    for h in range(group_size):
        head = kv * group_size + h
        query = q_ref[:, head * d : (head + 1) * d]
        grad = g_ref[:, head * d : (head + 1) * d]
        scores = jnp.concatenate([_nt(query, key) for key in keys], axis=1) * score_scale
        live = base_live & (offset < win_ref[first_head + head])
        scores = jnp.where(live, scores, jnp.float32(-1e30))
        top = jnp.max(scores, axis=1, keepdims=True)
        prob = jnp.exp(scores - top)
        prob = prob * (1.0 / jnp.sum(prob, axis=1, keepdims=True))
        prob_low = prob.astype(jnp.bfloat16)
        attended = _nn(prob_low[:, :piece_rows], values[0])
        for p in range(1, pieces):
            attended = attended + _nn(prob_low[:, p * piece_rows : (p + 1) * piece_rows], values[p])
        attended = attended.astype(jnp.bfloat16).astype(jnp.float32)
        delta = jnp.sum(grad.astype(jnp.float32) * attended, axis=1, keepdims=True)
        dprob = jnp.concatenate([_nt(grad, value) for value in values], axis=1)
        dscore = (prob * (dprob - delta)).astype(jnp.bfloat16)
        query_acc = _nn(dscore[:, :piece_rows], keys[0])
        for p in range(1, pieces):
            query_acc = query_acc + _nn(dscore[:, p * piece_rows : (p + 1) * piece_rows], keys[p])
        dq_ref[:, head * d : (head + 1) * d] = (query_acc * score_scale).astype(dq_ref.dtype)
        for p in range(pieces):
            cols = slice(p * piece_rows, (p + 1) * piece_rows)
            key_acc[p] = key_acc[p] + _tn(dscore[:, cols], query)
            value_acc[p] = value_acc[p] + _tn(prob_low[:, cols], grad)
    return [(key_acc[p] * score_scale, value_acc[p]) for p in range(pieces)]


def head_group_grads(windows, odd, query_ids, query, grad, payloads, half, width, key_block,
                     group_size):
    rows = query.shape[0]
    payload_rows = payloads[0].shape[0]
    value_block = key_block + payloads[0].shape[1] // (2 * width)
    smem = pl.BlockSpec(memory_space=pltpu.SMEM)
    key_spec = pl.BlockSpec((payload_rows, width), lambda i: (0, key_block))
    value_spec = pl.BlockSpec((payload_rows, width), lambda i: (0, value_block))
    query_spec = pl.BlockSpec((rows, group_size * width), lambda i: (0, half))
    id_spec = pl.BlockSpec((rows, 1), lambda i: (0, 0))
    pair_spec = pl.BlockSpec((rows, 2 * width), lambda i: (0, 0))
    wide = jax.ShapeDtypeStruct((rows, 2 * width), jnp.float32)
    low = jax.ShapeDtypeStruct((rows, 2 * width), jnp.bfloat16)
    out_shape = [jax.ShapeDtypeStruct((rows, group_size * width), jnp.bfloat16)]
    out_shape += [wide, wide, low, low, low, wide]
    kernel = functools.partial(
        attention_kernel, group_size=group_size, first_head=half * group_size * width // HEAD_DIMENSION
    )
    return pl.pallas_call(
        kernel,
        out_shape=out_shape,
        grid=(1,),
        in_specs=[smem, smem, id_spec, query_spec, query_spec]
        + [key_spec] * len(payloads)
        + [value_spec] * len(payloads),
        out_specs=[pl.BlockSpec((rows, group_size * width), lambda i: (0, 0))] + [pair_spec] * 6,
        name="attention_group",
    )(windows, odd, query_ids, query, grad, *payloads, *payloads)


def passed_along(value, axis, steps):
    count = lax.axis_size(axis)
    initial, last = (max(0, -steps), min(count, count - steps))
    return lax.ppermute(value, axis, [(source, source + steps) for source in range(initial, last)])


def permuted(value, axis, pairs, scope=None):
    return lax.ppermute(value, axis, [pair for pair in pairs if 0 <= pair[1] < lax.axis_size(axis)])


def on_device(query_proj, key_proj, value_projection, grad_out, doc_ids, advantages, head_window):
    tok_rows = query_proj.shape[0]
    kv_width = key_proj.shape[1]
    count = lax.axis_size("ctx")
    assert WINDOW // tok_rows == 4 and count % 2 == 0
    index = lax.axis_index("ctx")
    odd = (index % 2).astype(jnp.int32).reshape(1)
    doc_count = advantages.shape[0]
    matches = doc_ids[:, None] == jnp.arange(doc_count, dtype=jnp.int32)[None, :]
    token_weight = jnp.sum(jnp.where(matches, advantages[None, :], jnp.float32(0.0)), axis=1)
    grad_local = lax.all_to_all(grad_out, "tsp", split_axis=1, concat_axis=0, tiled=True)
    weighted = (token_weight[:, None] * grad_local.astype(jnp.float32)).astype(jnp.bfloat16)
    query_ids = (doc_ids + 1).astype(jnp.float32)[:, None]

    kv_heads = kv_width // HEAD_DIMENSION
    group_size = query_proj.shape[1] // kv_width
    halves = HALVES
    width = kv_width // halves
    evens = range(0, count, 2)
    odds = range(1, count, 2)
    everyone = range(count)
    swap = [(c, c + 1) for c in evens] + [(c, c - 1) for c in odds]
    arrived = []
    for half in range(halves):
        cols = slice(half * width, (half + 1) * width)
        paired = jnp.concatenate([key_proj[:, cols], value_projection[:, cols]], axis=1)
        id_rows = jnp.zeros((ID_ROWS, 2 * width), jnp.bfloat16)
        id_rows = id_rows.at[0, :].set(
            jnp.tile((doc_ids + 1).astype(jnp.bfloat16), 2 * width // tok_rows)
        )
        payload = jnp.concatenate([paired, id_rows], axis=0)
        got1 = permuted(payload, "ctx", [(c, c + 1) for c in evens])
        got2 = permuted(payload, "ctx", [(c, c + 2) for c in everyone])
        got3 = permuted(got2, "ctx", swap)
        got4 = permuted(got2, "ctx", [(c, c + 2) for c in everyone])
        got5 = permuted(got2, "ctx", [(c, c + 1) for c in odds])
        arrived.append([got1, got2, got3, got4, got5, payload])

    query_pieces, key_pieces, value_pieces = [], [], []
    for half in range(halves):
        query_part, part4, part2, part1, part3, back3, own_part = head_group_grads(
            head_window, odd, query_ids, query_proj, weighted, arrived[half], half, width, 0,
            group_size,
        )
        from5 = permuted(part3, "ctx", [(c, c + 1) for c in evens])
        from3 = permuted(back3, "ctx", swap)
        from1 = permuted(part1, "ctx", [(c, c - 1) for c in odds])
        send4 = (part4 + from5.astype(jnp.float32)).astype(jnp.bfloat16)
        from4 = permuted(send4, "ctx", [(c, c - 2) for c in everyone])
        send2 = (part2 + from4.astype(jnp.float32) + from3.astype(jnp.float32)).astype(jnp.bfloat16)
        from2 = permuted(send2, "ctx", [(c, c - 2) for c in everyone])
        summed = own_part + from2.astype(jnp.float32) + from1.astype(jnp.float32)
        query_pieces.append(query_part)
        key_pieces.append(summed[:, :width])
        value_pieces.append(summed[:, width:])
    query_grad = jnp.concatenate(query_pieces, axis=1)
    key_grad = jnp.concatenate(key_pieces, axis=1).astype(jnp.bfloat16)
    value_grad = jnp.concatenate(value_pieces, axis=1).astype(jnp.bfloat16)
    return (query_grad, key_grad, value_grad)


def solution(mesh):
    in_specs = (
        P(("group", "ctx"), "tsp"),
        P(("group", "ctx"), "tsp"),
        P(("group", "ctx"), "tsp"),
        P(("group", "ctx", "tsp"), None),
        P(("group", "ctx")),
        P("group"),
        P("tsp"),
    )
    out_specs = (P(("group", "ctx"), "tsp"), P(("group", "ctx"), "tsp"), P(("group", "ctx"), "tsp"))
    return jax.shard_map(
        on_device, mesh=mesh, in_specs=in_specs, out_specs=out_specs, check_vma=False
    )
```

```python
import functools
import jax
import jax.numpy as jnp
from jax import lax
from jax.experimental import pallas as pl
from jax.experimental.pallas import tpu as pltpu
from jax.sharding import PartitionSpec as P

HEAD_DIMENSION = 128
WINDOW = 1024
ID_ROWS = 16
HALVES = 2
score_scale = 168.0 ** (-0.5)


def _nt(a, b):
    return lax.dot_general(a, b, (((1,), (1,)), ((), ())), preferred_element_type=jnp.float32)


def _tn(a, b):
    return lax.dot_general(a, b, (((0,), (0,)), ((), ())), preferred_element_type=jnp.float32)


def _nn(a, b):
    return lax.dot_general(a, b, (((1,), (0,)), ((), ())), preferred_element_type=jnp.float32)


def attention_kernel(win_ref, odd_ref, qid_ref, q_ref, g_ref, *rest, group_size, first_head):
    key_refs = rest[:6]
    value_refs = rest[6:12]
    dq_ref, p4_ref, p2_ref, m1_ref, b3_ref, own_ref = rest[12:]
    d = HEAD_DIMENSION
    rows = q_ref.shape[0]
    width = key_refs[0].shape[1]
    odd = odd_ref[0] == 1

    def pick(odd_source, even_source):
        def load(index):
            return jnp.where(odd, odd_source[index], even_source[index])
        return load

    def plain(ref):
        def load(index):
            return ref[index]
        return load

    def arrange(refs):
        r1, r2, r3, r4, r5, own = refs
        return [plain(r4), pick(r3, r5), plain(r2), pick(r1, r3), plain(own)]

    key_sources = arrange(key_refs)
    value_sources = arrange(value_refs)
    pieces = len(key_sources)
    key_count = pieces * rows
    row = lax.broadcasted_iota(jnp.int32, (rows, key_count), 0)
    col = lax.broadcasted_iota(jnp.int32, (rows, key_count), 1)
    offset = row + (key_count - rows) - col
    key_ids = jnp.concatenate(
        [src((slice(rows, rows + 1), slice(0, rows))).astype(jnp.float32) for src in key_sources],
        axis=1,
    )
    base_live = (offset >= 0) & (key_ids == qid_ref[...])
    for kv in range(width // d):
        kcols = slice(kv * d, (kv + 1) * d)
        vcols = slice(width + kv * d, width + (kv + 1) * d)
        keys = [src((slice(0, rows), kcols)) for src in key_sources]
        values = [src((slice(0, rows), kcols)) for src in value_sources]
        parts = kv_head(win_ref, q_ref, g_ref, dq_ref, keys, values, offset, base_live, kv, group_size,
                        first_head)
        for target, p in ((p4_ref, 0), (p2_ref, 2)):
            target[:, kcols] = parts[p][0].astype(target.dtype)
            target[:, vcols] = parts[p][1].astype(target.dtype)
        m1_ref[:, kcols] = jnp.where(odd, parts[3][0], parts[1][0]).astype(m1_ref.dtype)
        m1_ref[:, vcols] = jnp.where(odd, parts[3][1], parts[1][1]).astype(m1_ref.dtype)
        b3_ref[:, kcols] = jnp.where(odd, parts[1][0], parts[3][0]).astype(b3_ref.dtype)
        b3_ref[:, vcols] = jnp.where(odd, parts[1][1], parts[3][1]).astype(b3_ref.dtype)
        own_ref[:, kcols] = parts[4][0]
        own_ref[:, vcols] = parts[4][1]


def kv_head(win_ref, q_ref, g_ref, dq_ref, keys, values, offset, base_live, kv, group_size,
            first_head):
    d = HEAD_DIMENSION
    pieces = len(keys)
    piece_rows = q_ref.shape[0]
    key_acc = [jnp.zeros((piece_rows, d), jnp.float32) for _ in range(pieces)]
    value_acc = [jnp.zeros((piece_rows, d), jnp.float32) for _ in range(pieces)]
    for h in range(group_size):
        head = kv * group_size + h
        query = q_ref[:, head * d : (head + 1) * d]
        grad = g_ref[:, head * d : (head + 1) * d]
        scores = jnp.concatenate([_nt(query, key) for key in keys], axis=1) * score_scale
        live = base_live & (offset < win_ref[first_head + head])
        scores = jnp.where(live, scores, jnp.float32(-1e30))
        top = jnp.max(scores, axis=1, keepdims=True)
        prob = jnp.exp(scores - top)
        prob = prob * (1.0 / jnp.sum(prob, axis=1, keepdims=True))
        prob_low = prob.astype(jnp.bfloat16)
        attended = _nn(prob_low[:, :piece_rows], values[0])
        for p in range(1, pieces):
            attended = attended + _nn(prob_low[:, p * piece_rows : (p + 1) * piece_rows], values[p])
        attended = attended.astype(jnp.bfloat16).astype(jnp.float32)
        delta = jnp.sum(grad.astype(jnp.float32) * attended, axis=1, keepdims=True)
        dprob = jnp.concatenate([_nt(grad, value) for value in values], axis=1)
        dscore = (prob * (dprob - delta)).astype(jnp.bfloat16)
        query_acc = _nn(dscore[:, :piece_rows], keys[0])
        for p in range(1, pieces):
            query_acc = query_acc + _nn(dscore[:, p * piece_rows : (p + 1) * piece_rows], keys[p])
        dq_ref[:, head * d : (head + 1) * d] = (query_acc * score_scale).astype(dq_ref.dtype)
        for p in range(pieces):
            cols = slice(p * piece_rows, (p + 1) * piece_rows)
            key_acc[p] = key_acc[p] + _tn(dscore[:, cols], query)
            value_acc[p] = value_acc[p] + _tn(prob_low[:, cols], grad)
    return [(key_acc[p] * score_scale, value_acc[p]) for p in range(pieces)]


def head_group_grads(windows, odd, query_ids, query, grad, payloads, half, width, key_block,
                     group_size):
    rows = query.shape[0]
    payload_rows = payloads[0].shape[0]
    value_block = key_block + payloads[0].shape[1] // (2 * width)
    smem = pl.BlockSpec(memory_space=pltpu.SMEM)
    key_spec = pl.BlockSpec((payload_rows, width), lambda i: (0, key_block))
    value_spec = pl.BlockSpec((payload_rows, width), lambda i: (0, value_block))
    query_spec = pl.BlockSpec((rows, group_size * width), lambda i: (0, half))
    id_spec = pl.BlockSpec((rows, 1), lambda i: (0, 0))
    pair_spec = pl.BlockSpec((rows, 2 * width), lambda i: (0, 0))
    wide = jax.ShapeDtypeStruct((rows, 2 * width), jnp.float32)
    low = jax.ShapeDtypeStruct((rows, 2 * width), jnp.bfloat16)
    out_shape = [jax.ShapeDtypeStruct((rows, group_size * width), jnp.bfloat16)]
    out_shape += [low, wide, low, low, wide]
    kernel = functools.partial(
        attention_kernel, group_size=group_size, first_head=half * group_size * width // HEAD_DIMENSION
    )
    return pl.pallas_call(
        kernel,
        out_shape=out_shape,
        grid=(1,),
        in_specs=[smem, smem, id_spec, query_spec, query_spec]
        + [key_spec] * len(payloads)
        + [value_spec] * len(payloads),
        out_specs=[pl.BlockSpec((rows, group_size * width), lambda i: (0, 0))] + [pair_spec] * 5,
        name="attention_group",
    )(windows, odd, query_ids, query, grad, *payloads, *payloads)


def passed_along(value, axis, steps):
    count = lax.axis_size(axis)
    initial, last = (max(0, -steps), min(count, count - steps))
    return lax.ppermute(value, axis, [(source, source + steps) for source in range(initial, last)])


def permuted(value, axis, pairs, scope=None):
    return lax.ppermute(value, axis, [pair for pair in pairs if 0 <= pair[1] < lax.axis_size(axis)])


def on_device(query_proj, key_proj, value_projection, grad_out, doc_ids, advantages, head_window):
    tok_rows = query_proj.shape[0]
    kv_width = key_proj.shape[1]
    count = lax.axis_size("ctx")
    assert WINDOW // tok_rows == 4 and count % 2 == 0
    index = lax.axis_index("ctx")
    odd = (index % 2).astype(jnp.int32).reshape(1)
    doc_count = advantages.shape[0]
    matches = doc_ids[:, None] == jnp.arange(doc_count, dtype=jnp.int32)[None, :]
    token_weight = jnp.sum(jnp.where(matches, advantages[None, :], jnp.float32(0.0)), axis=1)
    grad_local = lax.all_to_all(grad_out, "tsp", split_axis=1, concat_axis=0, tiled=True)
    weighted = (token_weight[:, None] * grad_local.astype(jnp.float32)).astype(jnp.bfloat16)
    query_ids = (doc_ids + 1).astype(jnp.float32)[:, None]

    kv_heads = kv_width // HEAD_DIMENSION
    group_size = query_proj.shape[1] // kv_width
    halves = HALVES
    width = kv_width // halves
    evens = range(0, count, 2)
    odds = range(1, count, 2)
    everyone = range(count)
    swap = [(c, c + 1) for c in evens] + [(c, c - 1) for c in odds]
    arrived = []
    for half in range(halves):
        cols = slice(half * width, (half + 1) * width)
        paired = jnp.concatenate([key_proj[:, cols], value_projection[:, cols]], axis=1)
        id_rows = jnp.zeros((ID_ROWS, 2 * width), jnp.bfloat16)
        id_rows = id_rows.at[0, :].set(
            jnp.tile((doc_ids + 1).astype(jnp.bfloat16), 2 * width // tok_rows)
        )
        payload = jnp.concatenate([paired, id_rows], axis=0)
        got1 = permuted(payload, "ctx", [(c, c + 1) for c in evens])
        got2 = permuted(payload, "ctx", [(c, c + 2) for c in everyone])
        got3 = permuted(got2, "ctx", swap)
        got4 = permuted(got2, "ctx", [(c, c + 2) for c in everyone])
        got5 = permuted(got2, "ctx", [(c, c + 1) for c in odds])
        arrived.append([got1, got2, got3, got4, got5, payload])

    query_pieces, key_pieces, value_pieces = [], [], []
    for half in range(halves):
        query_part, send4, part2, back1, back3, own_part = head_group_grads(
            head_window, odd, query_ids, query_proj, weighted, arrived[half], half, width, 0,
            group_size,
        )
        is_odd = odd[0] == 1
        from1 = permuted(back1, "ctx", [(c, c - 1) for c in everyone]).astype(jnp.float32)
        from3 = permuted(back3, "ctx", swap)
        from4 = permuted(send4, "ctx", [(c, c - 2) for c in everyone])
        send2 = part2 + from4.astype(jnp.float32) + from3.astype(jnp.float32)
        send2 = (send2 + jnp.where(is_odd, from1, jnp.float32(0.0))).astype(jnp.bfloat16)
        from2 = permuted(send2, "ctx", [(c, c - 2) for c in everyone])
        summed = own_part + from2.astype(jnp.float32) + jnp.where(is_odd, jnp.float32(0.0), from1)
        query_pieces.append(query_part)
        key_pieces.append(summed[:, :width])
        value_pieces.append(summed[:, width:])
    query_grad = jnp.concatenate(query_pieces, axis=1)
    key_grad = jnp.concatenate(key_pieces, axis=1).astype(jnp.bfloat16)
    value_grad = jnp.concatenate(value_pieces, axis=1).astype(jnp.bfloat16)
    return (query_grad, key_grad, value_grad)


def solution(mesh):
    in_specs = (
        P(("group", "ctx"), "tsp"),
        P(("group", "ctx"), "tsp"),
        P(("group", "ctx"), "tsp"),
        P(("group", "ctx", "tsp"), None),
        P(("group", "ctx")),
        P("group"),
        P("tsp"),
    )
    out_specs = (P(("group", "ctx"), "tsp"), P(("group", "ctx"), "tsp"), P(("group", "ctx"), "tsp"))
    return jax.shard_map(
        on_device, mesh=mesh, in_specs=in_specs, out_specs=out_specs, check_vma=False
    )
```

```python
import functools
import jax
import jax.numpy as jnp
from jax import lax
from jax.experimental import pallas as pl
from jax.experimental.pallas import tpu as pltpu
from jax.sharding import PartitionSpec as P

HEAD_DIMENSION = 128
WINDOW = 1024
ID_ROWS = 16
HALVES = 2
score_scale = 168.0 ** (-0.5)


def _nt(a, b):
    return lax.dot_general(a, b, (((1,), (1,)), ((), ())), preferred_element_type=jnp.float32)


def _tn(a, b):
    return lax.dot_general(a, b, (((0,), (0,)), ((), ())), preferred_element_type=jnp.float32)


def _nn(a, b):
    return lax.dot_general(a, b, (((1,), (0,)), ((), ())), preferred_element_type=jnp.float32)


def attention_kernel(win_ref, odd_ref, qid_ref, q_ref, g_ref, *rest, group_size, first_head):
    key_refs = rest[:6]
    value_refs = rest[6:12]
    dq_ref, p4_ref, p2_ref, m1_ref, b3_ref, own_ref = rest[12:]
    d = HEAD_DIMENSION
    rows = q_ref.shape[0]
    width = key_refs[0].shape[1]
    odd = odd_ref[0] == 1

    def pick(odd_source, even_source):
        def load(index):
            return jnp.where(odd, odd_source[index], even_source[index])
        return load

    def plain(ref):
        def load(index):
            return ref[index]
        return load

    def arrange(refs):
        r1, r2, r3, r4, r5, own = refs
        return [plain(r4), pick(r3, r5), plain(r2), pick(r1, r3), plain(own)]

    key_sources = arrange(key_refs)
    value_sources = arrange(value_refs)
    pieces = len(key_sources)
    key_count = pieces * rows
    row = lax.broadcasted_iota(jnp.int32, (rows, key_count), 0)
    col = lax.broadcasted_iota(jnp.int32, (rows, key_count), 1)
    offset = row + (key_count - rows) - col
    key_ids = jnp.concatenate(
        [src((slice(rows, rows + 1), slice(0, rows))).astype(jnp.float32) for src in key_sources],
        axis=1,
    )
    base_live = (offset >= 0) & (key_ids == qid_ref[...])
    for kv in range(width // d):
        kcols = slice(kv * d, (kv + 1) * d)
        vcols = slice(width + kv * d, width + (kv + 1) * d)
        keys = [src((slice(0, rows), kcols)) for src in key_sources]
        values = [src((slice(0, rows), kcols)) for src in value_sources]
        parts = kv_head(win_ref, q_ref, g_ref, dq_ref, keys, values, offset, base_live, kv, group_size,
                        first_head)
        for target, p in ((p4_ref, 0), (p2_ref, 2)):
            target[:, kcols] = parts[p][0].astype(target.dtype)
            target[:, vcols] = parts[p][1].astype(target.dtype)
        m1_ref[:, kcols] = jnp.where(odd, parts[3][0], parts[1][0]).astype(m1_ref.dtype)
        m1_ref[:, vcols] = jnp.where(odd, parts[3][1], parts[1][1]).astype(m1_ref.dtype)
        b3_ref[:, kcols] = jnp.where(odd, parts[1][0], parts[3][0]).astype(b3_ref.dtype)
        b3_ref[:, vcols] = jnp.where(odd, parts[1][1], parts[3][1]).astype(b3_ref.dtype)
        own_ref[:, kcols] = parts[4][0]
        own_ref[:, vcols] = parts[4][1]


def kv_head(win_ref, q_ref, g_ref, dq_ref, keys, values, offset, base_live, kv, group_size,
            first_head):
    d = HEAD_DIMENSION
    pieces = len(keys)
    piece_rows = q_ref.shape[0]
    key_acc = [jnp.zeros((piece_rows, d), jnp.float32) for _ in range(pieces)]
    value_acc = [jnp.zeros((piece_rows, d), jnp.float32) for _ in range(pieces)]
    for h in range(group_size):
        head = kv * group_size + h
        query = q_ref[:, head * d : (head + 1) * d]
        grad = g_ref[:, head * d : (head + 1) * d]
        scores = jnp.concatenate([_nt(query, key) for key in keys], axis=1) * score_scale
        live = base_live & (offset < win_ref[first_head + head])
        scores = jnp.where(live, scores, jnp.float32(-1e30))
        top = jnp.max(scores, axis=1, keepdims=True)
        prob = jnp.exp(scores - top)
        prob = prob * (1.0 / jnp.sum(prob, axis=1, keepdims=True))
        prob_low = prob.astype(jnp.bfloat16)
        attended = _nn(prob_low[:, :piece_rows], values[0])
        for p in range(1, pieces):
            attended = attended + _nn(prob_low[:, p * piece_rows : (p + 1) * piece_rows], values[p])
        attended = attended.astype(jnp.bfloat16).astype(jnp.float32)
        delta = jnp.sum(grad.astype(jnp.float32) * attended, axis=1, keepdims=True)
        dprob = jnp.concatenate([_nt(grad, value) for value in values], axis=1)
        dscore = (prob * (dprob - delta)).astype(jnp.bfloat16)
        query_acc = _nn(dscore[:, :piece_rows], keys[0])
        for p in range(1, pieces):
            query_acc = query_acc + _nn(dscore[:, p * piece_rows : (p + 1) * piece_rows], keys[p])
        dq_ref[:, head * d : (head + 1) * d] = (query_acc * score_scale).astype(dq_ref.dtype)
        for p in range(pieces):
            cols = slice(p * piece_rows, (p + 1) * piece_rows)
            key_acc[p] = key_acc[p] + _tn(dscore[:, cols], query)
            value_acc[p] = value_acc[p] + _tn(prob_low[:, cols], grad)
    return [(key_acc[p] * score_scale, value_acc[p]) for p in range(pieces)]


def head_group_grads(windows, odd, query_ids, query, grad, payloads, half, width, key_block,
                     group_size):
    rows = query.shape[0]
    payload_rows = payloads[0].shape[0]
    value_block = key_block + payloads[0].shape[1] // (2 * width)
    smem = pl.BlockSpec(memory_space=pltpu.SMEM)
    key_spec = pl.BlockSpec((payload_rows, width), lambda i: (0, key_block))
    value_spec = pl.BlockSpec((payload_rows, width), lambda i: (0, value_block))
    query_spec = pl.BlockSpec((rows, group_size * width), lambda i: (0, half))
    id_spec = pl.BlockSpec((rows, 1), lambda i: (0, 0))
    pair_spec = pl.BlockSpec((rows, 2 * width), lambda i: (0, 0))
    wide = jax.ShapeDtypeStruct((rows, 2 * width), jnp.float32)
    low = jax.ShapeDtypeStruct((rows, 2 * width), jnp.bfloat16)
    out_shape = [jax.ShapeDtypeStruct((rows, group_size * width), jnp.bfloat16)]
    out_shape += [low, wide, low, low, wide]
    kernel = functools.partial(
        attention_kernel, group_size=group_size, first_head=half * group_size * width // HEAD_DIMENSION
    )
    return pl.pallas_call(
        kernel,
        out_shape=out_shape,
        grid=(1,),
        in_specs=[smem, smem, id_spec, query_spec, query_spec]
        + [key_spec] * len(payloads)
        + [value_spec] * len(payloads),
        out_specs=[pl.BlockSpec((rows, group_size * width), lambda i: (0, 0))] + [pair_spec] * 5,
        name="attention_group",
    )(windows, odd, query_ids, query, grad, *payloads, *payloads)


def passed_along(value, axis, steps):
    count = lax.axis_size(axis)
    initial, last = (max(0, -steps), min(count, count - steps))
    return lax.ppermute(value, axis, [(source, source + steps) for source in range(initial, last)])


def permuted(value, axis, pairs, scope=None):
    return lax.ppermute(value, axis, [pair for pair in pairs if 0 <= pair[1] < lax.axis_size(axis)])


def on_device(query_proj, key_proj, value_projection, grad_out, doc_ids, advantages, head_window):
    tok_rows = query_proj.shape[0]
    kv_width = key_proj.shape[1]
    count = lax.axis_size("ctx")
    assert WINDOW // tok_rows == 4 and count % 2 == 0
    index = lax.axis_index("ctx")
    odd = (index % 2).astype(jnp.int32).reshape(1)
    doc_count = advantages.shape[0]
    matches = doc_ids[:, None] == jnp.arange(doc_count, dtype=jnp.int32)[None, :]
    token_weight = jnp.sum(jnp.where(matches, advantages[None, :], jnp.float32(0.0)), axis=1)
    grad_local = lax.all_to_all(grad_out, "tsp", split_axis=1, concat_axis=0, tiled=True)
    weighted = (token_weight[:, None] * grad_local.astype(jnp.float32)).astype(jnp.bfloat16)
    query_ids = (doc_ids + 1).astype(jnp.float32)[:, None]

    kv_heads = kv_width // HEAD_DIMENSION
    group_size = query_proj.shape[1] // kv_width
    halves = HALVES
    width = kv_width // halves
    evens = range(0, count, 2)
    odds = range(1, count, 2)
    everyone = range(count)
    swap = [(c, c + 1) for c in evens] + [(c, c - 1) for c in odds]
    paired = jnp.concatenate([key_proj, value_projection], axis=1)
    id_rows = jnp.zeros((ID_ROWS, 2 * kv_width), jnp.bfloat16)
    id_rows = id_rows.at[0, :].set(
        jnp.tile((doc_ids + 1).astype(jnp.bfloat16), 2 * kv_width // tok_rows)
    )
    payload = jnp.concatenate([paired, id_rows], axis=0)
    got1 = permuted(payload, "ctx", [(c, c + 1) for c in evens])
    got2 = permuted(payload, "ctx", [(c, c + 2) for c in everyone])
    got3 = permuted(got2, "ctx", swap)
    got4 = permuted(got2, "ctx", [(c, c + 2) for c in everyone])
    got5 = permuted(got2, "ctx", [(c, c + 1) for c in odds])
    arrived = [got1, got2, got3, got4, got5, payload]

    query_pieces, key_pieces, value_pieces = [], [], []
    for half in range(halves):
        query_part, send4, part2, back1, back3, own_part = head_group_grads(
            head_window, odd, query_ids, query_proj, weighted, arrived, half, width, half,
            group_size,
        )
        is_odd = odd[0] == 1
        from1 = permuted(back1, "ctx", [(c, c - 1) for c in everyone]).astype(jnp.float32)
        from3 = permuted(back3, "ctx", swap)
        from4 = permuted(send4, "ctx", [(c, c - 2) for c in everyone])
        send2 = part2 + from4.astype(jnp.float32) + from3.astype(jnp.float32)
        send2 = (send2 + jnp.where(is_odd, from1, jnp.float32(0.0))).astype(jnp.bfloat16)
        from2 = permuted(send2, "ctx", [(c, c - 2) for c in everyone])
        summed = own_part + from2.astype(jnp.float32) + jnp.where(is_odd, jnp.float32(0.0), from1)
        query_pieces.append(query_part)
        key_pieces.append(summed[:, :width])
        value_pieces.append(summed[:, width:])
    query_grad = jnp.concatenate(query_pieces, axis=1)
    key_grad = jnp.concatenate(key_pieces, axis=1).astype(jnp.bfloat16)
    value_grad = jnp.concatenate(value_pieces, axis=1).astype(jnp.bfloat16)
    return (query_grad, key_grad, value_grad)


def solution(mesh):
    in_specs = (
        P(("group", "ctx"), "tsp"),
        P(("group", "ctx"), "tsp"),
        P(("group", "ctx"), "tsp"),
        P(("group", "ctx", "tsp"), None),
        P(("group", "ctx")),
        P("group"),
        P("tsp"),
    )
    out_specs = (P(("group", "ctx"), "tsp"), P(("group", "ctx"), "tsp"), P(("group", "ctx"), "tsp"))
    return jax.shard_map(
        on_device, mesh=mesh, in_specs=in_specs, out_specs=out_specs, check_vma=False
    )
```

```python
import functools
import jax
import jax.numpy as jnp
from jax import lax
from jax.experimental import pallas as pl
from jax.experimental.pallas import tpu as pltpu
from jax.sharding import PartitionSpec as P

HEAD_DIMENSION = 128
WINDOW = 1024
ID_ROWS = 16
HALVES = 2
score_scale = 168.0 ** (-0.5)


def _nt(a, b):
    return lax.dot_general(a, b, (((1,), (1,)), ((), ())), preferred_element_type=jnp.float32)


def _tn(a, b):
    return lax.dot_general(a, b, (((0,), (0,)), ((), ())), preferred_element_type=jnp.float32)


def _nn(a, b):
    return lax.dot_general(a, b, (((1,), (0,)), ((), ())), preferred_element_type=jnp.float32)


def attention_kernel(win_ref, odd_ref, qid_ref, q_ref, g_ref, *rest, group_size, first_head):
    key_refs = rest[:6]
    value_refs = rest[6:12]
    dq_ref, p4_ref, p2_ref, m1_ref, b3_ref, own_ref = rest[12:]
    d = HEAD_DIMENSION
    rows = q_ref.shape[0]
    width = key_refs[0].shape[1]
    odd = odd_ref[0] == 1

    def pick(odd_source, even_source):
        def load(index):
            return jnp.where(odd, odd_source[index], even_source[index])
        return load

    def plain(ref):
        def load(index):
            return ref[index]
        return load

    def arrange(refs):
        r1, r2, r3, r4, r5, own = refs
        return [plain(r4), pick(r3, r5), plain(r2), pick(r1, r3), plain(own)]

    key_sources = arrange(key_refs)
    value_sources = arrange(value_refs)
    pieces = len(key_sources)
    key_count = pieces * rows
    row = lax.broadcasted_iota(jnp.int32, (rows, key_count), 0)
    col = lax.broadcasted_iota(jnp.int32, (rows, key_count), 1)
    offset = row + (key_count - rows) - col
    key_ids = jnp.concatenate(
        [src((slice(rows, rows + 1), slice(0, rows))).astype(jnp.float32) for src in key_sources],
        axis=1,
    )
    base_live = (offset >= 0) & (key_ids == qid_ref[...])
    for kv in range(width // d):
        kcols = slice(kv * d, (kv + 1) * d)
        vcols = slice(width + kv * d, width + (kv + 1) * d)
        keys = [src((slice(0, rows), kcols)) for src in key_sources]
        values = [src((slice(0, rows), kcols)) for src in value_sources]
        parts = kv_head(win_ref, q_ref, g_ref, dq_ref, keys, values, offset, base_live, kv, group_size,
                        first_head)
        for target, p in ((p4_ref, 0), (p2_ref, 2)):
            target[:, kcols] = parts[p][0].astype(target.dtype)
            target[:, vcols] = parts[p][1].astype(target.dtype)
        m1_ref[:, kcols] = jnp.where(odd, parts[3][0], parts[1][0]).astype(m1_ref.dtype)
        m1_ref[:, vcols] = jnp.where(odd, parts[3][1], parts[1][1]).astype(m1_ref.dtype)
        b3_ref[:, kcols] = jnp.where(odd, parts[1][0], parts[3][0]).astype(b3_ref.dtype)
        b3_ref[:, vcols] = jnp.where(odd, parts[1][1], parts[3][1]).astype(b3_ref.dtype)
        own_ref[:, kcols] = parts[4][0]
        own_ref[:, vcols] = parts[4][1]


def kv_head(win_ref, q_ref, g_ref, dq_ref, keys, values, offset, base_live, kv, group_size,
            first_head):
    d = HEAD_DIMENSION
    pieces = len(keys)
    piece_rows = q_ref.shape[0]
    key_acc = [jnp.zeros((piece_rows, d), jnp.float32) for _ in range(pieces)]
    value_acc = [jnp.zeros((piece_rows, d), jnp.float32) for _ in range(pieces)]
    all_keys = jnp.concatenate(keys, axis=0)
    all_values = jnp.concatenate(values, axis=0)
    for h in range(group_size):
        head = kv * group_size + h
        query = q_ref[:, head * d : (head + 1) * d]
        grad = g_ref[:, head * d : (head + 1) * d]
        scores = _nt(query, all_keys) * score_scale
        live = base_live & (offset < win_ref[first_head + head])
        scores = jnp.where(live, scores, jnp.float32(-1e30))
        top = jnp.max(scores, axis=1, keepdims=True)
        prob = jnp.exp(scores - top)
        prob = prob * (1.0 / jnp.sum(prob, axis=1, keepdims=True))
        prob_low = prob.astype(jnp.bfloat16)
        attended = _nn(prob_low, all_values).astype(jnp.bfloat16).astype(jnp.float32)
        delta = jnp.sum(grad.astype(jnp.float32) * attended, axis=1, keepdims=True)
        dprob = _nt(grad, all_values)
        dscore = (prob * (dprob - delta)).astype(jnp.bfloat16)
        query_acc = _nn(dscore, all_keys)
        dq_ref[:, head * d : (head + 1) * d] = (query_acc * score_scale).astype(dq_ref.dtype)
        for p in range(pieces):
            cols = slice(p * piece_rows, (p + 1) * piece_rows)
            key_acc[p] = key_acc[p] + _tn(dscore[:, cols], query)
            value_acc[p] = value_acc[p] + _tn(prob_low[:, cols], grad)
    return [(key_acc[p] * score_scale, value_acc[p]) for p in range(pieces)]


def head_group_grads(windows, odd, query_ids, query, grad, payloads, half, width, key_block,
                     group_size):
    rows = query.shape[0]
    payload_rows = payloads[0].shape[0]
    value_block = key_block + payloads[0].shape[1] // (2 * width)
    smem = pl.BlockSpec(memory_space=pltpu.SMEM)
    key_spec = pl.BlockSpec((payload_rows, width), lambda i: (0, key_block))
    value_spec = pl.BlockSpec((payload_rows, width), lambda i: (0, value_block))
    query_spec = pl.BlockSpec((rows, group_size * width), lambda i: (0, half))
    id_spec = pl.BlockSpec((rows, 1), lambda i: (0, 0))
    pair_spec = pl.BlockSpec((rows, 2 * width), lambda i: (0, 0))
    wide = jax.ShapeDtypeStruct((rows, 2 * width), jnp.float32)
    low = jax.ShapeDtypeStruct((rows, 2 * width), jnp.bfloat16)
    out_shape = [jax.ShapeDtypeStruct((rows, group_size * width), jnp.bfloat16)]
    out_shape += [low, wide, low, low, wide]
    kernel = functools.partial(
        attention_kernel, group_size=group_size, first_head=half * group_size * width // HEAD_DIMENSION
    )
    return pl.pallas_call(
        kernel,
        out_shape=out_shape,
        grid=(1,),
        in_specs=[smem, smem, id_spec, query_spec, query_spec]
        + [key_spec] * len(payloads)
        + [value_spec] * len(payloads),
        out_specs=[pl.BlockSpec((rows, group_size * width), lambda i: (0, 0))] + [pair_spec] * 5,
        name="attention_group",
    )(windows, odd, query_ids, query, grad, *payloads, *payloads)


def passed_along(value, axis, steps):
    count = lax.axis_size(axis)
    initial, last = (max(0, -steps), min(count, count - steps))
    return lax.ppermute(value, axis, [(source, source + steps) for source in range(initial, last)])


def permuted(value, axis, pairs, scope=None):
    return lax.ppermute(value, axis, [pair for pair in pairs if 0 <= pair[1] < lax.axis_size(axis)])


def on_device(query_proj, key_proj, value_projection, grad_out, doc_ids, advantages, head_window):
    tok_rows = query_proj.shape[0]
    kv_width = key_proj.shape[1]
    count = lax.axis_size("ctx")
    assert WINDOW // tok_rows == 4 and count % 2 == 0
    index = lax.axis_index("ctx")
    odd = (index % 2).astype(jnp.int32).reshape(1)
    doc_count = advantages.shape[0]
    matches = doc_ids[:, None] == jnp.arange(doc_count, dtype=jnp.int32)[None, :]
    token_weight = jnp.sum(jnp.where(matches, advantages[None, :], jnp.float32(0.0)), axis=1)
    grad_local = lax.all_to_all(grad_out, "tsp", split_axis=1, concat_axis=0, tiled=True)
    weighted = (token_weight[:, None] * grad_local.astype(jnp.float32)).astype(jnp.bfloat16)
    query_ids = (doc_ids + 1).astype(jnp.float32)[:, None]

    kv_heads = kv_width // HEAD_DIMENSION
    group_size = query_proj.shape[1] // kv_width
    halves = HALVES
    width = kv_width // halves
    evens = range(0, count, 2)
    odds = range(1, count, 2)
    everyone = range(count)
    swap = [(c, c + 1) for c in evens] + [(c, c - 1) for c in odds]
    arrived = []
    for half in range(halves):
        cols = slice(half * width, (half + 1) * width)
        paired = jnp.concatenate([key_proj[:, cols], value_projection[:, cols]], axis=1)
        id_rows = jnp.zeros((ID_ROWS, 2 * width), jnp.bfloat16)
        id_rows = id_rows.at[0, :].set(
            jnp.tile((doc_ids + 1).astype(jnp.bfloat16), 2 * width // tok_rows)
        )
        payload = jnp.concatenate([paired, id_rows], axis=0)
        got1 = permuted(payload, "ctx", [(c, c + 1) for c in evens])
        got2 = permuted(payload, "ctx", [(c, c + 2) for c in everyone])
        got3 = permuted(got2, "ctx", swap)
        got4 = permuted(got2, "ctx", [(c, c + 2) for c in everyone])
        got5 = permuted(got2, "ctx", [(c, c + 1) for c in odds])
        arrived.append([got1, got2, got3, got4, got5, payload])

    query_pieces, key_pieces, value_pieces = [], [], []
    for half in range(halves):
        query_part, send4, part2, back1, back3, own_part = head_group_grads(
            head_window, odd, query_ids, query_proj, weighted, arrived[half], half, width, 0,
            group_size,
        )
        is_odd = odd[0] == 1
        from1 = permuted(back1, "ctx", [(c, c - 1) for c in everyone]).astype(jnp.float32)
        from3 = permuted(back3, "ctx", swap)
        from4 = permuted(send4, "ctx", [(c, c - 2) for c in everyone])
        send2 = part2 + from4.astype(jnp.float32) + from3.astype(jnp.float32)
        send2 = (send2 + jnp.where(is_odd, from1, jnp.float32(0.0))).astype(jnp.bfloat16)
        from2 = permuted(send2, "ctx", [(c, c - 2) for c in everyone])
        summed = own_part + from2.astype(jnp.float32) + jnp.where(is_odd, jnp.float32(0.0), from1)
        query_pieces.append(query_part)
        key_pieces.append(summed[:, :width])
        value_pieces.append(summed[:, width:])
    query_grad = jnp.concatenate(query_pieces, axis=1)
    key_grad = jnp.concatenate(key_pieces, axis=1).astype(jnp.bfloat16)
    value_grad = jnp.concatenate(value_pieces, axis=1).astype(jnp.bfloat16)
    return (query_grad, key_grad, value_grad)


def solution(mesh):
    in_specs = (
        P(("group", "ctx"), "tsp"),
        P(("group", "ctx"), "tsp"),
        P(("group", "ctx"), "tsp"),
        P(("group", "ctx", "tsp"), None),
        P(("group", "ctx")),
        P("group"),
        P("tsp"),
    )
    out_specs = (P(("group", "ctx"), "tsp"), P(("group", "ctx"), "tsp"), P(("group", "ctx"), "tsp"))
    return jax.shard_map(
        on_device, mesh=mesh, in_specs=in_specs, out_specs=out_specs, check_vma=False
    )
```

```python
import functools
import jax
import jax.numpy as jnp
from jax import lax
from jax.experimental import pallas as pl
from jax.experimental.pallas import tpu as pltpu
from jax.sharding import PartitionSpec as P

HEAD_DIMENSION = 128
WINDOW = 1024
ID_ROWS = 16
HALVES = 2
score_scale = 168.0 ** (-0.5)


def _nt(a, b):
    return lax.dot_general(a, b, (((1,), (1,)), ((), ())), preferred_element_type=jnp.float32)


def _tn(a, b):
    return lax.dot_general(a, b, (((0,), (0,)), ((), ())), preferred_element_type=jnp.float32)


def _nn(a, b):
    return lax.dot_general(a, b, (((1,), (0,)), ((), ())), preferred_element_type=jnp.float32)


def attention_kernel(win_ref, odd_ref, qid_ref, q_ref, g_ref, *rest, group_size, first_head):
    key_refs = rest[:6]
    value_refs = rest[6:12]
    dq_ref, p4_ref, p2_ref, m1_ref, b3_ref, own_ref = rest[12:]
    d = HEAD_DIMENSION
    rows = q_ref.shape[0]
    width = key_refs[0].shape[1]
    odd = odd_ref[0] == 1

    def pick(odd_source, even_source):
        def load(index):
            return jnp.where(odd, odd_source[index], even_source[index])
        return load

    def plain(ref):
        def load(index):
            return ref[index]
        return load

    def arrange(refs):
        r1, r2, r3, r4, r5, own = refs
        return [plain(r4), pick(r3, r5), plain(r2), pick(r1, r3), plain(own)]

    key_sources = arrange(key_refs)
    value_sources = arrange(value_refs)
    pieces = len(key_sources)
    key_count = pieces * rows
    row = lax.broadcasted_iota(jnp.int32, (rows, key_count), 0)
    col = lax.broadcasted_iota(jnp.int32, (rows, key_count), 1)
    offset = row + (key_count - rows) - col
    key_ids = jnp.concatenate(
        [src((slice(rows, rows + 1), slice(0, rows))).astype(jnp.float32) for src in key_sources],
        axis=1,
    )
    base_live = (offset >= 0) & (key_ids == qid_ref[...])
    for kv in range(width // d):
        kcols = slice(kv * d, (kv + 1) * d)
        vcols = slice(width + kv * d, width + (kv + 1) * d)
        keys = [src((slice(0, rows), kcols)) for src in key_sources]
        values = [src((slice(0, rows), kcols)) for src in value_sources]
        parts = kv_head(win_ref, q_ref, g_ref, dq_ref, keys, values, offset, base_live, kv, group_size,
                        first_head)
        for target, p in ((p4_ref, 0), (p2_ref, 2)):
            target[:, kcols] = parts[p][0].astype(target.dtype)
            target[:, vcols] = parts[p][1].astype(target.dtype)
        m1_ref[:, kcols] = jnp.where(odd, parts[3][0], parts[1][0]).astype(m1_ref.dtype)
        m1_ref[:, vcols] = jnp.where(odd, parts[3][1], parts[1][1]).astype(m1_ref.dtype)
        b3_ref[:, kcols] = jnp.where(odd, parts[1][0], parts[3][0]).astype(b3_ref.dtype)
        b3_ref[:, vcols] = jnp.where(odd, parts[1][1], parts[3][1]).astype(b3_ref.dtype)
        own_ref[:, kcols] = parts[4][0]
        own_ref[:, vcols] = parts[4][1]


def kv_head(win_ref, q_ref, g_ref, dq_ref, keys, values, offset, base_live, kv, group_size,
            first_head):
    d = HEAD_DIMENSION
    pieces = len(keys)
    piece_rows = q_ref.shape[0]
    key_acc = [jnp.zeros((piece_rows, d), jnp.float32) for _ in range(pieces)]
    value_acc = [jnp.zeros((piece_rows, d), jnp.float32) for _ in range(pieces)]
    for h in range(group_size):
        head = kv * group_size + h
        query = q_ref[:, head * d : (head + 1) * d]
        grad = g_ref[:, head * d : (head + 1) * d]
        scores = jnp.concatenate([_nt(query, key) for key in keys], axis=1) * score_scale
        live = base_live & (offset < win_ref[first_head + head])
        scores = jnp.where(live, scores, jnp.float32(-1e30))
        top = jnp.max(scores, axis=1, keepdims=True)
        prob = jnp.exp(scores - top)
        prob = prob * (1.0 / jnp.sum(prob, axis=1, keepdims=True))
        prob_low = prob.astype(jnp.bfloat16)
        attended = _nn(prob_low[:, :piece_rows], values[0])
        for p in range(1, pieces):
            attended = attended + _nn(prob_low[:, p * piece_rows : (p + 1) * piece_rows], values[p])
        attended = attended.astype(jnp.bfloat16).astype(jnp.float32)
        delta = jnp.sum(grad.astype(jnp.float32) * attended, axis=1, keepdims=True)
        dprob = jnp.concatenate([_nt(grad, value) for value in values], axis=1)
        dscore = (prob * (dprob - delta)).astype(jnp.bfloat16)
        query_acc = _nn(dscore[:, :piece_rows], keys[0])
        for p in range(1, pieces):
            query_acc = query_acc + _nn(dscore[:, p * piece_rows : (p + 1) * piece_rows], keys[p])
        dq_ref[:, head * d : (head + 1) * d] = (query_acc * score_scale).astype(dq_ref.dtype)
        for p in range(pieces):
            cols = slice(p * piece_rows, (p + 1) * piece_rows)
            key_acc[p] = key_acc[p] + _tn(dscore[:, cols], query)
            value_acc[p] = value_acc[p] + _tn(prob_low[:, cols], grad)
    return [(key_acc[p] * score_scale, value_acc[p]) for p in range(pieces)]


def head_group_grads(windows, odd, query_ids, query, grad, payloads, half, width, key_block,
                     group_size):
    rows = query.shape[0]
    payload_rows = payloads[0].shape[0]
    value_block = key_block + payloads[0].shape[1] // (2 * width)
    smem = pl.BlockSpec(memory_space=pltpu.SMEM)
    key_spec = pl.BlockSpec((payload_rows, width), lambda i: (0, key_block))
    value_spec = pl.BlockSpec((payload_rows, width), lambda i: (0, value_block))
    query_spec = pl.BlockSpec((rows, group_size * width), lambda i: (0, half))
    id_spec = pl.BlockSpec((rows, 1), lambda i: (0, 0))
    pair_spec = pl.BlockSpec((rows, 2 * width), lambda i: (0, 0))
    wide = jax.ShapeDtypeStruct((rows, 2 * width), jnp.float32)
    low = jax.ShapeDtypeStruct((rows, 2 * width), jnp.bfloat16)
    out_shape = [jax.ShapeDtypeStruct((rows, group_size * width), jnp.bfloat16)]
    out_shape += [low, wide, low, low, wide]
    kernel = functools.partial(
        attention_kernel, group_size=group_size, first_head=half * group_size * width // HEAD_DIMENSION
    )
    return pl.pallas_call(
        kernel,
        out_shape=out_shape,
        grid=(1,),
        in_specs=[smem, smem, id_spec, query_spec, query_spec]
        + [key_spec] * len(payloads)
        + [value_spec] * len(payloads),
        out_specs=[pl.BlockSpec((rows, group_size * width), lambda i: (0, 0))] + [pair_spec] * 5,
        name="attention_group",
    )(windows, odd, query_ids, query, grad, *payloads, *payloads)


def passed_along(value, axis, steps):
    count = lax.axis_size(axis)
    initial, last = (max(0, -steps), min(count, count - steps))
    return lax.ppermute(value, axis, [(source, source + steps) for source in range(initial, last)])


def permuted(value, axis, pairs, scope=None):
    return lax.ppermute(value, axis, [pair for pair in pairs if 0 <= pair[1] < lax.axis_size(axis)])


def on_device(query_proj, key_proj, value_projection, grad_out, doc_ids, advantages, head_window):
    tok_rows = query_proj.shape[0]
    kv_width = key_proj.shape[1]
    count = lax.axis_size("ctx")
    assert WINDOW // tok_rows == 4 and count % 2 == 0
    index = lax.axis_index("ctx")
    odd = (index % 2).astype(jnp.int32).reshape(1)
    doc_count = advantages.shape[0]
    matches = doc_ids[:, None] == jnp.arange(doc_count, dtype=jnp.int32)[None, :]
    token_weight = jnp.sum(jnp.where(matches, advantages[None, :], jnp.float32(0.0)), axis=1)
    grad_local = lax.all_to_all(grad_out, "tsp", split_axis=1, concat_axis=0, tiled=True)
    weighted = (token_weight[:, None] * grad_local.astype(jnp.float32)).astype(jnp.bfloat16)
    query_ids = (doc_ids + 1).astype(jnp.float32)[:, None]

    kv_heads = kv_width // HEAD_DIMENSION
    group_size = query_proj.shape[1] // kv_width
    halves = HALVES
    width = kv_width // halves
    evens = range(0, count, 2)
    odds = range(1, count, 2)
    everyone = range(count)
    swap = [(c, c + 1) for c in evens] + [(c, c - 1) for c in odds]
    arrived = []
    for half in range(halves):
        cols = slice(half * width, (half + 1) * width)
        paired = jnp.concatenate([key_proj[:, cols], value_projection[:, cols]], axis=1)
        id_rows = jnp.zeros((ID_ROWS, 2 * width), jnp.bfloat16)
        id_rows = id_rows.at[0, :].set(
            jnp.tile((doc_ids + 1).astype(jnp.bfloat16), 2 * width // tok_rows)
        )
        payload = jnp.concatenate([paired, id_rows], axis=0)
        got2 = permuted(payload, "ctx", [(c, c + 2) for c in everyone])
        got3 = permuted(got2, "ctx", swap)
        got4 = permuted(got2, "ctx", [(c, c + 2) for c in everyone])
        forward = jnp.where(odd[0] == 1, got2, payload)
        got15 = permuted(forward, "ctx", [(c, c + 1) for c in everyone])
        arrived.append([got15, got2, got3, got4, got15, payload])

    query_pieces, key_pieces, value_pieces = [], [], []
    for half in range(halves):
        query_part, send4, part2, back1, back3, own_part = head_group_grads(
            head_window, odd, query_ids, query_proj, weighted, arrived[half], half, width, 0,
            group_size,
        )
        is_odd = odd[0] == 1
        from1 = permuted(back1, "ctx", [(c, c - 1) for c in everyone]).astype(jnp.float32)
        from3 = permuted(back3, "ctx", swap)
        from4 = permuted(send4, "ctx", [(c, c - 2) for c in everyone])
        send2 = part2 + from4.astype(jnp.float32) + from3.astype(jnp.float32)
        send2 = (send2 + jnp.where(is_odd, from1, jnp.float32(0.0))).astype(jnp.bfloat16)
        from2 = permuted(send2, "ctx", [(c, c - 2) for c in everyone])
        summed = own_part + from2.astype(jnp.float32) + jnp.where(is_odd, jnp.float32(0.0), from1)
        query_pieces.append(query_part)
        key_pieces.append(summed[:, :width])
        value_pieces.append(summed[:, width:])
    query_grad = jnp.concatenate(query_pieces, axis=1)
    key_grad = jnp.concatenate(key_pieces, axis=1).astype(jnp.bfloat16)
    value_grad = jnp.concatenate(value_pieces, axis=1).astype(jnp.bfloat16)
    return (query_grad, key_grad, value_grad)


def solution(mesh):
    in_specs = (
        P(("group", "ctx"), "tsp"),
        P(("group", "ctx"), "tsp"),
        P(("group", "ctx"), "tsp"),
        P(("group", "ctx", "tsp"), None),
        P(("group", "ctx")),
        P("group"),
        P("tsp"),
    )
    out_specs = (P(("group", "ctx"), "tsp"), P(("group", "ctx"), "tsp"), P(("group", "ctx"), "tsp"))
    return jax.shard_map(
        on_device, mesh=mesh, in_specs=in_specs, out_specs=out_specs, check_vma=False
    )
```

```python
import functools
import jax
import jax.numpy as jnp
from jax import lax
from jax.experimental import pallas as pl
from jax.experimental.pallas import tpu as pltpu
from jax.sharding import PartitionSpec as P

HEAD_DIMENSION = 128
WINDOW = 1024
ID_ROWS = 16
HALVES = 2
score_scale = 168.0 ** (-0.5)


def _nt(a, b):
    return lax.dot_general(a, b, (((1,), (1,)), ((), ())), preferred_element_type=jnp.float32)


def _tn(a, b):
    return lax.dot_general(a, b, (((0,), (0,)), ((), ())), preferred_element_type=jnp.float32)


def _nn(a, b):
    return lax.dot_general(a, b, (((1,), (0,)), ((), ())), preferred_element_type=jnp.float32)


def attention_kernel(win_ref, odd_ref, qid_ref, q_ref, g_ref, *rest, group_size, first_head):
    key_refs = rest[:6]
    value_refs = rest[6:12]
    dq_ref, p4_ref, p2_ref, m1_ref, b3_ref, own_ref = rest[12:]
    d = HEAD_DIMENSION
    rows = q_ref.shape[0]
    width = key_refs[0].shape[1]
    odd = odd_ref[0] == 1

    def pick(odd_source, even_source):
        def load(index):
            return jnp.where(odd, odd_source[index], even_source[index])
        return load

    def plain(ref):
        def load(index):
            return ref[index]
        return load

    def arrange(refs):
        r1, r2, r3, r4, r5, own = refs
        return [plain(r4), pick(r3, r5), plain(r2), pick(r1, r3), plain(own)]

    key_sources = arrange(key_refs)
    value_sources = arrange(value_refs)
    pieces = len(key_sources)
    key_count = pieces * rows
    row = lax.broadcasted_iota(jnp.int32, (rows, key_count), 0)
    col = lax.broadcasted_iota(jnp.int32, (rows, key_count), 1)
    offset = row + (key_count - rows) - col
    key_ids = jnp.concatenate(
        [src((slice(rows, rows + 1), slice(0, rows))).astype(jnp.float32) for src in key_sources],
        axis=1,
    )
    base_live = (offset >= 0) & (key_ids == qid_ref[...])
    for kv in range(width // d):
        kcols = slice(kv * d, (kv + 1) * d)
        vcols = slice(width + kv * d, width + (kv + 1) * d)
        keys = [src((slice(0, rows), kcols)) for src in key_sources]
        values = [src((slice(0, rows), kcols)) for src in value_sources]
        parts = kv_head(win_ref, q_ref, g_ref, dq_ref, keys, values, offset, base_live, kv, group_size,
                        first_head)
        for target, p in ((p4_ref, 0), (p2_ref, 2)):
            target[:, kcols] = parts[p][0].astype(target.dtype)
            target[:, vcols] = parts[p][1].astype(target.dtype)
        m1_ref[:, kcols] = jnp.where(odd, parts[3][0], parts[1][0]).astype(m1_ref.dtype)
        m1_ref[:, vcols] = jnp.where(odd, parts[3][1], parts[1][1]).astype(m1_ref.dtype)
        b3_ref[:, kcols] = jnp.where(odd, parts[1][0], parts[3][0]).astype(b3_ref.dtype)
        b3_ref[:, vcols] = jnp.where(odd, parts[1][1], parts[3][1]).astype(b3_ref.dtype)
        own_ref[:, kcols] = parts[4][0]
        own_ref[:, vcols] = parts[4][1]


def kv_head(win_ref, q_ref, g_ref, dq_ref, keys, values, offset, base_live, kv, group_size,
            first_head):
    d = HEAD_DIMENSION
    pieces = len(keys)
    piece_rows = q_ref.shape[0]
    key_acc = [jnp.zeros((piece_rows, d), jnp.float32) for _ in range(pieces)]
    value_acc = [jnp.zeros((piece_rows, d), jnp.float32) for _ in range(pieces)]
    for h in range(group_size):
        head = kv * group_size + h
        query = q_ref[:, head * d : (head + 1) * d]
        grad = g_ref[:, head * d : (head + 1) * d]
        scores = jnp.concatenate([_nt(query, key) for key in keys], axis=1) * score_scale
        live = base_live & (offset < win_ref[first_head + head])
        scores = jnp.where(live, scores, jnp.float32(-1e30))
        top = jnp.max(scores, axis=1, keepdims=True)
        prob = jnp.exp(scores - top)
        prob = prob * (1.0 / jnp.sum(prob, axis=1, keepdims=True))
        prob_low = prob.astype(jnp.bfloat16)
        attended = _nn(prob_low[:, :piece_rows], values[0])
        for p in range(1, pieces):
            attended = attended + _nn(prob_low[:, p * piece_rows : (p + 1) * piece_rows], values[p])
        attended = attended.astype(jnp.bfloat16).astype(jnp.float32)
        delta = jnp.sum(grad.astype(jnp.float32) * attended, axis=1, keepdims=True)
        dprob = jnp.concatenate([_nt(grad, value) for value in values], axis=1)
        dscore = (prob * (dprob - delta)).astype(jnp.bfloat16)
        query_acc = _nn(dscore[:, :piece_rows], keys[0])
        for p in range(1, pieces):
            query_acc = query_acc + _nn(dscore[:, p * piece_rows : (p + 1) * piece_rows], keys[p])
        dq_ref[:, head * d : (head + 1) * d] = (query_acc * score_scale).astype(dq_ref.dtype)
        for p in range(pieces):
            cols = slice(p * piece_rows, (p + 1) * piece_rows)
            key_acc[p] = key_acc[p] + _tn(dscore[:, cols], query)
            value_acc[p] = value_acc[p] + _tn(prob_low[:, cols], grad)
    return [(key_acc[p] * score_scale, value_acc[p]) for p in range(pieces)]


def head_group_grads(windows, odd, query_ids, query, grad, payloads, half, width, key_block,
                     group_size):
    rows = query.shape[0]
    payload_rows = payloads[0].shape[0]
    value_block = key_block + payloads[0].shape[1] // (2 * width)
    smem = pl.BlockSpec(memory_space=pltpu.SMEM)
    key_spec = pl.BlockSpec((payload_rows, width), lambda i: (0, key_block))
    value_spec = pl.BlockSpec((payload_rows, width), lambda i: (0, value_block))
    query_spec = pl.BlockSpec((rows, group_size * width), lambda i: (0, half))
    id_spec = pl.BlockSpec((rows, 1), lambda i: (0, 0))
    pair_spec = pl.BlockSpec((rows, 2 * width), lambda i: (0, 0))
    wide = jax.ShapeDtypeStruct((rows, 2 * width), jnp.float32)
    low = jax.ShapeDtypeStruct((rows, 2 * width), jnp.bfloat16)
    out_shape = [jax.ShapeDtypeStruct((rows, group_size * width), jnp.bfloat16)]
    out_shape += [low, wide, low, low, wide]
    kernel = functools.partial(
        attention_kernel, group_size=group_size, first_head=half * group_size * width // HEAD_DIMENSION
    )
    return pl.pallas_call(
        kernel,
        out_shape=out_shape,
        grid=(1,),
        in_specs=[smem, smem, id_spec, query_spec, query_spec]
        + [key_spec] * len(payloads)
        + [value_spec] * len(payloads),
        out_specs=[pl.BlockSpec((rows, group_size * width), lambda i: (0, 0))] + [pair_spec] * 5,
        name="attention_group",
    )(windows, odd, query_ids, query, grad, *payloads, *payloads)


def passed_along(value, axis, steps):
    count = lax.axis_size(axis)
    initial, last = (max(0, -steps), min(count, count - steps))
    return lax.ppermute(value, axis, [(source, source + steps) for source in range(initial, last)])


def permuted(value, axis, pairs, scope=None):
    return lax.ppermute(value, axis, [pair for pair in pairs if 0 <= pair[1] < lax.axis_size(axis)])


def on_device(query_proj, key_proj, value_projection, grad_out, doc_ids, advantages, head_window):
    tok_rows = query_proj.shape[0]
    kv_width = key_proj.shape[1]
    count = lax.axis_size("ctx")
    assert WINDOW // tok_rows == 4 and count % 2 == 0
    index = lax.axis_index("ctx")
    odd = (index % 2).astype(jnp.int32).reshape(1)
    doc_count = advantages.shape[0]
    matches = doc_ids[:, None] == jnp.arange(doc_count, dtype=jnp.int32)[None, :]
    token_weight = jnp.sum(jnp.where(matches, advantages[None, :], jnp.float32(0.0)), axis=1)
    grad_local = lax.all_to_all(grad_out, "tsp", split_axis=1, concat_axis=0, tiled=True)
    weighted = (token_weight[:, None] * grad_local.astype(jnp.float32)).astype(jnp.bfloat16)
    query_ids = (doc_ids + 1).astype(jnp.float32)[:, None]

    kv_heads = kv_width // HEAD_DIMENSION
    group_size = query_proj.shape[1] // kv_width
    halves = HALVES
    width = kv_width // halves
    evens = range(0, count, 2)
    odds = range(1, count, 2)
    everyone = range(count)
    swap = [(c, c + 1) for c in evens] + [(c, c - 1) for c in odds]
    arrived = []
    for half in range(halves):
        cols = slice(half * width, (half + 1) * width)
        paired = jnp.concatenate([key_proj[:, cols], value_projection[:, cols]], axis=1)
        id_rows = jnp.zeros((ID_ROWS, 2 * width), jnp.bfloat16)
        id_rows = id_rows.at[0, :].set(
            jnp.tile((doc_ids + 1).astype(jnp.bfloat16), 2 * width // tok_rows)
        )
        payload = jnp.concatenate([paired, id_rows], axis=0)
        got1 = permuted(payload, "ctx", [(c, c + 1) for c in evens])
        got2 = permuted(payload, "ctx", [(c, c + 2) for c in everyone])
        got3 = permuted(got2, "ctx", swap)
        got4 = permuted(got2, "ctx", [(c, c + 2) for c in everyone])
        got5 = permuted(got2, "ctx", [(c, c + 1) for c in odds])
        arrived.append([got1, got2, got3, got4, got5, payload])

    results = [
        head_group_grads(
            head_window, odd, query_ids, query_proj, weighted, arrived[half], half, width, 0,
            group_size,
        )
        for half in range(halves)
    ]
    for half in range(halves - 1):
        results[half], _ = lax.optimization_barrier((results[half], results[-1][0]))
    query_pieces, key_pieces, value_pieces = [], [], []
    for half in range(halves):
        query_part, send4, part2, back1, back3, own_part = results[half]
        is_odd = odd[0] == 1
        from1 = permuted(back1, "ctx", [(c, c - 1) for c in everyone]).astype(jnp.float32)
        from3 = permuted(back3, "ctx", swap)
        from4 = permuted(send4, "ctx", [(c, c - 2) for c in everyone])
        send2 = part2 + from4.astype(jnp.float32) + from3.astype(jnp.float32)
        send2 = (send2 + jnp.where(is_odd, from1, jnp.float32(0.0))).astype(jnp.bfloat16)
        from2 = permuted(send2, "ctx", [(c, c - 2) for c in everyone])
        summed = own_part + from2.astype(jnp.float32) + jnp.where(is_odd, jnp.float32(0.0), from1)
        query_pieces.append(query_part)
        key_pieces.append(summed[:, :width])
        value_pieces.append(summed[:, width:])
    query_grad = jnp.concatenate(query_pieces, axis=1)
    key_grad = jnp.concatenate(key_pieces, axis=1).astype(jnp.bfloat16)
    value_grad = jnp.concatenate(value_pieces, axis=1).astype(jnp.bfloat16)
    return (query_grad, key_grad, value_grad)


def solution(mesh):
    in_specs = (
        P(("group", "ctx"), "tsp"),
        P(("group", "ctx"), "tsp"),
        P(("group", "ctx"), "tsp"),
        P(("group", "ctx", "tsp"), None),
        P(("group", "ctx")),
        P("group"),
        P("tsp"),
    )
    out_specs = (P(("group", "ctx"), "tsp"), P(("group", "ctx"), "tsp"), P(("group", "ctx"), "tsp"))
    return jax.shard_map(
        on_device, mesh=mesh, in_specs=in_specs, out_specs=out_specs, check_vma=False
    )
```

```python
import functools
import jax
import jax.numpy as jnp
from jax import lax
from jax.experimental import pallas as pl
from jax.experimental.pallas import tpu as pltpu
from jax.sharding import PartitionSpec as P

HEAD_DIMENSION = 128
WINDOW = 1024
ID_ROWS = 8
HALVES = 2
score_scale = 168.0 ** (-0.5)


def _nt(a, b):
    return lax.dot_general(a, b, (((1,), (1,)), ((), ())), preferred_element_type=jnp.float32)


def _tn(a, b):
    return lax.dot_general(a, b, (((0,), (0,)), ((), ())), preferred_element_type=jnp.float32)


def _nn(a, b):
    return lax.dot_general(a, b, (((1,), (0,)), ((), ())), preferred_element_type=jnp.float32)


def attention_kernel(win_ref, odd_ref, qid_ref, q_ref, g_ref, *rest, group_size, first_head):
    key_refs = rest[:6]
    value_refs = rest[6:12]
    dq_ref, p4_ref, p2_ref, m1_ref, b3_ref, own_ref = rest[12:]
    d = HEAD_DIMENSION
    rows = q_ref.shape[0]
    width = key_refs[0].shape[1]
    odd = odd_ref[0] == 1

    def pick(odd_source, even_source):
        def load(index):
            return jnp.where(odd, odd_source[index], even_source[index])
        return load

    def plain(ref):
        def load(index):
            return ref[index]
        return load

    def arrange(refs):
        r1, r2, r3, r4, r5, own = refs
        return [plain(r4), pick(r3, r5), plain(r2), pick(r1, r3), plain(own)]

    key_sources = arrange(key_refs)
    value_sources = arrange(value_refs)
    pieces = len(key_sources)
    key_count = pieces * rows
    row = lax.broadcasted_iota(jnp.int32, (rows, key_count), 0)
    col = lax.broadcasted_iota(jnp.int32, (rows, key_count), 1)
    offset = row + (key_count - rows) - col
    key_ids = jnp.concatenate(
        [src((slice(rows, rows + 1), slice(0, rows))).astype(jnp.float32) for src in key_sources],
        axis=1,
    )
    base_live = (offset >= 0) & (key_ids == qid_ref[...])
    for kv in range(width // d):
        kcols = slice(kv * d, (kv + 1) * d)
        vcols = slice(width + kv * d, width + (kv + 1) * d)
        keys = [src((slice(0, rows), kcols)) for src in key_sources]
        values = [src((slice(0, rows), kcols)) for src in value_sources]
        parts = kv_head(win_ref, q_ref, g_ref, dq_ref, keys, values, offset, base_live, kv, group_size,
                        first_head)
        for target, p in ((p4_ref, 0), (p2_ref, 2)):
            target[:, kcols] = parts[p][0].astype(target.dtype)
            target[:, vcols] = parts[p][1].astype(target.dtype)
        m1_ref[:, kcols] = jnp.where(odd, parts[3][0], parts[1][0]).astype(m1_ref.dtype)
        m1_ref[:, vcols] = jnp.where(odd, parts[3][1], parts[1][1]).astype(m1_ref.dtype)
        b3_ref[:, kcols] = jnp.where(odd, parts[1][0], parts[3][0]).astype(b3_ref.dtype)
        b3_ref[:, vcols] = jnp.where(odd, parts[1][1], parts[3][1]).astype(b3_ref.dtype)
        own_ref[:, kcols] = parts[4][0]
        own_ref[:, vcols] = parts[4][1]


def kv_head(win_ref, q_ref, g_ref, dq_ref, keys, values, offset, base_live, kv, group_size,
            first_head):
    d = HEAD_DIMENSION
    pieces = len(keys)
    piece_rows = q_ref.shape[0]
    key_acc = [jnp.zeros((piece_rows, d), jnp.float32) for _ in range(pieces)]
    value_acc = [jnp.zeros((piece_rows, d), jnp.float32) for _ in range(pieces)]
    for h in range(group_size):
        head = kv * group_size + h
        query = q_ref[:, head * d : (head + 1) * d]
        grad = g_ref[:, head * d : (head + 1) * d]
        scores = jnp.concatenate([_nt(query, key) for key in keys], axis=1) * score_scale
        live = base_live & (offset < win_ref[first_head + head])
        scores = jnp.where(live, scores, jnp.float32(-1e30))
        top = jnp.max(scores, axis=1, keepdims=True)
        prob = jnp.exp(scores - top)
        prob = prob * (1.0 / jnp.sum(prob, axis=1, keepdims=True))
        prob_low = prob.astype(jnp.bfloat16)
        attended = _nn(prob_low[:, :piece_rows], values[0])
        for p in range(1, pieces):
            attended = attended + _nn(prob_low[:, p * piece_rows : (p + 1) * piece_rows], values[p])
        attended = attended.astype(jnp.bfloat16).astype(jnp.float32)
        delta = jnp.sum(grad.astype(jnp.float32) * attended, axis=1, keepdims=True)
        dprob = jnp.concatenate([_nt(grad, value) for value in values], axis=1)
        dscore = (prob * (dprob - delta)).astype(jnp.bfloat16)
        query_acc = _nn(dscore[:, :piece_rows], keys[0])
        for p in range(1, pieces):
            query_acc = query_acc + _nn(dscore[:, p * piece_rows : (p + 1) * piece_rows], keys[p])
        dq_ref[:, head * d : (head + 1) * d] = (query_acc * score_scale).astype(dq_ref.dtype)
        for p in range(pieces):
            cols = slice(p * piece_rows, (p + 1) * piece_rows)
            key_acc[p] = key_acc[p] + _tn(dscore[:, cols], query)
            value_acc[p] = value_acc[p] + _tn(prob_low[:, cols], grad)
    return [(key_acc[p] * score_scale, value_acc[p]) for p in range(pieces)]


def head_group_grads(windows, odd, query_ids, query, grad, payloads, half, width, key_block,
                     group_size):
    rows = query.shape[0]
    payload_rows = payloads[0].shape[0]
    value_block = key_block + payloads[0].shape[1] // (2 * width)
    smem = pl.BlockSpec(memory_space=pltpu.SMEM)
    key_spec = pl.BlockSpec((payload_rows, width), lambda i: (0, key_block))
    value_spec = pl.BlockSpec((payload_rows, width), lambda i: (0, value_block))
    query_spec = pl.BlockSpec((rows, group_size * width), lambda i: (0, half))
    id_spec = pl.BlockSpec((rows, 1), lambda i: (0, 0))
    pair_spec = pl.BlockSpec((rows, 2 * width), lambda i: (0, 0))
    wide = jax.ShapeDtypeStruct((rows, 2 * width), jnp.float32)
    low = jax.ShapeDtypeStruct((rows, 2 * width), jnp.bfloat16)
    out_shape = [jax.ShapeDtypeStruct((rows, group_size * width), jnp.bfloat16)]
    out_shape += [low, wide, low, low, wide]
    kernel = functools.partial(
        attention_kernel, group_size=group_size, first_head=half * group_size * width // HEAD_DIMENSION
    )
    return pl.pallas_call(
        kernel,
        out_shape=out_shape,
        grid=(1,),
        in_specs=[smem, smem, id_spec, query_spec, query_spec]
        + [key_spec] * len(payloads)
        + [value_spec] * len(payloads),
        out_specs=[pl.BlockSpec((rows, group_size * width), lambda i: (0, 0))] + [pair_spec] * 5,
        name="attention_group",
    )(windows, odd, query_ids, query, grad, *payloads, *payloads)


def passed_along(value, axis, steps):
    count = lax.axis_size(axis)
    initial, last = (max(0, -steps), min(count, count - steps))
    return lax.ppermute(value, axis, [(source, source + steps) for source in range(initial, last)])


def permuted(value, axis, pairs, scope=None):
    return lax.ppermute(value, axis, [pair for pair in pairs if 0 <= pair[1] < lax.axis_size(axis)])


def on_device(query_proj, key_proj, value_projection, grad_out, doc_ids, advantages, head_window):
    tok_rows = query_proj.shape[0]
    kv_width = key_proj.shape[1]
    count = lax.axis_size("ctx")
    assert WINDOW // tok_rows == 4 and count % 2 == 0
    index = lax.axis_index("ctx")
    odd = (index % 2).astype(jnp.int32).reshape(1)
    doc_count = advantages.shape[0]
    matches = doc_ids[:, None] == jnp.arange(doc_count, dtype=jnp.int32)[None, :]
    token_weight = jnp.sum(jnp.where(matches, advantages[None, :], jnp.float32(0.0)), axis=1)
    grad_local = lax.all_to_all(grad_out, "tsp", split_axis=1, concat_axis=0, tiled=True)
    weighted = (token_weight[:, None] * grad_local.astype(jnp.float32)).astype(jnp.bfloat16)
    query_ids = (doc_ids + 1).astype(jnp.float32)[:, None]

    kv_heads = kv_width // HEAD_DIMENSION
    group_size = query_proj.shape[1] // kv_width
    halves = HALVES
    width = kv_width // halves
    evens = range(0, count, 2)
    odds = range(1, count, 2)
    everyone = range(count)
    swap = [(c, c + 1) for c in evens] + [(c, c - 1) for c in odds]
    arrived = []
    for half in range(halves):
        cols = slice(half * width, (half + 1) * width)
        paired = jnp.concatenate([key_proj[:, cols], value_projection[:, cols]], axis=1)
        id_rows = jnp.zeros((ID_ROWS, 2 * width), jnp.bfloat16)
        id_rows = id_rows.at[0, :].set(
            jnp.tile((doc_ids + 1).astype(jnp.bfloat16), 2 * width // tok_rows)
        )
        payload = jnp.concatenate([paired, id_rows], axis=0)
        got1 = permuted(payload, "ctx", [(c, c + 1) for c in evens])
        got2 = permuted(payload, "ctx", [(c, c + 2) for c in everyone])
        got3 = permuted(got2, "ctx", swap)
        got4 = permuted(got2, "ctx", [(c, c + 2) for c in everyone])
        got5 = permuted(got2, "ctx", [(c, c + 1) for c in odds])
        arrived.append([got1, got2, got3, got4, got5, payload])

    query_pieces, key_pieces, value_pieces = [], [], []
    for half in range(halves):
        query_part, send4, part2, back1, back3, own_part = head_group_grads(
            head_window, odd, query_ids, query_proj, weighted, arrived[half], half, width, 0,
            group_size,
        )
        is_odd = odd[0] == 1
        from1 = permuted(back1, "ctx", [(c, c - 1) for c in everyone]).astype(jnp.float32)
        from3 = permuted(back3, "ctx", swap)
        from4 = permuted(send4, "ctx", [(c, c - 2) for c in everyone])
        send2 = part2 + from4.astype(jnp.float32) + from3.astype(jnp.float32)
        send2 = (send2 + jnp.where(is_odd, from1, jnp.float32(0.0))).astype(jnp.bfloat16)
        from2 = permuted(send2, "ctx", [(c, c - 2) for c in everyone])
        summed = own_part + from2.astype(jnp.float32) + jnp.where(is_odd, jnp.float32(0.0), from1)
        query_pieces.append(query_part)
        key_pieces.append(summed[:, :width])
        value_pieces.append(summed[:, width:])
    query_grad = jnp.concatenate(query_pieces, axis=1)
    key_grad = jnp.concatenate(key_pieces, axis=1).astype(jnp.bfloat16)
    value_grad = jnp.concatenate(value_pieces, axis=1).astype(jnp.bfloat16)
    return (query_grad, key_grad, value_grad)


def solution(mesh):
    in_specs = (
        P(("group", "ctx"), "tsp"),
        P(("group", "ctx"), "tsp"),
        P(("group", "ctx"), "tsp"),
        P(("group", "ctx", "tsp"), None),
        P(("group", "ctx")),
        P("group"),
        P("tsp"),
    )
    out_specs = (P(("group", "ctx"), "tsp"), P(("group", "ctx"), "tsp"), P(("group", "ctx"), "tsp"))
    return jax.shard_map(
        on_device, mesh=mesh, in_specs=in_specs, out_specs=out_specs, check_vma=False
    )
```
